128 devices in a mesh: gx: 4 (over x_lo, core), gy: 8 (over y, x_hi), gz: 4 (over z).
Axes of the slice: x: 4 (x_hi: 2, x_lo: 2; x = x_hi * 2 + x_lo), y: 4, z: 4, core: 2. Of those that a mesh axis runs over, the one named last changes fastest.
Arguments:
- state: float32 [4, 96, 128, 2048], P(None, 'gz', 'gx', 'gy'), may hold values from -5 to 5
- mixing: float32 [2, 96, 128, 2048], P(None, 'gz', 'gx', 'gy'), may hold values from 0.1 to 1000
- depth_levels: int32 [128, 2048], replicated, may hold values from 0 to 96
- wind: float32 [2, 128, 2048], P(None, 'gx', 'gy'), may hold values from -3 to 3
Outputs:
- state_next: float32 [4, 96, 128, 2048], P(None, 'gz', 'gx', 'gy')
The draws below stay inside these ranges and needn't reach their ends.
Inputs may be any that keep to these rules, and one draw needn't show every extreme that they name: `depth_levels`: levels at or beyond a column's count are land.
All inputs are finite; a program needn't handle non-finite values.
Results may differ from the reference program's by a relative error of at most 0.0003.
Values sent between devices are 32-bit elements; how exact they have to be, the bound alone decides.
No kernel may reach another device: no remote copies, remote signals or barrier semaphores. Data moves between devices by JAX's collectives and lax.ppermute only.
A program may use at most 192 MiB of HBM per device.

```python
import math
import jax
import jax.numpy as jnp
from jax import lax

NZ = 96
NX = 128
NY = 2048


def place_ends(drawn, key, low, top_value):
    place = [jax.random.randint(jax.random.fold_in(key, axis), (), 0, length) for axis, length in enumerate(drawn.shape)]
    widest = drawn.shape.index(max(drawn.shape))
    next_to = place[:widest] + [(place[widest] + 1) % drawn.shape[widest]] + place[widest + 1:]
    return drawn.at[tuple(place)].set(low).at[tuple(next_to)].set(top_value)


def block_scale(stream_key, dims, pieces, least, high):
    loudness = 1.0
    for dim, blocks in pieces:
        draws = jax.random.uniform(jax.random.fold_in(jax.random.fold_in(stream_key, 6), dim), (blocks,), jnp.float32, least / len(pieces), high / len(pieces))
        loudness = loudness * jnp.repeat(jnp.exp(draws), dims[dim] // blocks).reshape((-1,) + (1,) * (len(dims) - 1 - dim))
    return loudness


def gaussian(own_key, extent, scale, bound, pieces=(), held_as=jnp.bfloat16):
    level = block_scale(own_key, extent, pieces, -0.22, 0.18) if pieces else 1.0
    array = jax.random.normal(own_key, extent, jnp.float32) * scale * level
    return jnp.minimum(jnp.maximum(array, -bound), bound).astype(held_as)


def setup_inputs(seed: int = 0) -> dict:
    seeds = jax.random.split(jax.random.key(seed), 5)
    return {
        "state": gaussian(seeds[0], (4, NZ, NX, NY), 1.0, 5.0, ((1, 4), (2, 4), (3, 8)), jnp.float32),
        "mixing": jnp.clip(jnp.exp(math.log(1000.0) - 9.2103404 * jax.random.uniform(seeds[1], (2, NZ, NX, NY), jnp.float32) ** block_scale(seeds[1], (2, NZ, NX, NY), ((1, 4), (2, 4), (3, 8)), -0.2, 0.2)), 0.1, 1000.0),
        "depth_levels": place_ends(jax.random.randint(seeds[2], (NX, NY), 0, NZ + 1), jax.random.fold_in(seeds[2], 1), 0, NZ).astype(jnp.int32),
        "wind": gaussian(seeds[3], (2, NX, NY), 0.5, 3.0, ((1, 4), (2, 8)), jnp.float32),
    }


def density_of(fields, wet_mask):
    return (-0.3 * fields[0] + 0.7 * fields[1] - 0.05 * fields[0] * fields[0]) * wet_mask


def advance(padded, wet_pad, pressure, wall_face, coriolis):
    wet_x = wet_pad[:, :-1, 1:-1] * wet_pad[:, 1:, 1:-1]
    wet_y = wet_pad[:, 1:-1, :-1] * wet_pad[:, 1:-1, 1:] * wall_face
    east_vel = 0.5 * (padded[2, :, :-1, 1:-1] + padded[2, :, 1:, 1:-1]) * wet_x
    north_vel = 0.5 * (padded[3, :, 1:-1, :-1] + padded[3, :, 1:-1, 1:]) * wet_y
    west_side = padded[:, :, :-1, 1:-1]
    east_side = padded[:, :, 1:, 1:-1]
    flux_x = 0.25 * (jnp.maximum(east_vel, 0.0) * west_side + jnp.minimum(east_vel, 0.0) * east_side) - 0.08 * wet_x * (east_side - west_side)
    south_side = padded[:, :, 1:-1, :-1]
    north_side = padded[:, :, 1:-1, 1:]
    flux_y = 0.25 * (jnp.maximum(north_vel, 0.0) * south_side + jnp.minimum(north_vel, 0.0) * north_side) - 0.08 * wet_y * (north_side - south_side)
    interior = padded[:, :, 1:-1, 1:-1]
    moved = interior - (flux_x[:, :, 1:] - flux_x[:, :, :-1] + flux_y[:, :, :, 1:] - flux_y[:, :, :, :-1])
    centre = pressure[:, 1:-1, 1:-1]
    grad_x = 0.5 * (wet_x[:, 1:] * (pressure[:, 2:, 1:-1] - centre) + wet_x[:, :-1] * (centre - pressure[:, :-2, 1:-1]))
    grad_y = 0.5 * (wet_y[:, :, 1:] * (pressure[:, 1:-1, 2:] - centre) + wet_y[:, :, :-1] * (centre - pressure[:, 1:-1, :-2]))
    east_new = moved[2] + 0.3 * coriolis * interior[3] - grad_x
    north_new = moved[3] - 0.3 * coriolis * interior[2] - grad_y
    wet_inner = wet_pad[:, 1:-1, 1:-1]
    return jnp.stack([moved[0], moved[1], east_new, north_new]) * wet_inner


def tridiagonal(forced, coupling):
    below = jnp.repeat(coupling, 2, axis=0)
    above = jnp.concatenate([jnp.zeros_like(below[:, :1]), below[:, :-1]], axis=1)
    rhs_lev = jnp.moveaxis(forced, 1, 0)
    below_lev = jnp.moveaxis(below, 1, 0)
    above_lev = jnp.moveaxis(above, 1, 0)

    def forward(carry, item):
        ratio_prev, value_prev = carry
        rhs_here, below_here, above_here = item
        divisor = 1.0 + above_here * (1.0 - ratio_prev) + below_here
        ratio = below_here / divisor
        value = (rhs_here + above_here * value_prev) / divisor
        return (ratio, value), (ratio, value)

    zero_level = jnp.zeros_like(rhs_lev[0])
    _, (ratios, values) = lax.scan(forward, (zero_level, zero_level), (rhs_lev, below_lev, above_lev), unroll=8)

    def backward(later, item):
        ratio, value = item
        result = value + ratio * later
        return result, result

    _, solved = lax.scan(backward, zero_level, (ratios, values), reverse=True, unroll=8)
    return jnp.moveaxis(solved, 0, 1)


def reference(state, mixing, depth_levels, wind):
    levels = jnp.arange(NZ, dtype=jnp.int32)
    wet = (levels[:, None, None] < depth_levels[None]).astype(jnp.float32)
    wet_next = ((levels + 1)[:, None, None] < depth_levels[None]).astype(jnp.float32)
    density_field = density_of(state, wet)
    pressure = 0.03 * (jnp.cumsum(density_field, axis=0) - 0.5 * density_field)
    padded = jnp.pad(state, ((0, 0), (0, 0), (1, 1), (1, 1)), mode="wrap")
    wet_pad = jnp.pad(wet, ((0, 0), (1, 1), (1, 1)), mode="wrap")
    pressure_pad = jnp.pad(pressure, ((0, 0), (1, 1), (1, 1)), mode="wrap")
    face_row = jnp.arange(NY + 1, dtype=jnp.int32) - 1
    wall_face = ((face_row >= 0) & (face_row <= NY - 2)).astype(jnp.float32)
    coriolis = 0.5 + (jnp.arange(NY, dtype=jnp.int32).astype(jnp.float32) + 0.5) / NY
    forced = advance(padded, wet_pad, pressure_pad, wall_face, coriolis)
    top_level = (levels == 0).astype(jnp.float32)
    forced = forced.at[2:].add(wind[:, None] * top_level[None, :, None, None] * wet[None])
    coupling = mixing * (wet * wet_next)[None]
    return tridiagonal(forced, coupling)
```

```python
import jax
import jax.numpy as jnp
from jax import lax
from jax.experimental import pallas as pl
from jax.experimental.pallas import tpu as pltpu
from jax.sharding import PartitionSpec as P


def padded_2(array, sides, width):
    for axis, dim in sides:
        peers, length = (lax.axis_size(axis), array.shape[dim])
        up = [(i, (i + 1) % peers) for i in range(peers)]
        down = [(j, i) for i, j in up]
        last = lax.slice_in_dim(array, length - width, length, axis=dim)
        initial = lax.slice_in_dim(array, 0, width, axis=dim)
        before = lax.ppermute(last, axis, up)
        after = lax.ppermute(initial, axis, down)
        array = jnp.concatenate([before, array, after], axis=dim)
    return array


def density_of(fields, wet_mask):
    return (-0.3 * fields[0] + 0.7 * fields[1] - 0.05 * fields[0] * fields[0]) * wet_mask


def advance(padded, wet_pad, pressure, wall_face, coriolis):
    wet_x = wet_pad[:, :-1, 1:-1] * wet_pad[:, 1:, 1:-1]
    wet_y = wet_pad[:, 1:-1, :-1] * wet_pad[:, 1:-1, 1:] * wall_face
    east_vel = 0.5 * (padded[2, :, :-1, 1:-1] + padded[2, :, 1:, 1:-1]) * wet_x
    north_vel = 0.5 * (padded[3, :, 1:-1, :-1] + padded[3, :, 1:-1, 1:]) * wet_y
    west_side = padded[:, :, :-1, 1:-1]
    east_side = padded[:, :, 1:, 1:-1]
    flux_x = 0.25 * (
        jnp.maximum(east_vel, 0.0) * west_side + jnp.minimum(east_vel, 0.0) * east_side
    ) - 0.08 * wet_x * (east_side - west_side)
    south_side = padded[:, :, 1:-1, :-1]
    north_side = padded[:, :, 1:-1, 1:]
    flux_y = 0.25 * (
        jnp.maximum(north_vel, 0.0) * south_side + jnp.minimum(north_vel, 0.0) * north_side
    ) - 0.08 * wet_y * (north_side - south_side)
    interior = padded[:, :, 1:-1, 1:-1]
    moved = interior - (
        flux_x[:, :, 1:] - flux_x[:, :, :-1] + flux_y[:, :, :, 1:] - flux_y[:, :, :, :-1]
    )
    centre = pressure[:, 1:-1, 1:-1]
    grad_x = 0.5 * (
        wet_x[:, 1:] * (pressure[:, 2:, 1:-1] - centre)
        + wet_x[:, :-1] * (centre - pressure[:, :-2, 1:-1])
    )
    grad_y = 0.5 * (
        wet_y[:, :, 1:] * (pressure[:, 1:-1, 2:] - centre)
        + wet_y[:, :, :-1] * (centre - pressure[:, 1:-1, :-2])
    )
    east_new = moved[2] + 0.3 * coriolis * interior[3] - grad_x
    north_new = moved[3] - 0.3 * coriolis * interior[2] - grad_y
    wet_inner = wet_pad[:, 1:-1, 1:-1]
    return jnp.stack([moved[0], moved[1], east_new, north_new]) * wet_inner


def local_solve_kernel(f_ref, c_ref, ctop_ref, y_ref, u_ref, v_ref, ratio_s):
    levels = f_ref.shape[1]
    ctop = ctop_ref[...]
    ratio_prev = None
    vy_prev = None
    vu_prev = None
    for k in range(levels):
        above = ctop if k == 0 else c_ref[:, k - 1]
        below = c_ref[:, k]
        if k == 0:
            divisor = 1.0 + above + below
        else:
            divisor = 1.0 + above * (1.0 - ratio_prev) + below
        inv = 1.0 / divisor
        ratio = below * inv
        rhs = f_ref[:, k]
        if k == 0:
            vy = rhs * jnp.repeat(inv, 2, axis=0)
            vu = ctop * inv
        else:
            vy = (rhs + jnp.repeat(above, 2, axis=0) * vy_prev) * jnp.repeat(inv, 2, axis=0)
            vu = above * vu_prev * inv
        ratio_s[:, k] = ratio
        y_ref[:, k] = vy
        u_ref[:, k] = vu
        ratio_prev, vy_prev, vu_prev = ratio, vy, vu
    y_later = vy_prev
    u_later = vu_prev
    v_later = ratio_prev
    v_ref[:, levels - 1] = v_later
    for k in range(levels - 2, -1, -1):
        ratio = ratio_s[:, k]
        y_later = y_ref[:, k] + jnp.repeat(ratio, 2, axis=0) * y_later
        u_later = u_ref[:, k] + ratio * u_later
        v_later = ratio * v_later
        y_ref[:, k] = y_later
        u_ref[:, k] = u_later
        v_ref[:, k] = v_later


def local_solve(forced, coupling, ctop):
    fields, levels, cols_x, cols_y = forced.shape
    pairs = coupling.shape[0]
    bx = 8 if cols_x % 8 == 0 else cols_x
    grid = (cols_x // bx,)
    fspec = pl.BlockSpec((fields, levels, bx, cols_y), lambda i: (0, 0, i, 0))
    cspec = pl.BlockSpec((pairs, levels, bx, cols_y), lambda i: (0, 0, i, 0))
    tspec = pl.BlockSpec((pairs, bx, cols_y), lambda i: (0, i, 0))
    return pl.pallas_call(
        local_solve_kernel,
        grid=grid,
        in_specs=[fspec, cspec, tspec],
        out_specs=[fspec, cspec, cspec],
        out_shape=[
            jax.ShapeDtypeStruct(forced.shape, jnp.float32),
            jax.ShapeDtypeStruct(coupling.shape, jnp.float32),
            jax.ShapeDtypeStruct(coupling.shape, jnp.float32),
        ],
        scratch_shapes=[pltpu.VMEM((pairs, levels, bx, cols_y), jnp.float32)],
    )(forced, coupling, ctop)


def interface_values(summary, place, peers):
    fields = 4
    y0 = summary[:, 0:fields]
    y1 = summary[:, fields:2 * fields]
    rest = jnp.repeat(summary[:, 2 * fields:], 2, axis=1)
    u0 = rest[:, 0:4]
    u1 = rest[:, 4:8]
    v0 = rest[:, 8:12]
    v1 = rest[:, 12:16]
    pt, qt, pb, qb = [], [], [], []
    for q in range(peers):
        if q == 0:
            pt_q, qt_q = y0[q], v0[q]
            pb_q, qb_q = y1[q], v1[q]
        else:
            d = 1.0 - u0[q] * qb[-1]
            inv = 1.0 / d
            pt_q = (y0[q] + u0[q] * pb[-1]) * inv
            qt_q = v0[q] * inv
            pb_q = y1[q] + u1[q] * (pb[-1] + qb[-1] * pt_q)
            qb_q = v1[q] + u1[q] * qb[-1] * qt_q
        pt.append(pt_q)
        qt.append(qt_q)
        pb.append(pb_q)
        qb.append(qb_q)
    tops = [None] * peers
    bots = [None] * peers
    t_next = jnp.zeros_like(pt[0])
    for q in range(peers - 1, -1, -1):
        tops[q] = pt[q] + qt[q] * t_next
        bots[q] = pb[q] + qb[q] * t_next
        t_next = tops[q]
    above = jnp.zeros_like(pt[0])
    below = jnp.zeros_like(pt[0])
    for q in range(peers):
        if q >= 1:
            above = jnp.where(place == q, bots[q - 1], above)
        if q <= peers - 2:
            below = jnp.where(place == q, tops[q + 1], below)
    return above, below


def per_device(state, mixing, depth_levels, wind):
    fields, lev_count, col_x, col_y = state.shape
    total_x, total_y = depth_levels.shape
    peers_z = lax.axis_size("gz")
    place_z = lax.axis_index("gz")
    start_x = lax.axis_index("gx") * col_x
    start_y = lax.axis_index("gy") * col_y
    start_z = place_z * lev_count
    down_z = [(i, i + 1) for i in range(peers_z - 1)]
    mix_above = lax.ppermute(mixing[:, lev_count - 1], "gz", down_z)
    padded = padded_2(state, (("gx", 2), ("gy", 3)), 1)
    row_index = (start_x - 1 + jnp.arange(col_x + 2, dtype=jnp.int32)) % total_x
    col_index = (start_y - 1 + jnp.arange(col_y + 2, dtype=jnp.int32)) % total_y
    depth_pad = jnp.take(jnp.take(depth_levels, row_index, axis=0), col_index, axis=1)
    levels = start_z + jnp.arange(lev_count, dtype=jnp.int32)
    wet_pad = (levels[:, None, None] < depth_pad[None]).astype(jnp.float32)
    density_field = density_of(padded, wet_pad)
    inclusive = jnp.cumsum(density_field, axis=0)
    column_total = inclusive[-1]
    gathered = lax.all_gather(column_total, "gz")
    shallower = jnp.zeros_like(column_total)
    for q in range(peers_z):
        shallower = shallower + jnp.where(q < place_z, gathered[q], 0.0)
    pressure = 0.03 * (shallower[None] + inclusive - 0.5 * density_field)
    face_row = start_y - 1 + jnp.arange(col_y + 1, dtype=jnp.int32)
    wall_face = ((face_row >= 0) & (face_row <= total_y - 2)).astype(jnp.float32)
    row_global = start_y + jnp.arange(col_y, dtype=jnp.int32)
    coriolis = 0.5 + (row_global.astype(jnp.float32) + 0.5) / total_y
    forced = advance(padded, wet_pad, pressure, wall_face, coriolis)
    wet_inner = wet_pad[:, 1:-1, 1:-1]
    depth_inner = depth_pad[1:-1, 1:-1]
    wet_next = ((levels + 1)[:, None, None] < depth_inner[None]).astype(jnp.float32)
    top_level = (levels == 0).astype(jnp.float32)
    forced = forced.at[2:].add(wind[:, None] * top_level[None, :, None, None] * wet_inner[None])
    coupling = mixing * (wet_inner * wet_next)[None]
    wet_up = ((start_z - 1) < depth_inner).astype(jnp.float32)
    ctop = mix_above * (wet_up * wet_inner[0])[None]
    ctop = jnp.where(place_z > 0, ctop, 0.0)
    y, u, v = local_solve(forced, coupling, ctop)
    last = lev_count - 1
    summary = jnp.concatenate(
        [y[:, 0], y[:, last], u[:, 0], u[:, last], v[:, 0], v[:, last]], axis=0
    )
    gathered_ends = lax.all_gather(summary, "gz")
    x_above, x_below = interface_values(gathered_ends, place_z, peers_z)
    u4 = jnp.repeat(u, 2, axis=0)
    v4 = jnp.repeat(v, 2, axis=0)
    return y + x_above[:, None] * u4 + x_below[:, None] * v4


def solution(mesh):
    return jax.shard_map(
        per_device,
        mesh=mesh,
        in_specs=(P(None, "gz", "gx", "gy"), P(None, "gz", "gx", "gy"), P(), P(None, "gx", "gy")),
        out_specs=P(None, "gz", "gx", "gy"),
        check_vma=False,
    )
```

```python
import jax
import jax.numpy as jnp
from jax import lax
from jax.experimental import pallas as pl
from jax.experimental.pallas import tpu as pltpu
from jax.sharding import PartitionSpec as P


def padded_2(array, sides, width):
    for axis, dim in sides:
        peers, length = (lax.axis_size(axis), array.shape[dim])
        up = [(i, (i + 1) % peers) for i in range(peers)]
        down = [(j, i) for i, j in up]
        last = lax.slice_in_dim(array, length - width, length, axis=dim)
        initial = lax.slice_in_dim(array, 0, width, axis=dim)
        before = lax.ppermute(last, axis, up)
        after = lax.ppermute(initial, axis, down)
        array = jnp.concatenate([before, array, after], axis=dim)
    return array


def density_of(fields, wet_mask):
    return (-0.3 * fields[0] + 0.7 * fields[1] - 0.05 * fields[0] * fields[0]) * wet_mask


def advance(padded, wet_pad, pressure, wall_face, coriolis):
    wet_x = wet_pad[:, :-1, 1:-1] * wet_pad[:, 1:, 1:-1]
    wet_y = wet_pad[:, 1:-1, :-1] * wet_pad[:, 1:-1, 1:] * wall_face
    east_vel = 0.5 * (padded[2, :, :-1, 1:-1] + padded[2, :, 1:, 1:-1]) * wet_x
    north_vel = 0.5 * (padded[3, :, 1:-1, :-1] + padded[3, :, 1:-1, 1:]) * wet_y
    west_side = padded[:, :, :-1, 1:-1]
    east_side = padded[:, :, 1:, 1:-1]
    flux_x = 0.25 * (
        jnp.maximum(east_vel, 0.0) * west_side + jnp.minimum(east_vel, 0.0) * east_side
    ) - 0.08 * wet_x * (east_side - west_side)
    south_side = padded[:, :, 1:-1, :-1]
    north_side = padded[:, :, 1:-1, 1:]
    flux_y = 0.25 * (
        jnp.maximum(north_vel, 0.0) * south_side + jnp.minimum(north_vel, 0.0) * north_side
    ) - 0.08 * wet_y * (north_side - south_side)
    interior = padded[:, :, 1:-1, 1:-1]
    moved = interior - (
        flux_x[:, :, 1:] - flux_x[:, :, :-1] + flux_y[:, :, :, 1:] - flux_y[:, :, :, :-1]
    )
    centre = pressure[:, 1:-1, 1:-1]
    grad_x = 0.5 * (
        wet_x[:, 1:] * (pressure[:, 2:, 1:-1] - centre)
        + wet_x[:, :-1] * (centre - pressure[:, :-2, 1:-1])
    )
    grad_y = 0.5 * (
        wet_y[:, :, 1:] * (pressure[:, 1:-1, 2:] - centre)
        + wet_y[:, :, :-1] * (centre - pressure[:, 1:-1, :-2])
    )
    east_new = moved[2] + 0.3 * coriolis * interior[3] - grad_x
    north_new = moved[3] - 0.3 * coriolis * interior[2] - grad_y
    wet_inner = wet_pad[:, 1:-1, 1:-1]
    return jnp.stack([moved[0], moved[1], east_new, north_new]) * wet_inner


def coupling_kernel(c_ref, ctop_ref, ratio_ref, inv_ref, u_ref, v_ref, ends_ref):
    levels = c_ref.shape[1]
    ctop = ctop_ref[...]
    ratio_prev = None
    vu_prev = None
    for k in range(levels):
        above = ctop if k == 0 else c_ref[:, k - 1]
        below = c_ref[:, k]
        if k == 0:
            divisor = 1.0 + above + below
        else:
            divisor = 1.0 + above * (1.0 - ratio_prev) + below
        inv = 1.0 / divisor
        ratio = below * inv
        vu = ctop * inv if k == 0 else above * vu_prev * inv
        ratio_ref[:, k] = ratio
        inv_ref[:, k] = inv
        u_ref[:, k] = vu
        ratio_prev, vu_prev = ratio, vu
    u_later = vu_prev
    v_later = ratio_prev
    pairs = c_ref.shape[0]
    ends_ref[pairs:2 * pairs] = u_later
    ends_ref[3 * pairs:4 * pairs] = v_later
    v_ref[:, levels - 1] = v_later
    for k in range(levels - 2, -1, -1):
        ratio = ratio_ref[:, k]
        u_later = u_ref[:, k] + ratio * u_later
        v_later = ratio * v_later
        u_ref[:, k] = u_later
        v_ref[:, k] = v_later
    ends_ref[0:pairs] = u_later
    ends_ref[2 * pairs:3 * pairs] = v_later


def field_kernel(f_ref, c_ref, ctop_ref, ratio_ref, inv_ref, y_ref, ends_ref):
    levels = f_ref.shape[1]
    fields = f_ref.shape[0]
    vy = None
    for k in range(levels):
        inv = jnp.repeat(inv_ref[:, k], 2, axis=0)
        rhs = f_ref[:, k]
        if k == 0:
            vy = rhs * inv
        else:
            above = jnp.repeat(c_ref[:, k - 1], 2, axis=0)
            vy = (rhs + above * vy) * inv
        y_ref[:, k] = vy
    y_later = vy
    ends_ref[fields:2 * fields] = y_later
    for k in range(levels - 2, -1, -1):
        ratio = jnp.repeat(ratio_ref[:, k], 2, axis=0)
        y_later = y_ref[:, k] + ratio * y_later
        y_ref[:, k] = y_later
    ends_ref[0:fields] = y_later


def _specs(lead, levels, bx, cols_y):
    return pl.BlockSpec((lead, levels, bx, cols_y), lambda i: (0, 0, i, 0))


def _plane_spec(lead, bx, cols_y):
    return pl.BlockSpec((lead, bx, cols_y), lambda i: (0, i, 0))


def coupling_solve(coupling, ctop):
    pairs, levels, cols_x, cols_y = coupling.shape
    bx = 8 if cols_x % 8 == 0 else cols_x
    cspec = _specs(pairs, levels, bx, cols_y)
    full = jax.ShapeDtypeStruct(coupling.shape, jnp.float32)
    return pl.pallas_call(
        coupling_kernel,
        grid=(cols_x // bx,),
        in_specs=[cspec, _plane_spec(pairs, bx, cols_y)],
        out_specs=[cspec, cspec, cspec, cspec, _plane_spec(4 * pairs, bx, cols_y)],
        out_shape=[full, full, full, full,
                   jax.ShapeDtypeStruct((4 * pairs, cols_x, cols_y), jnp.float32)],
    )(coupling, ctop)


def field_solve(forced, coupling, ctop, ratio, inv):
    fields, levels, cols_x, cols_y = forced.shape
    pairs = coupling.shape[0]
    bx = 8 if cols_x % 8 == 0 else cols_x
    fspec = _specs(fields, levels, bx, cols_y)
    cspec = _specs(pairs, levels, bx, cols_y)
    return pl.pallas_call(
        field_kernel,
        grid=(cols_x // bx,),
        in_specs=[fspec, cspec, _plane_spec(pairs, bx, cols_y), cspec, cspec],
        out_specs=[fspec, _plane_spec(2 * fields, bx, cols_y)],
        out_shape=[jax.ShapeDtypeStruct(forced.shape, jnp.float32),
                   jax.ShapeDtypeStruct((2 * fields, cols_x, cols_y), jnp.float32)],
    )(forced, coupling, ctop, ratio, inv)


def interface_values(y_ends, uv_ends, place, peers):
    fields = 4
    y0 = y_ends[:, 0:fields]
    y1 = y_ends[:, fields:2 * fields]
    rest = jnp.repeat(uv_ends, 2, axis=1)
    u0 = rest[:, 0:4]
    u1 = rest[:, 4:8]
    v0 = rest[:, 8:12]
    v1 = rest[:, 12:16]
    pt, qt, pb, qb = [], [], [], []
    for q in range(peers):
        if q == 0:
            pt_q, qt_q = y0[q], v0[q]
            pb_q, qb_q = y1[q], v1[q]
        else:
            inv = 1.0 / (1.0 - u0[q] * qb[-1])
            pt_q = (y0[q] + u0[q] * pb[-1]) * inv
            qt_q = v0[q] * inv
            pb_q = y1[q] + u1[q] * (pb[-1] + qb[-1] * pt_q)
            qb_q = v1[q] + u1[q] * qb[-1] * qt_q
        pt.append(pt_q)
        qt.append(qt_q)
        pb.append(pb_q)
        qb.append(qb_q)
    tops = [None] * peers
    bots = [None] * peers
    t_next = jnp.zeros_like(pt[0])
    for q in range(peers - 1, -1, -1):
        tops[q] = pt[q] + qt[q] * t_next
        bots[q] = pb[q] + qb[q] * t_next
        t_next = tops[q]
    above = jnp.zeros_like(pt[0])
    below = jnp.zeros_like(pt[0])
    for q in range(peers):
        if q >= 1:
            above = jnp.where(place == q, bots[q - 1], above)
        if q <= peers - 2:
            below = jnp.where(place == q, tops[q + 1], below)
    return above, below


def per_device(state, mixing, depth_levels, wind):
    fields, lev_count, col_x, col_y = state.shape
    total_x, total_y = depth_levels.shape
    peers_z = lax.axis_size("gz")
    place_z = lax.axis_index("gz")
    start_x = lax.axis_index("gx") * col_x
    start_y = lax.axis_index("gy") * col_y
    start_z = place_z * lev_count
    down_z = [(i, i + 1) for i in range(peers_z - 1)]
    mix_above = lax.ppermute(mixing[:, lev_count - 1], "gz", down_z)
    levels = start_z + jnp.arange(lev_count, dtype=jnp.int32)
    depth_inner = lax.dynamic_slice(depth_levels, (start_x, start_y), (col_x, col_y))
    wet_here = (levels[:, None, None] < depth_inner[None]).astype(jnp.float32)
    wet_next = ((levels + 1)[:, None, None] < depth_inner[None]).astype(jnp.float32)
    coupling = mixing * (wet_here * wet_next)[None]
    wet_up = ((start_z - 1) < depth_inner).astype(jnp.float32)
    ctop = mix_above * (wet_up * wet_here[0])[None]
    ctop = jnp.where(place_z > 0, ctop, 0.0)
    ratio, inv, u, v, uv_ends = coupling_solve(coupling, ctop)
    uv_all = lax.all_gather(uv_ends, "gz")
    padded = padded_2(state, (("gx", 2), ("gy", 3)), 1)
    row_index = (start_x - 1 + jnp.arange(col_x + 2, dtype=jnp.int32)) % total_x
    col_index = (start_y - 1 + jnp.arange(col_y + 2, dtype=jnp.int32)) % total_y
    depth_pad = jnp.take(jnp.take(depth_levels, row_index, axis=0), col_index, axis=1)
    wet_pad = (levels[:, None, None] < depth_pad[None]).astype(jnp.float32)
    density_field = density_of(padded, wet_pad)
    inclusive = jnp.cumsum(density_field, axis=0)
    column_total = inclusive[-1]
    shallower = jnp.zeros_like(column_total)
    for hop in range(1, peers_z):
        pairs_z = [(i, i + hop) for i in range(peers_z - hop)]
        shallower = shallower + lax.ppermute(column_total, "gz", pairs_z)
    pressure = 0.03 * (shallower[None] + inclusive - 0.5 * density_field)
    face_row = start_y - 1 + jnp.arange(col_y + 1, dtype=jnp.int32)
    wall_face = ((face_row >= 0) & (face_row <= total_y - 2)).astype(jnp.float32)
    row_global = start_y + jnp.arange(col_y, dtype=jnp.int32)
    coriolis = 0.5 + (row_global.astype(jnp.float32) + 0.5) / total_y
    forced = advance(padded, wet_pad, pressure, wall_face, coriolis)
    wet_inner = wet_pad[:, 1:-1, 1:-1]
    top_level = (levels == 0).astype(jnp.float32)
    forced = forced.at[2:].add(wind[:, None] * top_level[None, :, None, None] * wet_inner[None])
    y, y_ends = field_solve(forced, coupling, ctop, ratio, inv)
    y_all = lax.all_gather(y_ends, "gz")
    x_above, x_below = interface_values(y_all, uv_all, place_z, peers_z)
    u4 = jnp.repeat(u, 2, axis=0)
    v4 = jnp.repeat(v, 2, axis=0)
    return y + x_above[:, None] * u4 + x_below[:, None] * v4


def solution(mesh):
    return jax.shard_map(
        per_device,
        mesh=mesh,
        in_specs=(P(None, "gz", "gx", "gy"), P(None, "gz", "gx", "gy"), P(), P(None, "gx", "gy")),
        out_specs=P(None, "gz", "gx", "gy"),
        check_vma=False,
    )
```

```python
import jax
import jax.numpy as jnp
from jax import lax
from jax.experimental import pallas as pl
from jax.experimental.pallas import tpu as pltpu
from jax.sharding import PartitionSpec as P


def padded_2(array, sides, width):
    for axis, dim in sides:
        peers, length = (lax.axis_size(axis), array.shape[dim])
        up = [(i, (i + 1) % peers) for i in range(peers)]
        down = [(j, i) for i, j in up]
        last = lax.slice_in_dim(array, length - width, length, axis=dim)
        initial = lax.slice_in_dim(array, 0, width, axis=dim)
        before = lax.ppermute(last, axis, up)
        after = lax.ppermute(initial, axis, down)
        array = jnp.concatenate([before, array, after], axis=dim)
    return array


def density_of(fields, wet_mask):
    return (-0.3 * fields[0] + 0.7 * fields[1] - 0.05 * fields[0] * fields[0]) * wet_mask


def advance(padded, wet_pad, pressure, wall_face, coriolis):
    wet_x = wet_pad[:, :-1, 1:-1] * wet_pad[:, 1:, 1:-1]
    wet_y = wet_pad[:, 1:-1, :-1] * wet_pad[:, 1:-1, 1:] * wall_face
    east_vel = 0.5 * (padded[2, :, :-1, 1:-1] + padded[2, :, 1:, 1:-1]) * wet_x
    north_vel = 0.5 * (padded[3, :, 1:-1, :-1] + padded[3, :, 1:-1, 1:]) * wet_y
    west_side = padded[:, :, :-1, 1:-1]
    east_side = padded[:, :, 1:, 1:-1]
    flux_x = 0.25 * (
        jnp.maximum(east_vel, 0.0) * west_side + jnp.minimum(east_vel, 0.0) * east_side
    ) - 0.08 * wet_x * (east_side - west_side)
    south_side = padded[:, :, 1:-1, :-1]
    north_side = padded[:, :, 1:-1, 1:]
    flux_y = 0.25 * (
        jnp.maximum(north_vel, 0.0) * south_side + jnp.minimum(north_vel, 0.0) * north_side
    ) - 0.08 * wet_y * (north_side - south_side)
    interior = padded[:, :, 1:-1, 1:-1]
    moved = interior - (
        flux_x[:, :, 1:] - flux_x[:, :, :-1] + flux_y[:, :, :, 1:] - flux_y[:, :, :, :-1]
    )
    centre = pressure[:, 1:-1, 1:-1]
    grad_x = 0.5 * (
        wet_x[:, 1:] * (pressure[:, 2:, 1:-1] - centre)
        + wet_x[:, :-1] * (centre - pressure[:, :-2, 1:-1])
    )
    grad_y = 0.5 * (
        wet_y[:, :, 1:] * (pressure[:, 1:-1, 2:] - centre)
        + wet_y[:, :, :-1] * (centre - pressure[:, 1:-1, :-2])
    )
    east_new = moved[2] + 0.3 * coriolis * interior[3] - grad_x
    north_new = moved[3] - 0.3 * coriolis * interior[2] - grad_y
    wet_inner = wet_pad[:, 1:-1, 1:-1]
    return jnp.stack([moved[0], moved[1], east_new, north_new]) * wet_inner


def coupling_kernel(c_ref, ctop_ref, ratio_ref, inv_ref, u_ref, v_ref, ends_ref):
    levels = c_ref.shape[1]
    ctop = ctop_ref[...]
    ratio_prev = None
    vu_prev = None
    for k in range(levels):
        above = ctop if k == 0 else c_ref[:, k - 1]
        below = c_ref[:, k]
        if k == 0:
            divisor = 1.0 + above + below
        else:
            divisor = 1.0 + above * (1.0 - ratio_prev) + below
        inv = 1.0 / divisor
        ratio = below * inv
        vu = ctop * inv if k == 0 else above * vu_prev * inv
        ratio_ref[:, k] = ratio
        inv_ref[:, k] = inv
        u_ref[:, k] = vu
        ratio_prev, vu_prev = ratio, vu
    u_later = vu_prev
    v_later = ratio_prev
    pairs = c_ref.shape[0]
    ends_ref[pairs:2 * pairs] = u_later
    ends_ref[3 * pairs:4 * pairs] = v_later
    v_ref[:, levels - 1] = v_later
    for k in range(levels - 2, -1, -1):
        ratio = ratio_ref[:, k]
        u_later = u_ref[:, k] + ratio * u_later
        v_later = ratio * v_later
        u_ref[:, k] = u_later
        v_ref[:, k] = v_later
    ends_ref[0:pairs] = u_later
    ends_ref[2 * pairs:3 * pairs] = v_later


def field_kernel(f_ref, c_ref, ctop_ref, ratio_ref, inv_ref, y_ref, ends_ref):
    levels = f_ref.shape[1]
    fields = f_ref.shape[0]
    vy = None
    for k in range(levels):
        inv = jnp.repeat(inv_ref[:, k], 2, axis=0)
        rhs = f_ref[:, k]
        if k == 0:
            vy = rhs * inv
        else:
            above = jnp.repeat(c_ref[:, k - 1], 2, axis=0)
            vy = (rhs + above * vy) * inv
        y_ref[:, k] = vy
    y_later = vy
    ends_ref[fields:2 * fields] = y_later
    for k in range(levels - 2, -1, -1):
        ratio = jnp.repeat(ratio_ref[:, k], 2, axis=0)
        y_later = y_ref[:, k] + ratio * y_later
        y_ref[:, k] = y_later
    ends_ref[0:fields] = y_later


def _specs(lead, levels, bx, cols_y):
    return pl.BlockSpec((lead, levels, bx, cols_y), lambda i: (0, 0, i, 0))


def _plane_spec(lead, bx, cols_y):
    return pl.BlockSpec((lead, bx, cols_y), lambda i: (0, i, 0))


def coupling_solve(coupling, ctop):
    pairs, levels, cols_x, cols_y = coupling.shape
    bx = 8 if cols_x % 8 == 0 else cols_x
    cspec = _specs(pairs, levels, bx, cols_y)
    full = jax.ShapeDtypeStruct(coupling.shape, jnp.float32)
    return pl.pallas_call(
        coupling_kernel,
        grid=(cols_x // bx,),
        in_specs=[cspec, _plane_spec(pairs, bx, cols_y)],
        out_specs=[cspec, cspec, cspec, cspec, _plane_spec(4 * pairs, bx, cols_y)],
        out_shape=[full, full, full, full,
                   jax.ShapeDtypeStruct((4 * pairs, cols_x, cols_y), jnp.float32)],
    )(coupling, ctop)


def field_solve(forced, coupling, ctop, ratio, inv):
    fields, levels, cols_x, cols_y = forced.shape
    pairs = coupling.shape[0]
    bx = 8 if cols_x % 8 == 0 else cols_x
    fspec = _specs(fields, levels, bx, cols_y)
    cspec = _specs(pairs, levels, bx, cols_y)
    return pl.pallas_call(
        field_kernel,
        grid=(cols_x // bx,),
        in_specs=[fspec, cspec, _plane_spec(pairs, bx, cols_y), cspec, cspec],
        out_specs=[fspec, _plane_spec(2 * fields, bx, cols_y)],
        out_shape=[jax.ShapeDtypeStruct(forced.shape, jnp.float32),
                   jax.ShapeDtypeStruct((2 * fields, cols_x, cols_y), jnp.float32)],
    )(forced, coupling, ctop, ratio, inv)


def interface_values(y_ends, uv_ends, place, peers):
    fields = 4
    y0 = y_ends[:, 0:fields]
    y1 = y_ends[:, fields:2 * fields]
    rest = jnp.repeat(uv_ends, 2, axis=1)
    u0 = rest[:, 0:4]
    u1 = rest[:, 4:8]
    v0 = rest[:, 8:12]
    v1 = rest[:, 12:16]
    pt, qt, pb, qb = [], [], [], []
    for q in range(peers):
        if q == 0:
            pt_q, qt_q = y0[q], v0[q]
            pb_q, qb_q = y1[q], v1[q]
        else:
            inv = 1.0 / (1.0 - u0[q] * qb[-1])
            pt_q = (y0[q] + u0[q] * pb[-1]) * inv
            qt_q = v0[q] * inv
            pb_q = y1[q] + u1[q] * (pb[-1] + qb[-1] * pt_q)
            qb_q = v1[q] + u1[q] * qb[-1] * qt_q
        pt.append(pt_q)
        qt.append(qt_q)
        pb.append(pb_q)
        qb.append(qb_q)
    tops = [None] * peers
    bots = [None] * peers
    t_next = jnp.zeros_like(pt[0])
    for q in range(peers - 1, -1, -1):
        tops[q] = pt[q] + qt[q] * t_next
        bots[q] = pb[q] + qb[q] * t_next
        t_next = tops[q]
    above = jnp.zeros_like(pt[0])
    below = jnp.zeros_like(pt[0])
    for q in range(peers):
        if q >= 1:
            above = jnp.where(place == q, bots[q - 1], above)
        if q <= peers - 2:
            below = jnp.where(place == q, tops[q + 1], below)
    return above, below


def gather_by_permutes(part, axis, place, peers):
    received = [part]
    for hop in range(1, peers):
        shift = [(i, (i + hop) % peers) for i in range(peers)]
        received.append(lax.ppermute(part, axis, shift))
    rows = []
    for q in range(peers):
        row = received[0]
        for hop in range(1, peers):
            row = jnp.where((place - hop) % peers == q, received[hop], row)
        rows.append(row)
    return jnp.stack(rows)


def per_device(state, mixing, depth_levels, wind):
    fields, lev_count, col_x, col_y = state.shape
    total_x, total_y = depth_levels.shape
    peers_z = lax.axis_size("gz")
    place_z = lax.axis_index("gz")
    start_x = lax.axis_index("gx") * col_x
    start_y = lax.axis_index("gy") * col_y
    start_z = place_z * lev_count
    down_z = [(i, i + 1) for i in range(peers_z - 1)]
    mix_above = lax.ppermute(mixing[:, lev_count - 1], "gz", down_z)
    levels = start_z + jnp.arange(lev_count, dtype=jnp.int32)
    depth_inner = lax.dynamic_slice(depth_levels, (start_x, start_y), (col_x, col_y))
    wet_here = (levels[:, None, None] < depth_inner[None]).astype(jnp.float32)
    wet_next = ((levels + 1)[:, None, None] < depth_inner[None]).astype(jnp.float32)
    coupling = mixing * (wet_here * wet_next)[None]
    wet_up = ((start_z - 1) < depth_inner).astype(jnp.float32)
    ctop = mix_above * (wet_up * wet_here[0])[None]
    ctop = jnp.where(place_z > 0, ctop, 0.0)
    ratio, inv, u, v, uv_ends = coupling_solve(coupling, ctop)
    uv_all = lax.all_gather(uv_ends, "gz")
    padded = padded_2(state, (("gx", 2), ("gy", 3)), 1)
    row_index = (start_x - 1 + jnp.arange(col_x + 2, dtype=jnp.int32)) % total_x
    col_index = (start_y - 1 + jnp.arange(col_y + 2, dtype=jnp.int32)) % total_y
    depth_pad = jnp.take(jnp.take(depth_levels, row_index, axis=0), col_index, axis=1)
    wet_pad = (levels[:, None, None] < depth_pad[None]).astype(jnp.float32)
    density_field = density_of(padded, wet_pad)
    inclusive = jnp.cumsum(density_field, axis=0)
    column_total = inclusive[-1]
    shallower = jnp.zeros_like(column_total)
    for hop in range(1, peers_z):
        pairs_z = [(i, i + hop) for i in range(peers_z - hop)]
        shallower = shallower + lax.ppermute(column_total, "gz", pairs_z)
    pressure = 0.03 * (shallower[None] + inclusive - 0.5 * density_field)
    face_row = start_y - 1 + jnp.arange(col_y + 1, dtype=jnp.int32)
    wall_face = ((face_row >= 0) & (face_row <= total_y - 2)).astype(jnp.float32)
    row_global = start_y + jnp.arange(col_y, dtype=jnp.int32)
    coriolis = 0.5 + (row_global.astype(jnp.float32) + 0.5) / total_y
    forced = advance(padded, wet_pad, pressure, wall_face, coriolis)
    wet_inner = wet_pad[:, 1:-1, 1:-1]
    top_level = (levels == 0).astype(jnp.float32)
    forced = forced.at[2:].add(wind[:, None] * top_level[None, :, None, None] * wet_inner[None])
    y, y_ends = field_solve(forced, coupling, ctop, ratio, inv)
    y_all = gather_by_permutes(y_ends, "gz", place_z, peers_z)
    x_above, x_below = interface_values(y_all, uv_all, place_z, peers_z)
    u4 = jnp.repeat(u, 2, axis=0)
    v4 = jnp.repeat(v, 2, axis=0)
    return y + x_above[:, None] * u4 + x_below[:, None] * v4


def solution(mesh):
    return jax.shard_map(
        per_device,
        mesh=mesh,
        in_specs=(P(None, "gz", "gx", "gy"), P(None, "gz", "gx", "gy"), P(), P(None, "gx", "gy")),
        out_specs=P(None, "gz", "gx", "gy"),
        check_vma=False,
    )
```

```python
import jax
import jax.numpy as jnp
from jax import lax
from jax.experimental import pallas as pl
from jax.experimental.pallas import tpu as pltpu
from jax.sharding import PartitionSpec as P


def padded_2(array, sides, width):
    for axis, dim in sides:
        peers, length = (lax.axis_size(axis), array.shape[dim])
        up = [(i, (i + 1) % peers) for i in range(peers)]
        down = [(j, i) for i, j in up]
        last = lax.slice_in_dim(array, length - width, length, axis=dim)
        initial = lax.slice_in_dim(array, 0, width, axis=dim)
        before = lax.ppermute(last, axis, up)
        after = lax.ppermute(initial, axis, down)
        array = jnp.concatenate([before, array, after], axis=dim)
    return array


def density_of(fields, wet_mask):
    return (-0.3 * fields[0] + 0.7 * fields[1] - 0.05 * fields[0] * fields[0]) * wet_mask


def advance(padded, wet_pad, pressure, wall_face, coriolis):
    wet_x = wet_pad[:, :-1, 1:-1] * wet_pad[:, 1:, 1:-1]
    wet_y = wet_pad[:, 1:-1, :-1] * wet_pad[:, 1:-1, 1:] * wall_face
    east_vel = 0.5 * (padded[2, :, :-1, 1:-1] + padded[2, :, 1:, 1:-1]) * wet_x
    north_vel = 0.5 * (padded[3, :, 1:-1, :-1] + padded[3, :, 1:-1, 1:]) * wet_y
    west_side = padded[:, :, :-1, 1:-1]
    east_side = padded[:, :, 1:, 1:-1]
    flux_x = 0.25 * (
        jnp.maximum(east_vel, 0.0) * west_side + jnp.minimum(east_vel, 0.0) * east_side
    ) - 0.08 * wet_x * (east_side - west_side)
    south_side = padded[:, :, 1:-1, :-1]
    north_side = padded[:, :, 1:-1, 1:]
    flux_y = 0.25 * (
        jnp.maximum(north_vel, 0.0) * south_side + jnp.minimum(north_vel, 0.0) * north_side
    ) - 0.08 * wet_y * (north_side - south_side)
    interior = padded[:, :, 1:-1, 1:-1]
    moved = interior - (
        flux_x[:, :, 1:] - flux_x[:, :, :-1] + flux_y[:, :, :, 1:] - flux_y[:, :, :, :-1]
    )
    centre = pressure[:, 1:-1, 1:-1]
    grad_x = 0.5 * (
        wet_x[:, 1:] * (pressure[:, 2:, 1:-1] - centre)
        + wet_x[:, :-1] * (centre - pressure[:, :-2, 1:-1])
    )
    grad_y = 0.5 * (
        wet_y[:, :, 1:] * (pressure[:, 1:-1, 2:] - centre)
        + wet_y[:, :, :-1] * (centre - pressure[:, 1:-1, :-2])
    )
    east_new = moved[2] + 0.3 * coriolis * interior[3] - grad_x
    north_new = moved[3] - 0.3 * coriolis * interior[2] - grad_y
    wet_inner = wet_pad[:, 1:-1, 1:-1]
    return jnp.stack([moved[0], moved[1], east_new, north_new]) * wet_inner


def coupling_kernel(c_ref, ctop_ref, ratio_ref, inv_ref, u_ref, v_ref, ends_ref):
    levels = c_ref.shape[1]
    ctop = ctop_ref[...]
    ratio_prev = None
    vu_prev = None
    for k in range(levels):
        above = ctop if k == 0 else c_ref[:, k - 1]
        below = c_ref[:, k]
        if k == 0:
            divisor = 1.0 + above + below
        else:
            divisor = 1.0 + above * (1.0 - ratio_prev) + below
        inv = 1.0 / divisor
        ratio = below * inv
        vu = ctop * inv if k == 0 else above * vu_prev * inv
        ratio_ref[:, k] = ratio
        inv_ref[:, k] = inv
        u_ref[:, k] = vu
        ratio_prev, vu_prev = ratio, vu
    u_later = vu_prev
    v_later = ratio_prev
    pairs = c_ref.shape[0]
    ends_ref[pairs:2 * pairs] = u_later
    ends_ref[3 * pairs:4 * pairs] = v_later
    v_ref[:, levels - 1] = v_later
    for k in range(levels - 2, -1, -1):
        ratio = ratio_ref[:, k]
        u_later = u_ref[:, k] + ratio * u_later
        v_later = ratio * v_later
        u_ref[:, k] = u_later
        v_ref[:, k] = v_later
    ends_ref[0:pairs] = u_later
    ends_ref[2 * pairs:3 * pairs] = v_later


def field_kernel(f_ref, c_ref, ctop_ref, ratio_ref, inv_ref, y_ref, ends_ref):
    levels = f_ref.shape[1]
    fields = f_ref.shape[0]
    vy = None
    for k in range(levels):
        inv = jnp.repeat(inv_ref[:, k], 2, axis=0)
        rhs = f_ref[:, k]
        if k == 0:
            vy = rhs * inv
        else:
            above = jnp.repeat(c_ref[:, k - 1], 2, axis=0)
            vy = (rhs + above * vy) * inv
        y_ref[:, k] = vy
    y_later = vy
    ends_ref[fields:2 * fields] = y_later
    for k in range(levels - 2, -1, -1):
        ratio = jnp.repeat(ratio_ref[:, k], 2, axis=0)
        y_later = y_ref[:, k] + ratio * y_later
        y_ref[:, k] = y_later
    ends_ref[0:fields] = y_later


def _specs(lead, levels, bx, cols_y):
    return pl.BlockSpec((lead, levels, bx, cols_y), lambda i: (0, 0, i, 0))


def _plane_spec(lead, bx, cols_y):
    return pl.BlockSpec((lead, bx, cols_y), lambda i: (0, i, 0))


def coupling_solve(coupling, ctop):
    pairs, levels, cols_x, cols_y = coupling.shape
    bx = 8 if cols_x % 8 == 0 else cols_x
    cspec = _specs(pairs, levels, bx, cols_y)
    full = jax.ShapeDtypeStruct(coupling.shape, jnp.float32)
    return pl.pallas_call(
        coupling_kernel,
        grid=(cols_x // bx,),
        in_specs=[cspec, _plane_spec(pairs, bx, cols_y)],
        out_specs=[cspec, cspec, cspec, cspec, _plane_spec(4 * pairs, bx, cols_y)],
        out_shape=[full, full, full, full,
                   jax.ShapeDtypeStruct((4 * pairs, cols_x, cols_y), jnp.float32)],
    )(coupling, ctop)


def field_solve(forced, coupling, ctop, ratio, inv):
    fields, levels, cols_x, cols_y = forced.shape
    pairs = coupling.shape[0]
    bx = 8 if cols_x % 8 == 0 else cols_x
    fspec = _specs(fields, levels, bx, cols_y)
    cspec = _specs(pairs, levels, bx, cols_y)
    return pl.pallas_call(
        field_kernel,
        grid=(cols_x // bx,),
        in_specs=[fspec, cspec, _plane_spec(pairs, bx, cols_y), cspec, cspec],
        out_specs=[fspec, _plane_spec(2 * fields, bx, cols_y)],
        out_shape=[jax.ShapeDtypeStruct(forced.shape, jnp.float32),
                   jax.ShapeDtypeStruct((2 * fields, cols_x, cols_y), jnp.float32)],
    )(forced, coupling, ctop, ratio, inv)


def interface_values(y_ends, uv_ends, place, peers):
    fields = 4
    y0 = y_ends[:, 0:fields]
    y1 = y_ends[:, fields:2 * fields]
    rest = jnp.repeat(uv_ends, 2, axis=1)
    u0 = rest[:, 0:4]
    u1 = rest[:, 4:8]
    v0 = rest[:, 8:12]
    v1 = rest[:, 12:16]
    pt, qt, pb, qb = [], [], [], []
    for q in range(peers):
        if q == 0:
            pt_q, qt_q = y0[q], v0[q]
            pb_q, qb_q = y1[q], v1[q]
        else:
            inv = 1.0 / (1.0 - u0[q] * qb[-1])
            pt_q = (y0[q] + u0[q] * pb[-1]) * inv
            qt_q = v0[q] * inv
            pb_q = y1[q] + u1[q] * (pb[-1] + qb[-1] * pt_q)
            qb_q = v1[q] + u1[q] * qb[-1] * qt_q
        pt.append(pt_q)
        qt.append(qt_q)
        pb.append(pb_q)
        qb.append(qb_q)
    tops = [None] * peers
    bots = [None] * peers
    t_next = jnp.zeros_like(pt[0])
    for q in range(peers - 1, -1, -1):
        tops[q] = pt[q] + qt[q] * t_next
        bots[q] = pb[q] + qb[q] * t_next
        t_next = tops[q]
    above = jnp.zeros_like(pt[0])
    below = jnp.zeros_like(pt[0])
    for q in range(peers):
        if q >= 1:
            above = jnp.where(place == q, bots[q - 1], above)
        if q <= peers - 2:
            below = jnp.where(place == q, tops[q + 1], below)
    return above, below


def gather_by_permutes(part, axis, place, peers):
    received = [part]
    for hop in range(1, peers):
        shift = [(i, (i + hop) % peers) for i in range(peers)]
        received.append(lax.ppermute(part, axis, shift))
    rows = []
    for q in range(peers):
        row = received[0]
        for hop in range(1, peers):
            row = jnp.where((place - hop) % peers == q, received[hop], row)
        rows.append(row)
    return jnp.stack(rows)


def _density(t, s, w):
    return (-0.3 * t + 0.7 * s - 0.05 * t * t) * w


def _flux(vel, lo, hi, w):
    return 0.25 * (jnp.maximum(vel, 0.0) * lo + jnp.minimum(vel, 0.0) * hi) - 0.08 * w * (hi - lo)


def fused_kernel(st_ref, xw_ref, xe_ref, ys_ref, yn_ref,
                 dc_ref, de_ref, dw_ref, dn_ref, ds_ref,
                 dxw_ref, dxe_ref, dys_ref, dyn_ref,
                 sc_ref, sxw_ref, sxe_ref, sys_ref, syn_ref,
                 lane_ref, wind_ref, c_ref, inv_ref, ratio_ref,
                 y_ref, ends_ref):
    fields, levels, nx, ny = st_ref.shape
    row = lax.broadcasted_iota(jnp.int32, (nx, ny), 0)
    lane = lax.broadcasted_iota(jnp.int32, (nx, ny), 1)
    wall_n = lane_ref[0:1]
    wall_s = lane_ref[1:2]
    cor03 = lane_ref[2:3]
    d_c, d_e, d_w, d_n, d_s = dc_ref[...], de_ref[...], dw_ref[...], dn_ref[...], ds_ref[...]
    d_xw, d_xe, d_ys, d_yn = dxw_ref[...], dxe_ref[...], dys_ref[...], dyn_ref[...]

    def east(r, h):
        return jnp.where(row == nx - 1, h, pltpu.roll(r, nx - 1, 0))

    def west(r, h):
        return jnp.where(row == 0, h, pltpu.roll(r, 1, 0))

    def north(r, h):
        return jnp.where(lane == ny - 1, h, pltpu.roll(r, ny - 1, 1))

    def south(r, h):
        return jnp.where(lane == 0, h, pltpu.roll(r, 1, 1))

    def level(k, run, vy_prev):
        wc = (k < d_c).astype(jnp.float32)
        we = (k < d_e).astype(jnp.float32)
        ww = (k < d_w).astype(jnp.float32)
        wn = (k < d_n).astype(jnp.float32)
        ws = (k < d_s).astype(jnp.float32)
        wxw = (k < d_xw).astype(jnp.float32)
        wxe = (k < d_xe).astype(jnp.float32)
        wys = (k < d_ys).astype(jnp.float32)
        wyn = (k < d_yn).astype(jnp.float32)
        cen = [st_ref[f, k] for f in range(fields)]
        hxw = [xw_ref[f, k] for f in range(fields)]
        hxe = [xe_ref[f, k] for f in range(fields)]
        hys = [ys_ref[f, k] for f in range(fields)]
        hyn = [yn_ref[f, k] for f in range(fields)]
        run_c, run_xw, run_xe, run_ys, run_yn = run
        den_c = _density(cen[0], cen[1], wc)
        den_xw = _density(hxw[0], hxw[1], wxw)
        den_xe = _density(hxe[0], hxe[1], wxe)
        den_ys = _density(hys[0], hys[1], wys)
        den_yn = _density(hyn[0], hyn[1], wyn)
        run_c = run_c + den_c
        run_xw = run_xw + den_xw
        run_xe = run_xe + den_xe
        run_ys = run_ys + den_ys
        run_yn = run_yn + den_yn
        p_c = 0.03 * (sc_ref[...] + run_c - 0.5 * den_c)
        p_xw = 0.03 * (sxw_ref[...] + run_xw - 0.5 * den_xw)
        p_xe = 0.03 * (sxe_ref[...] + run_xe - 0.5 * den_xe)
        p_ys = 0.03 * (sys_ref[...] + run_ys - 0.5 * den_ys)
        p_yn = 0.03 * (syn_ref[...] + run_yn - 0.5 * den_yn)
        p_e = east(p_c, p_xe)
        p_w = west(p_c, p_xw)
        p_n = north(p_c, p_yn)
        p_s = south(p_c, p_ys)
        face_e = wc * we
        face_w = ww * wc
        face_n = wc * wn * wall_n
        face_s = ws * wc * wall_s
        nbr_e = [east(cen[f], hxe[f]) for f in range(fields)]
        nbr_w = [west(cen[f], hxw[f]) for f in range(fields)]
        nbr_n = [north(cen[f], hyn[f]) for f in range(fields)]
        nbr_s = [south(cen[f], hys[f]) for f in range(fields)]
        vel_e = 0.5 * (cen[2] + nbr_e[2]) * face_e
        vel_w = 0.5 * (nbr_w[2] + cen[2]) * face_w
        vel_n = 0.5 * (cen[3] + nbr_n[3]) * face_n
        vel_s = 0.5 * (nbr_s[3] + cen[3]) * face_s
        moved = []
        for f in range(fields):
            fe = _flux(vel_e, cen[f], nbr_e[f], face_e)
            fw = _flux(vel_w, nbr_w[f], cen[f], face_w)
            fn = _flux(vel_n, cen[f], nbr_n[f], face_n)
            fs = _flux(vel_s, nbr_s[f], cen[f], face_s)
            moved.append(cen[f] - (fe - fw + fn - fs))
        grad_x = 0.5 * (face_e * (p_e - p_c) + face_w * (p_c - p_w))
        grad_y = 0.5 * (face_n * (p_n - p_c) + face_s * (p_c - p_s))
        east_new = moved[2] + cor03 * cen[3] - grad_x
        north_new = moved[3] - cor03 * cen[2] - grad_y
        forced = [moved[0] * wc, moved[1] * wc, east_new * wc, north_new * wc]
        if isinstance(k, int) and k == 0:
            forced[2] = forced[2] + wind_ref[0] * wc
            forced[3] = forced[3] + wind_ref[1] * wc
        vy = []
        for f in range(fields):
            m = f // 2
            inv = inv_ref[m, k]
            if vy_prev is None:
                val = forced[f] * inv
            else:
                val = (forced[f] + c_ref[m, k - 1] * vy_prev[f]) * inv
            y_ref[f, k] = val
            vy.append(val)
        return (run_c, run_xw, run_xe, run_ys, run_yn), vy

    run0 = (jnp.zeros((nx, ny), jnp.float32), jnp.zeros((1, ny), jnp.float32),
            jnp.zeros((1, ny), jnp.float32), jnp.zeros((nx, 1), jnp.float32),
            jnp.zeros((nx, 1), jnp.float32))
    run, vy = level(0, run0, None)

    def step(k, carry):
        run, vy = carry
        run, vy = level(k, run, vy)
        return run, vy

    run, vy = lax.fori_loop(1, levels, step, (run, vy), unroll=2)
    for f in range(fields):
        ends_ref[fields + f] = vy[f]

    def back(j, later):
        k = levels - 2 - j
        out = []
        for f in range(fields):
            val = y_ref[f, k] + ratio_ref[f // 2, k] * later[f]
            y_ref[f, k] = val
            out.append(val)
        return out

    later = lax.fori_loop(0, levels - 1, back, vy, unroll=2)
    for f in range(fields):
        ends_ref[f] = later[f]


def fused_solve(*operands):
    st = operands[0]
    fields, levels, nx, ny = st.shape
    vmem = pl.BlockSpec(memory_space=pltpu.VMEM)
    return pl.pallas_call(
        fused_kernel,
        in_specs=[vmem] * len(operands),
        out_specs=[vmem, vmem],
        out_shape=[jax.ShapeDtypeStruct(st.shape, jnp.float32),
                   jax.ShapeDtypeStruct((2 * fields, nx, ny), jnp.float32)],
        compiler_params=pltpu.CompilerParams(vmem_limit_bytes=60 * 1024 * 1024),
    )(*operands)


def per_device(state, mixing, depth_levels, wind):
    fields, lev_count, col_x, col_y = state.shape
    total_x, total_y = depth_levels.shape
    peers_z = lax.axis_size("gz")
    place_z = lax.axis_index("gz")
    peers_x = lax.axis_size("gx")
    peers_y = lax.axis_size("gy")
    start_x = lax.axis_index("gx") * col_x
    start_y = lax.axis_index("gy") * col_y
    start_z = place_z * lev_count
    down_z = [(i, i + 1) for i in range(peers_z - 1)]
    mix_above = lax.ppermute(mixing[:, lev_count - 1], "gz", down_z)
    up_x = [(i, (i + 1) % peers_x) for i in range(peers_x)]
    dn_x = [(j, i) for i, j in up_x]
    up_y = [(i, (i + 1) % peers_y) for i in range(peers_y)]
    dn_y = [(j, i) for i, j in up_y]
    halo_xw = lax.ppermute(state[:, :, col_x - 1:], "gx", up_x)
    halo_xe = lax.ppermute(state[:, :, :1], "gx", dn_x)
    halo_ys = lax.ppermute(state[:, :, :, col_y - 1:], "gy", up_y)
    halo_yn = lax.ppermute(state[:, :, :, :1], "gy", dn_y)
    levels = start_z + jnp.arange(lev_count, dtype=jnp.int32)
    row_index = (start_x - 1 + jnp.arange(col_x + 2, dtype=jnp.int32)) % total_x
    col_index = (start_y - 1 + jnp.arange(col_y + 2, dtype=jnp.int32)) % total_y
    depth_pad = jnp.take(jnp.take(depth_levels, row_index, axis=0), col_index, axis=1) - start_z
    d_c = depth_pad[1:-1, 1:-1]
    d_e = depth_pad[2:, 1:-1]
    d_w = depth_pad[:-2, 1:-1]
    d_n = depth_pad[1:-1, 2:]
    d_s = depth_pad[1:-1, :-2]
    d_xw = depth_pad[0:1, 1:-1]
    d_xe = depth_pad[col_x + 1:, 1:-1]
    d_ys = depth_pad[1:-1, 0:1]
    d_yn = depth_pad[1:-1, col_y + 1:]
    local = jnp.arange(lev_count, dtype=jnp.int32)
    wet_here = (local[:, None, None] < d_c[None]).astype(jnp.float32)
    wet_next = ((local + 1)[:, None, None] < d_c[None]).astype(jnp.float32)
    coupling = mixing * (wet_here * wet_next)[None]
    wet_up = (-1 < d_c).astype(jnp.float32)
    ctop = mix_above * (wet_up * wet_here[0])[None]
    ctop = jnp.where(place_z > 0, ctop, 0.0)
    ratio, inv, u, v, uv_ends = coupling_solve(coupling, ctop)
    uv_all = lax.all_gather(uv_ends, "gz")
    lev3 = local[:, None, None]
    tot_c = jnp.sum(density_of(state, (lev3 < d_c[None]).astype(jnp.float32)), axis=0)
    tot_xw = jnp.sum(density_of(halo_xw, (lev3 < d_xw[None]).astype(jnp.float32)), axis=0)
    tot_xe = jnp.sum(density_of(halo_xe, (lev3 < d_xe[None]).astype(jnp.float32)), axis=0)
    tot_ys = jnp.sum(density_of(halo_ys, (lev3 < d_ys[None]).astype(jnp.float32)), axis=0)
    tot_yn = jnp.sum(density_of(halo_yn, (lev3 < d_yn[None]).astype(jnp.float32)), axis=0)
    side = jnp.zeros((2, col_y), jnp.float32)
    side = side.at[0, :col_x].set(tot_ys[:, 0]).at[1, :col_x].set(tot_yn[:, 0])
    pack = jnp.concatenate([tot_c, tot_xw, tot_xe, side], axis=0)
    shallower = jnp.zeros_like(pack)
    for hop in range(1, peers_z):
        pairs_z = [(i, i + hop) for i in range(peers_z - hop)]
        shallower = shallower + lax.ppermute(pack, "gz", pairs_z)
    s_c = shallower[:col_x]
    s_xw = shallower[col_x:col_x + 1]
    s_xe = shallower[col_x + 1:col_x + 2]
    s_ys = shallower[col_x + 2, :col_x][:, None]
    s_yn = shallower[col_x + 3, :col_x][:, None]
    face_row = start_y + jnp.arange(col_y, dtype=jnp.int32)
    wall_n = (face_row <= total_y - 2).astype(jnp.float32)
    wall_s = (face_row - 1 >= 0).astype(jnp.float32)
    coriolis = 0.5 + (face_row.astype(jnp.float32) + 0.5) / total_y
    lanes = jnp.stack([wall_n, wall_s, 0.3 * coriolis] + [jnp.zeros_like(wall_n)] * 5)
    wind_top = jnp.where(place_z == 0, wind, 0.0)
    y, y_ends = fused_solve(state, halo_xw, halo_xe, halo_ys, halo_yn,
                            d_c, d_e, d_w, d_n, d_s, d_xw, d_xe, d_ys, d_yn,
                            s_c, s_xw, s_xe, s_ys, s_yn, lanes, wind_top,
                            coupling, inv, ratio)
    y_all = gather_by_permutes(y_ends, "gz", place_z, peers_z)
    x_above, x_below = interface_values(y_all, uv_all, place_z, peers_z)
    u4 = jnp.repeat(u, 2, axis=0)
    v4 = jnp.repeat(v, 2, axis=0)
    return y + x_above[:, None] * u4 + x_below[:, None] * v4


def solution(mesh):
    return jax.shard_map(
        per_device,
        mesh=mesh,
        in_specs=(P(None, "gz", "gx", "gy"), P(None, "gz", "gx", "gy"), P(), P(None, "gx", "gy")),
        out_specs=P(None, "gz", "gx", "gy"),
        check_vma=False,
    )
```

```python
import jax
import jax.numpy as jnp
from jax import lax
from jax.experimental import pallas as pl
from jax.experimental.pallas import tpu as pltpu
from jax.sharding import PartitionSpec as P


def padded_2(array, sides, width):
    for axis, dim in sides:
        peers, length = (lax.axis_size(axis), array.shape[dim])
        up = [(i, (i + 1) % peers) for i in range(peers)]
        down = [(j, i) for i, j in up]
        last = lax.slice_in_dim(array, length - width, length, axis=dim)
        initial = lax.slice_in_dim(array, 0, width, axis=dim)
        before = lax.ppermute(last, axis, up)
        after = lax.ppermute(initial, axis, down)
        array = jnp.concatenate([before, array, after], axis=dim)
    return array


def density_of(fields, wet_mask):
    return (-0.3 * fields[0] + 0.7 * fields[1] - 0.05 * fields[0] * fields[0]) * wet_mask


def advance(padded, wet_pad, pressure, wall_face, coriolis):
    wet_x = wet_pad[:, :-1, 1:-1] * wet_pad[:, 1:, 1:-1]
    wet_y = wet_pad[:, 1:-1, :-1] * wet_pad[:, 1:-1, 1:] * wall_face
    east_vel = 0.5 * (padded[2, :, :-1, 1:-1] + padded[2, :, 1:, 1:-1]) * wet_x
    north_vel = 0.5 * (padded[3, :, 1:-1, :-1] + padded[3, :, 1:-1, 1:]) * wet_y
    west_side = padded[:, :, :-1, 1:-1]
    east_side = padded[:, :, 1:, 1:-1]
    flux_x = 0.25 * (
        jnp.maximum(east_vel, 0.0) * west_side + jnp.minimum(east_vel, 0.0) * east_side
    ) - 0.08 * wet_x * (east_side - west_side)
    south_side = padded[:, :, 1:-1, :-1]
    north_side = padded[:, :, 1:-1, 1:]
    flux_y = 0.25 * (
        jnp.maximum(north_vel, 0.0) * south_side + jnp.minimum(north_vel, 0.0) * north_side
    ) - 0.08 * wet_y * (north_side - south_side)
    interior = padded[:, :, 1:-1, 1:-1]
    moved = interior - (
        flux_x[:, :, 1:] - flux_x[:, :, :-1] + flux_y[:, :, :, 1:] - flux_y[:, :, :, :-1]
    )
    centre = pressure[:, 1:-1, 1:-1]
    grad_x = 0.5 * (
        wet_x[:, 1:] * (pressure[:, 2:, 1:-1] - centre)
        + wet_x[:, :-1] * (centre - pressure[:, :-2, 1:-1])
    )
    grad_y = 0.5 * (
        wet_y[:, :, 1:] * (pressure[:, 1:-1, 2:] - centre)
        + wet_y[:, :, :-1] * (centre - pressure[:, 1:-1, :-2])
    )
    east_new = moved[2] + 0.3 * coriolis * interior[3] - grad_x
    north_new = moved[3] - 0.3 * coriolis * interior[2] - grad_y
    wet_inner = wet_pad[:, 1:-1, 1:-1]
    return jnp.stack([moved[0], moved[1], east_new, north_new]) * wet_inner


def coupling_kernel(c_ref, ctop_ref, ratio_ref, inv_ref, u_ref, v_ref, ends_ref):
    levels = c_ref.shape[1]
    ctop = ctop_ref[...]
    ratio_prev = None
    vu_prev = None
    for k in range(levels):
        above = ctop if k == 0 else c_ref[:, k - 1]
        below = c_ref[:, k]
        if k == 0:
            divisor = 1.0 + above + below
        else:
            divisor = 1.0 + above * (1.0 - ratio_prev) + below
        inv = 1.0 / divisor
        ratio = below * inv
        vu = ctop * inv if k == 0 else above * vu_prev * inv
        ratio_ref[:, k] = ratio
        inv_ref[:, k] = inv
        u_ref[:, k] = vu
        ratio_prev, vu_prev = ratio, vu
    u_later = vu_prev
    v_later = ratio_prev
    pairs = c_ref.shape[0]
    ends_ref[pairs:2 * pairs] = u_later
    ends_ref[3 * pairs:4 * pairs] = v_later
    v_ref[:, levels - 1] = v_later
    for k in range(levels - 2, -1, -1):
        ratio = ratio_ref[:, k]
        u_later = u_ref[:, k] + ratio * u_later
        v_later = ratio * v_later
        u_ref[:, k] = u_later
        v_ref[:, k] = v_later
    ends_ref[0:pairs] = u_later
    ends_ref[2 * pairs:3 * pairs] = v_later


def field_kernel(f_ref, c_ref, ctop_ref, ratio_ref, inv_ref, y_ref, ends_ref):
    levels = f_ref.shape[1]
    fields = f_ref.shape[0]
    vy = None
    for k in range(levels):
        inv = jnp.repeat(inv_ref[:, k], 2, axis=0)
        rhs = f_ref[:, k]
        if k == 0:
            vy = rhs * inv
        else:
            above = jnp.repeat(c_ref[:, k - 1], 2, axis=0)
            vy = (rhs + above * vy) * inv
        y_ref[:, k] = vy
    y_later = vy
    ends_ref[fields:2 * fields] = y_later
    for k in range(levels - 2, -1, -1):
        ratio = jnp.repeat(ratio_ref[:, k], 2, axis=0)
        y_later = y_ref[:, k] + ratio * y_later
        y_ref[:, k] = y_later
    ends_ref[0:fields] = y_later


def _specs(lead, levels, bx, cols_y):
    return pl.BlockSpec((lead, levels, bx, cols_y), lambda i: (0, 0, i, 0))


def _plane_spec(lead, bx, cols_y):
    return pl.BlockSpec((lead, bx, cols_y), lambda i: (0, i, 0))


def coupling_solve(coupling, ctop):
    pairs, levels, cols_x, cols_y = coupling.shape
    bx = 8 if cols_x % 8 == 0 else cols_x
    cspec = _specs(pairs, levels, bx, cols_y)
    full = jax.ShapeDtypeStruct(coupling.shape, jnp.float32)
    return pl.pallas_call(
        coupling_kernel,
        grid=(cols_x // bx,),
        in_specs=[cspec, _plane_spec(pairs, bx, cols_y)],
        out_specs=[cspec, cspec, cspec, cspec, _plane_spec(4 * pairs, bx, cols_y)],
        out_shape=[full, full, full, full,
                   jax.ShapeDtypeStruct((4 * pairs, cols_x, cols_y), jnp.float32)],
    )(coupling, ctop)


def field_solve(forced, coupling, ctop, ratio, inv):
    fields, levels, cols_x, cols_y = forced.shape
    pairs = coupling.shape[0]
    bx = 8 if cols_x % 8 == 0 else cols_x
    fspec = _specs(fields, levels, bx, cols_y)
    cspec = _specs(pairs, levels, bx, cols_y)
    return pl.pallas_call(
        field_kernel,
        grid=(cols_x // bx,),
        in_specs=[fspec, cspec, _plane_spec(pairs, bx, cols_y), cspec, cspec],
        out_specs=[fspec, _plane_spec(2 * fields, bx, cols_y)],
        out_shape=[jax.ShapeDtypeStruct(forced.shape, jnp.float32),
                   jax.ShapeDtypeStruct((2 * fields, cols_x, cols_y), jnp.float32)],
    )(forced, coupling, ctop, ratio, inv)


def interface_values(y_ends, uv_ends, place, peers):
    fields = 4
    y0 = y_ends[:, 0:fields]
    y1 = y_ends[:, fields:2 * fields]
    rest = jnp.repeat(uv_ends, 2, axis=1)
    u0 = rest[:, 0:4]
    u1 = rest[:, 4:8]
    v0 = rest[:, 8:12]
    v1 = rest[:, 12:16]
    pt, qt, pb, qb = [], [], [], []
    for q in range(peers):
        if q == 0:
            pt_q, qt_q = y0[q], v0[q]
            pb_q, qb_q = y1[q], v1[q]
        else:
            inv = 1.0 / (1.0 - u0[q] * qb[-1])
            pt_q = (y0[q] + u0[q] * pb[-1]) * inv
            qt_q = v0[q] * inv
            pb_q = y1[q] + u1[q] * (pb[-1] + qb[-1] * pt_q)
            qb_q = v1[q] + u1[q] * qb[-1] * qt_q
        pt.append(pt_q)
        qt.append(qt_q)
        pb.append(pb_q)
        qb.append(qb_q)
    tops = [None] * peers
    bots = [None] * peers
    t_next = jnp.zeros_like(pt[0])
    for q in range(peers - 1, -1, -1):
        tops[q] = pt[q] + qt[q] * t_next
        bots[q] = pb[q] + qb[q] * t_next
        t_next = tops[q]
    above = jnp.zeros_like(pt[0])
    below = jnp.zeros_like(pt[0])
    for q in range(peers):
        if q >= 1:
            above = jnp.where(place == q, bots[q - 1], above)
        if q <= peers - 2:
            below = jnp.where(place == q, tops[q + 1], below)
    return above, below


def gather_by_permutes(part, axis, place, peers):
    received = [part]
    for hop in range(1, peers):
        shift = [(i, (i + hop) % peers) for i in range(peers)]
        received.append(lax.ppermute(part, axis, shift))
    rows = []
    for q in range(peers):
        row = received[0]
        for hop in range(1, peers):
            row = jnp.where((place - hop) % peers == q, received[hop], row)
        rows.append(row)
    return jnp.stack(rows)


def _density(t, s, w):
    return (-0.3 * t + 0.7 * s - 0.05 * t * t) * w


def _flux(vel, lo, hi, w):
    return 0.25 * (jnp.maximum(vel, 0.0) * lo + jnp.minimum(vel, 0.0) * hi) - 0.08 * w * (hi - lo)


def fused_kernel(st_ref, xw_ref, xe_ref, ys_ref, yn_ref,
                 dc_ref, de_ref, dw_ref, dn_ref, ds_ref,
                 dxw_ref, dxe_ref, dys_ref, dyn_ref,
                 sc_ref, sxw_ref, sxe_ref, sys_ref, syn_ref,
                 lane_ref, wind_ref, c_ref, inv_ref, ratio_ref,
                 y_ref, ends_ref):
    fields, levels, nx, ny = st_ref.shape
    row = lax.broadcasted_iota(jnp.int32, (nx, ny), 0)
    lane = lax.broadcasted_iota(jnp.int32, (nx, ny), 1)
    wall_n = lane_ref[0:1]
    wall_s = lane_ref[1:2]
    cor03 = lane_ref[2:3]
    d_c, d_e, d_w, d_n, d_s = dc_ref[...], de_ref[...], dw_ref[...], dn_ref[...], ds_ref[...]
    d_xw, d_xe, d_ys, d_yn = dxw_ref[...], dxe_ref[...], dys_ref[...], dyn_ref[...]

    def east(r, h):
        return jnp.where(row == nx - 1, h, pltpu.roll(r, nx - 1, 0))

    def west(r, h):
        return jnp.where(row == 0, h, pltpu.roll(r, 1, 0))

    def north(r, h):
        return jnp.where(lane == ny - 1, h, pltpu.roll(r, ny - 1, 1))

    def south(r, h):
        return jnp.where(lane == 0, h, pltpu.roll(r, 1, 1))

    def level(k, run, vy_prev):
        wc = (k < d_c).astype(jnp.float32)
        we = (k < d_e).astype(jnp.float32)
        ww = (k < d_w).astype(jnp.float32)
        wn = (k < d_n).astype(jnp.float32)
        ws = (k < d_s).astype(jnp.float32)
        wxw = (k < d_xw).astype(jnp.float32)
        wxe = (k < d_xe).astype(jnp.float32)
        wys = (k < d_ys).astype(jnp.float32)
        wyn = (k < d_yn).astype(jnp.float32)
        cen = [st_ref[f, k] for f in range(fields)]
        hxw = [xw_ref[f, pl.ds(k, 1), :] for f in range(fields)]
        hxe = [xe_ref[f, pl.ds(k, 1), :] for f in range(fields)]
        hys = [ys_ref[f, k] for f in range(fields)]
        hyn = [yn_ref[f, k] for f in range(fields)]
        run_c, run_xw, run_xe, run_ys, run_yn = run
        den_c = _density(cen[0], cen[1], wc)
        den_xw = _density(hxw[0], hxw[1], wxw)
        den_xe = _density(hxe[0], hxe[1], wxe)
        den_ys = _density(hys[0], hys[1], wys)
        den_yn = _density(hyn[0], hyn[1], wyn)
        run_c = run_c + den_c
        run_xw = run_xw + den_xw
        run_xe = run_xe + den_xe
        run_ys = run_ys + den_ys
        run_yn = run_yn + den_yn
        p_c = 0.03 * (sc_ref[...] + run_c - 0.5 * den_c)
        p_xw = 0.03 * (sxw_ref[...] + run_xw - 0.5 * den_xw)
        p_xe = 0.03 * (sxe_ref[...] + run_xe - 0.5 * den_xe)
        p_ys = 0.03 * (sys_ref[...] + run_ys - 0.5 * den_ys)
        p_yn = 0.03 * (syn_ref[...] + run_yn - 0.5 * den_yn)
        p_e = east(p_c, p_xe)
        p_w = west(p_c, p_xw)
        p_n = north(p_c, p_yn)
        p_s = south(p_c, p_ys)
        face_e = wc * we
        face_w = ww * wc
        face_n = wc * wn * wall_n
        face_s = ws * wc * wall_s
        nbr_e = [east(cen[f], hxe[f]) for f in range(fields)]
        nbr_w = [west(cen[f], hxw[f]) for f in range(fields)]
        nbr_n = [north(cen[f], hyn[f]) for f in range(fields)]
        nbr_s = [south(cen[f], hys[f]) for f in range(fields)]
        vel_e = 0.5 * (cen[2] + nbr_e[2]) * face_e
        vel_w = 0.5 * (nbr_w[2] + cen[2]) * face_w
        vel_n = 0.5 * (cen[3] + nbr_n[3]) * face_n
        vel_s = 0.5 * (nbr_s[3] + cen[3]) * face_s
        moved = []
        for f in range(fields):
            fe = _flux(vel_e, cen[f], nbr_e[f], face_e)
            fw = _flux(vel_w, nbr_w[f], cen[f], face_w)
            fn = _flux(vel_n, cen[f], nbr_n[f], face_n)
            fs = _flux(vel_s, nbr_s[f], cen[f], face_s)
            moved.append(cen[f] - (fe - fw + fn - fs))
        grad_x = 0.5 * (face_e * (p_e - p_c) + face_w * (p_c - p_w))
        grad_y = 0.5 * (face_n * (p_n - p_c) + face_s * (p_c - p_s))
        east_new = moved[2] + cor03 * cen[3] - grad_x
        north_new = moved[3] - cor03 * cen[2] - grad_y
        forced = [moved[0] * wc, moved[1] * wc, east_new * wc, north_new * wc]
        if isinstance(k, int) and k == 0:
            forced[2] = forced[2] + wind_ref[0] * wc
            forced[3] = forced[3] + wind_ref[1] * wc
        vy = []
        for f in range(fields):
            m = f // 2
            inv = inv_ref[m, k]
            if vy_prev is None:
                val = forced[f] * inv
            else:
                val = (forced[f] + c_ref[m, k - 1] * vy_prev[f]) * inv
            y_ref[f, k] = val
            vy.append(val)
        return (run_c, run_xw, run_xe, run_ys, run_yn), vy

    run0 = (jnp.zeros((nx, ny), jnp.float32), jnp.zeros((1, ny), jnp.float32),
            jnp.zeros((1, ny), jnp.float32), jnp.zeros((nx, 1), jnp.float32),
            jnp.zeros((nx, 1), jnp.float32))
    run, vy = level(0, run0, None)

    def step(k, carry):
        run, vy = carry
        run, vy = level(k, run, vy)
        return run, vy

    run, vy = lax.fori_loop(1, levels, step, (run, vy), unroll=2)
    for f in range(fields):
        ends_ref[fields + f] = vy[f]

    def back(j, later):
        k = levels - 2 - j
        out = []
        for f in range(fields):
            val = y_ref[f, k] + ratio_ref[f // 2, k] * later[f]
            y_ref[f, k] = val
            out.append(val)
        return out

    later = lax.fori_loop(0, levels - 1, back, vy, unroll=2)
    for f in range(fields):
        ends_ref[f] = later[f]


def fused_solve(*operands):
    st = operands[0]
    fields, levels, nx, ny = st.shape
    vmem = pl.BlockSpec(memory_space=pltpu.VMEM)
    return pl.pallas_call(
        fused_kernel,
        in_specs=[vmem] * len(operands),
        out_specs=[vmem, vmem],
        out_shape=[jax.ShapeDtypeStruct(st.shape, jnp.float32),
                   jax.ShapeDtypeStruct((2 * fields, nx, ny), jnp.float32)],
        compiler_params=pltpu.CompilerParams(vmem_limit_bytes=60 * 1024 * 1024),
    )(*operands)


def per_device(state, mixing, depth_levels, wind):
    fields, lev_count, col_x, col_y = state.shape
    total_x, total_y = depth_levels.shape
    peers_z = lax.axis_size("gz")
    place_z = lax.axis_index("gz")
    peers_x = lax.axis_size("gx")
    peers_y = lax.axis_size("gy")
    start_x = lax.axis_index("gx") * col_x
    start_y = lax.axis_index("gy") * col_y
    start_z = place_z * lev_count
    down_z = [(i, i + 1) for i in range(peers_z - 1)]
    mix_above = lax.ppermute(mixing[:, lev_count - 1], "gz", down_z)
    up_x = [(i, (i + 1) % peers_x) for i in range(peers_x)]
    dn_x = [(j, i) for i, j in up_x]
    up_y = [(i, (i + 1) % peers_y) for i in range(peers_y)]
    dn_y = [(j, i) for i, j in up_y]
    halo_xw = lax.ppermute(state[:, :, col_x - 1], "gx", up_x)
    halo_xe = lax.ppermute(state[:, :, 0], "gx", dn_x)
    halo_ys = lax.ppermute(state[:, :, :, col_y - 1], "gy", up_y)
    halo_yn = lax.ppermute(state[:, :, :, 0], "gy", dn_y)
    levels = start_z + jnp.arange(lev_count, dtype=jnp.int32)
    row_index = (start_x - 1 + jnp.arange(col_x + 2, dtype=jnp.int32)) % total_x
    col_index = (start_y - 1 + jnp.arange(col_y + 2, dtype=jnp.int32)) % total_y
    depth_pad = jnp.take(jnp.take(depth_levels, row_index, axis=0), col_index, axis=1) - start_z
    d_c = depth_pad[1:-1, 1:-1]
    d_e = depth_pad[2:, 1:-1]
    d_w = depth_pad[:-2, 1:-1]
    d_n = depth_pad[1:-1, 2:]
    d_s = depth_pad[1:-1, :-2]
    d_xw = depth_pad[0:1, 1:-1]
    d_xe = depth_pad[col_x + 1:, 1:-1]
    d_ys = depth_pad[1:-1, 0:1]
    d_yn = depth_pad[1:-1, col_y + 1:]
    local = jnp.arange(lev_count, dtype=jnp.int32)
    wet_here = (local[:, None, None] < d_c[None]).astype(jnp.float32)
    wet_next = ((local + 1)[:, None, None] < d_c[None]).astype(jnp.float32)
    coupling = mixing * (wet_here * wet_next)[None]
    wet_up = (-1 < d_c).astype(jnp.float32)
    ctop = mix_above * (wet_up * wet_here[0])[None]
    ctop = jnp.where(place_z > 0, ctop, 0.0)
    ratio, inv, u, v, uv_ends = coupling_solve(coupling, ctop)
    uv_all = lax.all_gather(uv_ends, "gz")
    lev3 = local[:, None, None]
    tot_c = jnp.sum(density_of(state, (lev3 < d_c[None]).astype(jnp.float32)), axis=0)
    lev2 = local[:, None]
    tot_xw = jnp.sum(density_of(halo_xw, (lev2 < d_xw[0][None]).astype(jnp.float32)), axis=0)
    tot_xe = jnp.sum(density_of(halo_xe, (lev2 < d_xe[0][None]).astype(jnp.float32)), axis=0)
    tot_ys = jnp.sum(density_of(halo_ys, (lev2 < d_ys[:, 0][None]).astype(jnp.float32)), axis=0)
    tot_yn = jnp.sum(density_of(halo_yn, (lev2 < d_yn[:, 0][None]).astype(jnp.float32)), axis=0)
    side = jnp.zeros((2, col_y), jnp.float32)
    side = side.at[0, :col_x].set(tot_ys).at[1, :col_x].set(tot_yn)
    pack = jnp.concatenate([tot_c, tot_xw[None], tot_xe[None], side], axis=0)
    shallower = jnp.zeros_like(pack)
    for hop in range(1, peers_z):
        pairs_z = [(i, i + hop) for i in range(peers_z - hop)]
        shallower = shallower + lax.ppermute(pack, "gz", pairs_z)
    s_c = shallower[:col_x]
    s_xw = shallower[col_x:col_x + 1]
    s_xe = shallower[col_x + 1:col_x + 2]
    s_ys = shallower[col_x + 2, :col_x][:, None]
    s_yn = shallower[col_x + 3, :col_x][:, None]
    face_row = start_y + jnp.arange(col_y, dtype=jnp.int32)
    wall_n = (face_row <= total_y - 2).astype(jnp.float32)
    wall_s = (face_row - 1 >= 0).astype(jnp.float32)
    coriolis = 0.5 + (face_row.astype(jnp.float32) + 0.5) / total_y
    lanes = jnp.stack([wall_n, wall_s, 0.3 * coriolis] + [jnp.zeros_like(wall_n)] * 5)
    wind_top = jnp.where(place_z == 0, wind, 0.0)
    y, y_ends = fused_solve(state, halo_xw, halo_xe, halo_ys[..., None], halo_yn[..., None],
                            d_c, d_e, d_w, d_n, d_s, d_xw, d_xe, d_ys, d_yn,
                            s_c, s_xw, s_xe, s_ys, s_yn, lanes, wind_top,
                            coupling, inv, ratio)
    y_all = gather_by_permutes(y_ends, "gz", place_z, peers_z)
    x_above, x_below = interface_values(y_all, uv_all, place_z, peers_z)
    pairs = u.shape[0]
    shape5 = (pairs, fields // pairs) + y.shape[1:]
    plane5 = (pairs, fields // pairs, 1, col_x, col_y)
    x = (y.reshape(shape5) + x_above.reshape(plane5) * u[:, None]
         + x_below.reshape(plane5) * v[:, None])
    return x.reshape(y.shape)


def solution(mesh):
    return jax.shard_map(
        per_device,
        mesh=mesh,
        in_specs=(P(None, "gz", "gx", "gy"), P(None, "gz", "gx", "gy"), P(), P(None, "gx", "gy")),
        out_specs=P(None, "gz", "gx", "gy"),
        check_vma=False,
    )
```

```python
import jax
import jax.numpy as jnp
from jax import lax
from jax.experimental import pallas as pl
from jax.experimental.pallas import tpu as pltpu
from jax.sharding import PartitionSpec as P


def padded_2(array, sides, width):
    for axis, dim in sides:
        peers, length = (lax.axis_size(axis), array.shape[dim])
        up = [(i, (i + 1) % peers) for i in range(peers)]
        down = [(j, i) for i, j in up]
        last = lax.slice_in_dim(array, length - width, length, axis=dim)
        initial = lax.slice_in_dim(array, 0, width, axis=dim)
        before = lax.ppermute(last, axis, up)
        after = lax.ppermute(initial, axis, down)
        array = jnp.concatenate([before, array, after], axis=dim)
    return array


def density_of(fields, wet_mask):
    return (-0.3 * fields[0] + 0.7 * fields[1] - 0.05 * fields[0] * fields[0]) * wet_mask


def advance(padded, wet_pad, pressure, wall_face, coriolis):
    wet_x = wet_pad[:, :-1, 1:-1] * wet_pad[:, 1:, 1:-1]
    wet_y = wet_pad[:, 1:-1, :-1] * wet_pad[:, 1:-1, 1:] * wall_face
    east_vel = 0.5 * (padded[2, :, :-1, 1:-1] + padded[2, :, 1:, 1:-1]) * wet_x
    north_vel = 0.5 * (padded[3, :, 1:-1, :-1] + padded[3, :, 1:-1, 1:]) * wet_y
    west_side = padded[:, :, :-1, 1:-1]
    east_side = padded[:, :, 1:, 1:-1]
    flux_x = 0.25 * (
        jnp.maximum(east_vel, 0.0) * west_side + jnp.minimum(east_vel, 0.0) * east_side
    ) - 0.08 * wet_x * (east_side - west_side)
    south_side = padded[:, :, 1:-1, :-1]
    north_side = padded[:, :, 1:-1, 1:]
    flux_y = 0.25 * (
        jnp.maximum(north_vel, 0.0) * south_side + jnp.minimum(north_vel, 0.0) * north_side
    ) - 0.08 * wet_y * (north_side - south_side)
    interior = padded[:, :, 1:-1, 1:-1]
    moved = interior - (
        flux_x[:, :, 1:] - flux_x[:, :, :-1] + flux_y[:, :, :, 1:] - flux_y[:, :, :, :-1]
    )
    centre = pressure[:, 1:-1, 1:-1]
    grad_x = 0.5 * (
        wet_x[:, 1:] * (pressure[:, 2:, 1:-1] - centre)
        + wet_x[:, :-1] * (centre - pressure[:, :-2, 1:-1])
    )
    grad_y = 0.5 * (
        wet_y[:, :, 1:] * (pressure[:, 1:-1, 2:] - centre)
        + wet_y[:, :, :-1] * (centre - pressure[:, 1:-1, :-2])
    )
    east_new = moved[2] + 0.3 * coriolis * interior[3] - grad_x
    north_new = moved[3] - 0.3 * coriolis * interior[2] - grad_y
    wet_inner = wet_pad[:, 1:-1, 1:-1]
    return jnp.stack([moved[0], moved[1], east_new, north_new]) * wet_inner


def coupling_kernel(c_ref, ctop_ref, ratio_ref, inv_ref, u_ref, v_ref, ends_ref):
    levels = c_ref.shape[1]
    ctop = ctop_ref[...]
    ratio_prev = None
    vu_prev = None
    for k in range(levels):
        above = ctop if k == 0 else c_ref[:, k - 1]
        below = c_ref[:, k]
        if k == 0:
            divisor = 1.0 + above + below
        else:
            divisor = 1.0 + above * (1.0 - ratio_prev) + below
        inv = 1.0 / divisor
        ratio = below * inv
        vu = ctop * inv if k == 0 else above * vu_prev * inv
        ratio_ref[:, k] = ratio
        inv_ref[:, k] = inv
        u_ref[:, k] = vu
        ratio_prev, vu_prev = ratio, vu
    u_later = vu_prev
    v_later = ratio_prev
    pairs = c_ref.shape[0]
    ends_ref[pairs:2 * pairs] = u_later
    ends_ref[3 * pairs:4 * pairs] = v_later
    v_ref[:, levels - 1] = v_later
    for k in range(levels - 2, -1, -1):
        ratio = ratio_ref[:, k]
        u_later = u_ref[:, k] + ratio * u_later
        v_later = ratio * v_later
        u_ref[:, k] = u_later
        v_ref[:, k] = v_later
    ends_ref[0:pairs] = u_later
    ends_ref[2 * pairs:3 * pairs] = v_later


def field_kernel(f_ref, c_ref, ctop_ref, ratio_ref, inv_ref, y_ref, ends_ref):
    levels = f_ref.shape[1]
    fields = f_ref.shape[0]
    vy = None
    for k in range(levels):
        inv = jnp.repeat(inv_ref[:, k], 2, axis=0)
        rhs = f_ref[:, k]
        if k == 0:
            vy = rhs * inv
        else:
            above = jnp.repeat(c_ref[:, k - 1], 2, axis=0)
            vy = (rhs + above * vy) * inv
        y_ref[:, k] = vy
    y_later = vy
    ends_ref[fields:2 * fields] = y_later
    for k in range(levels - 2, -1, -1):
        ratio = jnp.repeat(ratio_ref[:, k], 2, axis=0)
        y_later = y_ref[:, k] + ratio * y_later
        y_ref[:, k] = y_later
    ends_ref[0:fields] = y_later


def _specs(lead, levels, bx, cols_y):
    return pl.BlockSpec((lead, levels, bx, cols_y), lambda i: (0, 0, i, 0))


def _plane_spec(lead, bx, cols_y):
    return pl.BlockSpec((lead, bx, cols_y), lambda i: (0, i, 0))


def coupling_solve(coupling, ctop):
    pairs, levels, cols_x, cols_y = coupling.shape
    bx = 8 if cols_x % 8 == 0 else cols_x
    cspec = _specs(pairs, levels, bx, cols_y)
    full = jax.ShapeDtypeStruct(coupling.shape, jnp.float32)
    return pl.pallas_call(
        coupling_kernel,
        grid=(cols_x // bx,),
        in_specs=[cspec, _plane_spec(pairs, bx, cols_y)],
        out_specs=[cspec, cspec, cspec, cspec, _plane_spec(4 * pairs, bx, cols_y)],
        out_shape=[full, full, full, full,
                   jax.ShapeDtypeStruct((4 * pairs, cols_x, cols_y), jnp.float32)],
    )(coupling, ctop)


def field_solve(forced, coupling, ctop, ratio, inv):
    fields, levels, cols_x, cols_y = forced.shape
    pairs = coupling.shape[0]
    bx = 8 if cols_x % 8 == 0 else cols_x
    fspec = _specs(fields, levels, bx, cols_y)
    cspec = _specs(pairs, levels, bx, cols_y)
    return pl.pallas_call(
        field_kernel,
        grid=(cols_x // bx,),
        in_specs=[fspec, cspec, _plane_spec(pairs, bx, cols_y), cspec, cspec],
        out_specs=[fspec, _plane_spec(2 * fields, bx, cols_y)],
        out_shape=[jax.ShapeDtypeStruct(forced.shape, jnp.float32),
                   jax.ShapeDtypeStruct((2 * fields, cols_x, cols_y), jnp.float32)],
    )(forced, coupling, ctop, ratio, inv)


def interface_values(y_ends, uv_ends, place, peers):
    fields = 4
    pairs = uv_ends.shape[1] // 4
    grouped = (peers, pairs, fields // pairs) + y_ends.shape[2:]
    y0 = y_ends[:, 0:fields].reshape(grouped)
    y1 = y_ends[:, fields:2 * fields].reshape(grouped)
    u0 = uv_ends[:, 0:pairs][:, :, None]
    u1 = uv_ends[:, pairs:2 * pairs][:, :, None]
    v0 = uv_ends[:, 2 * pairs:3 * pairs][:, :, None]
    v1 = uv_ends[:, 3 * pairs:4 * pairs][:, :, None]
    pt, qt, pb, qb = [], [], [], []
    for q in range(peers):
        if q == 0:
            pt_q, qt_q = y0[q], v0[q]
            pb_q, qb_q = y1[q], v1[q]
        else:
            inv = 1.0 / (1.0 - u0[q] * qb[-1])
            pt_q = (y0[q] + u0[q] * pb[-1]) * inv
            qt_q = v0[q] * inv
            pb_q = y1[q] + u1[q] * (pb[-1] + qb[-1] * pt_q)
            qb_q = v1[q] + u1[q] * qb[-1] * qt_q
        pt.append(pt_q)
        qt.append(qt_q)
        pb.append(pb_q)
        qb.append(qb_q)
    tops = [None] * peers
    bots = [None] * peers
    t_next = jnp.zeros_like(pt[0])
    for q in range(peers - 1, -1, -1):
        tops[q] = pt[q] + qt[q] * t_next
        bots[q] = pb[q] + qb[q] * t_next
        t_next = tops[q]
    above = jnp.zeros_like(pt[0])
    below = jnp.zeros_like(pt[0])
    for q in range(peers):
        if q >= 1:
            above = jnp.where(place == q, bots[q - 1], above)
        if q <= peers - 2:
            below = jnp.where(place == q, tops[q + 1], below)
    return above, below


def gather_by_permutes(part, axis, place, peers):
    received = [part]
    for hop in range(1, peers):
        shift = [(i, (i + hop) % peers) for i in range(peers)]
        received.append(lax.ppermute(part, axis, shift))
    rows = []
    for q in range(peers):
        row = received[0]
        for hop in range(1, peers):
            row = jnp.where((place - hop) % peers == q, received[hop], row)
        rows.append(row)
    return jnp.stack(rows)


def _density(t, s, w):
    return (-0.3 * t + 0.7 * s - 0.05 * t * t) * w


def _flux(vel, lo, hi, w):
    return 0.25 * (jnp.maximum(vel, 0.0) * lo + jnp.minimum(vel, 0.0) * hi) - 0.08 * w * (hi - lo)


def fused_kernel(st_ref, xw_ref, xe_ref, ys_ref, yn_ref,
                 dc_ref, de_ref, dw_ref, dn_ref, ds_ref,
                 dxw_ref, dxe_ref, dys_ref, dyn_ref,
                 sc_ref, sxw_ref, sxe_ref, sys_ref, syn_ref,
                 lane_ref, wind_ref, c_ref, inv_ref, ratio_ref,
                 y_ref, ends_ref):
    fields, levels, nx, ny = st_ref.shape
    row = lax.broadcasted_iota(jnp.int32, (nx, ny), 0)
    lane = lax.broadcasted_iota(jnp.int32, (nx, ny), 1)
    wall_n = lane_ref[0:1]
    wall_s = lane_ref[1:2]
    cor03 = lane_ref[2:3]
    d_c, d_e, d_w, d_n, d_s = dc_ref[...], de_ref[...], dw_ref[...], dn_ref[...], ds_ref[...]
    d_xw, d_xe, d_ys, d_yn = dxw_ref[...], dxe_ref[...], dys_ref[...], dyn_ref[...]

    tx = xw_ref.shape[2]
    ty = ys_ref.shape[3]

    def rows(a):
        return a if tx == nx else jnp.concatenate([a] * (nx // tx), axis=0)

    def lanes(a):
        return a if ty == ny else jnp.concatenate([a] * (ny // ty), axis=1)

    def east(r, h):
        return jnp.where(row == nx - 1, rows(pltpu.roll(h, tx - 1, 0)), pltpu.roll(r, nx - 1, 0))

    def west(r, h):
        return jnp.where(row == 0, rows(pltpu.roll(h, 1, 0)), pltpu.roll(r, 1, 0))

    def north(r, h):
        return jnp.where(lane == ny - 1, lanes(pltpu.roll(h, ty - 1, 1)), pltpu.roll(r, ny - 1, 1))

    def south(r, h):
        return jnp.where(lane == 0, lanes(pltpu.roll(h, 1, 1)), pltpu.roll(r, 1, 1))

    def level(k, run, vy_prev):
        wc = (k < d_c).astype(jnp.float32)
        we = (k < d_e).astype(jnp.float32)
        ww = (k < d_w).astype(jnp.float32)
        wn = (k < d_n).astype(jnp.float32)
        ws = (k < d_s).astype(jnp.float32)
        wxw = (k < d_xw).astype(jnp.float32)
        wxe = (k < d_xe).astype(jnp.float32)
        wys = (k < d_ys).astype(jnp.float32)
        wyn = (k < d_yn).astype(jnp.float32)
        cen = [st_ref[f, k] for f in range(fields)]
        hxw = [xw_ref[f, k] for f in range(fields)]
        hxe = [xe_ref[f, k] for f in range(fields)]
        hys = [ys_ref[f, k] for f in range(fields)]
        hyn = [yn_ref[f, k] for f in range(fields)]
        run_c, run_xw, run_xe, run_ys, run_yn = run
        den_c = _density(cen[0], cen[1], wc)
        den_xw = _density(hxw[0], hxw[1], wxw)
        den_xe = _density(hxe[0], hxe[1], wxe)
        den_ys = _density(hys[0], hys[1], wys)
        den_yn = _density(hyn[0], hyn[1], wyn)
        run_c = run_c + den_c
        run_xw = run_xw + den_xw
        run_xe = run_xe + den_xe
        run_ys = run_ys + den_ys
        run_yn = run_yn + den_yn
        p_c = 0.03 * (sc_ref[...] + run_c - 0.5 * den_c)
        p_xw = 0.03 * (sxw_ref[...] + run_xw - 0.5 * den_xw)
        p_xe = 0.03 * (sxe_ref[...] + run_xe - 0.5 * den_xe)
        p_ys = 0.03 * (sys_ref[...] + run_ys - 0.5 * den_ys)
        p_yn = 0.03 * (syn_ref[...] + run_yn - 0.5 * den_yn)
        p_e = east(p_c, p_xe)
        p_w = west(p_c, p_xw)
        p_n = north(p_c, p_yn)
        p_s = south(p_c, p_ys)
        face_e = wc * we
        face_w = ww * wc
        face_n = wc * wn * wall_n
        face_s = ws * wc * wall_s
        nbr_e = [east(cen[f], hxe[f]) for f in range(fields)]
        nbr_w = [west(cen[f], hxw[f]) for f in range(fields)]
        nbr_n = [north(cen[f], hyn[f]) for f in range(fields)]
        nbr_s = [south(cen[f], hys[f]) for f in range(fields)]
        vel_e = 0.5 * (cen[2] + nbr_e[2]) * face_e
        vel_w = 0.5 * (nbr_w[2] + cen[2]) * face_w
        vel_n = 0.5 * (cen[3] + nbr_n[3]) * face_n
        vel_s = 0.5 * (nbr_s[3] + cen[3]) * face_s
        moved = []
        for f in range(fields):
            fe = _flux(vel_e, cen[f], nbr_e[f], face_e)
            fw = _flux(vel_w, nbr_w[f], cen[f], face_w)
            fn = _flux(vel_n, cen[f], nbr_n[f], face_n)
            fs = _flux(vel_s, nbr_s[f], cen[f], face_s)
            moved.append(cen[f] - (fe - fw + fn - fs))
        grad_x = 0.5 * (face_e * (p_e - p_c) + face_w * (p_c - p_w))
        grad_y = 0.5 * (face_n * (p_n - p_c) + face_s * (p_c - p_s))
        east_new = moved[2] + cor03 * cen[3] - grad_x
        north_new = moved[3] - cor03 * cen[2] - grad_y
        forced = [moved[0] * wc, moved[1] * wc, east_new * wc, north_new * wc]
        if isinstance(k, int) and k == 0:
            forced[2] = forced[2] + wind_ref[0] * wc
            forced[3] = forced[3] + wind_ref[1] * wc
        vy = []
        for f in range(fields):
            m = f // 2
            inv = inv_ref[m, k]
            if vy_prev is None:
                val = forced[f] * inv
            else:
                val = (forced[f] + c_ref[m, k - 1] * vy_prev[f]) * inv
            y_ref[f, k] = val
            vy.append(val)
        return (run_c, run_xw, run_xe, run_ys, run_yn), vy

    run0 = (jnp.zeros((nx, ny), jnp.float32), jnp.zeros((tx, ny), jnp.float32),
            jnp.zeros((tx, ny), jnp.float32), jnp.zeros((nx, ty), jnp.float32),
            jnp.zeros((nx, ty), jnp.float32))
    run, vy = level(0, run0, None)

    def step(k, carry):
        run, vy = carry
        run, vy = level(k, run, vy)
        return run, vy

    run, vy = lax.fori_loop(1, levels, step, (run, vy), unroll=2)
    for f in range(fields):
        ends_ref[fields + f] = vy[f]

    def back(j, later):
        k = levels - 2 - j
        out = []
        for f in range(fields):
            val = y_ref[f, k] + ratio_ref[f // 2, k] * later[f]
            y_ref[f, k] = val
            out.append(val)
        return out

    later = lax.fori_loop(0, levels - 1, back, vy, unroll=2)
    for f in range(fields):
        ends_ref[f] = later[f]


def fused_solve(*operands):
    st = operands[0]
    fields, levels, nx, ny = st.shape
    vmem = pl.BlockSpec(memory_space=pltpu.VMEM)
    return pl.pallas_call(
        fused_kernel,
        in_specs=[vmem] * len(operands),
        out_specs=[vmem, vmem],
        out_shape=[jax.ShapeDtypeStruct(st.shape, jnp.float32),
                   jax.ShapeDtypeStruct((2 * fields, nx, ny), jnp.float32)],
        compiler_params=pltpu.CompilerParams(vmem_limit_bytes=60 * 1024 * 1024),
    )(*operands)


def per_device(state, mixing, depth_levels, wind):
    fields, lev_count, col_x, col_y = state.shape
    total_x, total_y = depth_levels.shape
    peers_z = lax.axis_size("gz")
    place_z = lax.axis_index("gz")
    peers_x = lax.axis_size("gx")
    peers_y = lax.axis_size("gy")
    start_x = lax.axis_index("gx") * col_x
    start_y = lax.axis_index("gy") * col_y
    start_z = place_z * lev_count
    down_z = [(i, i + 1) for i in range(peers_z - 1)]
    mix_above = lax.ppermute(mixing[:, lev_count - 1], "gz", down_z)
    up_x = [(i, (i + 1) % peers_x) for i in range(peers_x)]
    dn_x = [(j, i) for i, j in up_x]
    up_y = [(i, (i + 1) % peers_y) for i in range(peers_y)]
    dn_y = [(j, i) for i, j in up_y]
    tx = min(8, col_x)
    ty = min(128, col_y)
    halo_xw = lax.ppermute(state[:, :, col_x - tx:], "gx", up_x)
    halo_xe = lax.ppermute(state[:, :, :tx], "gx", dn_x)
    halo_ys = lax.ppermute(state[:, :, :, col_y - ty:], "gy", up_y)
    halo_yn = lax.ppermute(state[:, :, :, :ty], "gy", dn_y)
    levels = start_z + jnp.arange(lev_count, dtype=jnp.int32)
    row_index = (start_x - 1 + jnp.arange(col_x + 2, dtype=jnp.int32)) % total_x
    col_index = (start_y - 1 + jnp.arange(col_y + 2, dtype=jnp.int32)) % total_y
    depth_pad = jnp.take(jnp.take(depth_levels, row_index, axis=0), col_index, axis=1) - start_z
    d_c = depth_pad[1:-1, 1:-1]
    d_e = depth_pad[2:, 1:-1]
    d_w = depth_pad[:-2, 1:-1]
    d_n = depth_pad[1:-1, 2:]
    d_s = depth_pad[1:-1, :-2]
    d_xw = depth_pad[0:1, 1:-1]
    d_xe = depth_pad[col_x + 1:, 1:-1]
    d_ys = depth_pad[1:-1, 0:1]
    d_yn = depth_pad[1:-1, col_y + 1:]
    local = jnp.arange(lev_count, dtype=jnp.int32)
    wet_here = (local[:, None, None] < d_c[None]).astype(jnp.float32)
    wet_next = ((local + 1)[:, None, None] < d_c[None]).astype(jnp.float32)
    coupling = mixing * (wet_here * wet_next)[None]
    wet_up = (-1 < d_c).astype(jnp.float32)
    ctop = mix_above * (wet_up * wet_here[0])[None]
    ctop = jnp.where(place_z > 0, ctop, 0.0)
    ratio, inv, u, v, uv_ends = coupling_solve(coupling, ctop)
    uv_all = lax.all_gather(uv_ends, "gz")
    lev3 = local[:, None, None]
    tot_c = jnp.sum(density_of(state, (lev3 < d_c[None]).astype(jnp.float32)), axis=0)
    lev2 = local[:, None]
    tot_xw = jnp.sum(density_of(halo_xw[:, :, tx - 1], (lev2 < d_xw[0][None]).astype(jnp.float32)), axis=0)
    tot_xe = jnp.sum(density_of(halo_xe[:, :, 0], (lev2 < d_xe[0][None]).astype(jnp.float32)), axis=0)
    tot_ys = jnp.sum(density_of(halo_ys[..., ty - 1], (lev2 < d_ys[:, 0][None]).astype(jnp.float32)), axis=0)
    tot_yn = jnp.sum(density_of(halo_yn[..., 0], (lev2 < d_yn[:, 0][None]).astype(jnp.float32)), axis=0)
    side = jnp.zeros((2, col_y), jnp.float32)
    side = side.at[0, :col_x].set(tot_ys).at[1, :col_x].set(tot_yn)
    pack = jnp.concatenate([tot_c, tot_xw[None], tot_xe[None], side], axis=0)
    shallower = jnp.zeros_like(pack)
    for hop in range(1, peers_z):
        pairs_z = [(i, i + hop) for i in range(peers_z - hop)]
        shallower = shallower + lax.ppermute(pack, "gz", pairs_z)
    s_c = shallower[:col_x]
    s_xw = shallower[col_x:col_x + 1]
    s_xe = shallower[col_x + 1:col_x + 2]
    s_ys = shallower[col_x + 2, :col_x][:, None]
    s_yn = shallower[col_x + 3, :col_x][:, None]
    face_row = start_y + jnp.arange(col_y, dtype=jnp.int32)
    wall_n = (face_row <= total_y - 2).astype(jnp.float32)
    wall_s = (face_row - 1 >= 0).astype(jnp.float32)
    coriolis = 0.5 + (face_row.astype(jnp.float32) + 0.5) / total_y
    lanes = jnp.stack([wall_n, wall_s, 0.3 * coriolis] + [jnp.zeros_like(wall_n)] * 5)
    wind_top = jnp.where(place_z == 0, wind, 0.0)
    tile_x = (tx, col_y)
    tile_y = (col_x, ty)
    y, y_ends = fused_solve(state, halo_xw, halo_xe, halo_ys, halo_yn,
                            d_c, d_e, d_w, d_n, d_s,
                            jnp.broadcast_to(d_xw, tile_x), jnp.broadcast_to(d_xe, tile_x),
                            jnp.broadcast_to(d_ys, tile_y), jnp.broadcast_to(d_yn, tile_y),
                            s_c, jnp.broadcast_to(s_xw, tile_x), jnp.broadcast_to(s_xe, tile_x),
                            jnp.broadcast_to(s_ys, tile_y), jnp.broadcast_to(s_yn, tile_y),
                            lanes, wind_top,
                            coupling, inv, ratio)
    y_all = gather_by_permutes(y_ends, "gz", place_z, peers_z)
    x_above, x_below = interface_values(y_all, uv_all, place_z, peers_z)
    pairs = u.shape[0]
    shape5 = (pairs, fields // pairs) + y.shape[1:]
    plane5 = (pairs, fields // pairs, 1, col_x, col_y)
    x_above = x_above.reshape(plane5)
    x_below = x_below.reshape(plane5)
    x = (y.reshape(shape5) + x_above.reshape(plane5) * u[:, None]
         + x_below.reshape(plane5) * v[:, None])
    return x.reshape(y.shape)


def solution(mesh):
    return jax.shard_map(
        per_device,
        mesh=mesh,
        in_specs=(P(None, "gz", "gx", "gy"), P(None, "gz", "gx", "gy"), P(), P(None, "gx", "gy")),
        out_specs=P(None, "gz", "gx", "gy"),
        check_vma=False,
    )
```

```python
import jax
import jax.numpy as jnp
from jax import lax
from jax.experimental import pallas as pl
from jax.experimental.pallas import tpu as pltpu
from jax.sharding import PartitionSpec as P


def padded_2(array, sides, width):
    for axis, dim in sides:
        peers, length = (lax.axis_size(axis), array.shape[dim])
        up = [(i, (i + 1) % peers) for i in range(peers)]
        down = [(j, i) for i, j in up]
        last = lax.slice_in_dim(array, length - width, length, axis=dim)
        initial = lax.slice_in_dim(array, 0, width, axis=dim)
        before = lax.ppermute(last, axis, up)
        after = lax.ppermute(initial, axis, down)
        array = jnp.concatenate([before, array, after], axis=dim)
    return array


def density_of(fields, wet_mask):
    return (-0.3 * fields[0] + 0.7 * fields[1] - 0.05 * fields[0] * fields[0]) * wet_mask


def advance(padded, wet_pad, pressure, wall_face, coriolis):
    wet_x = wet_pad[:, :-1, 1:-1] * wet_pad[:, 1:, 1:-1]
    wet_y = wet_pad[:, 1:-1, :-1] * wet_pad[:, 1:-1, 1:] * wall_face
    east_vel = 0.5 * (padded[2, :, :-1, 1:-1] + padded[2, :, 1:, 1:-1]) * wet_x
    north_vel = 0.5 * (padded[3, :, 1:-1, :-1] + padded[3, :, 1:-1, 1:]) * wet_y
    west_side = padded[:, :, :-1, 1:-1]
    east_side = padded[:, :, 1:, 1:-1]
    flux_x = 0.25 * (
        jnp.maximum(east_vel, 0.0) * west_side + jnp.minimum(east_vel, 0.0) * east_side
    ) - 0.08 * wet_x * (east_side - west_side)
    south_side = padded[:, :, 1:-1, :-1]
    north_side = padded[:, :, 1:-1, 1:]
    flux_y = 0.25 * (
        jnp.maximum(north_vel, 0.0) * south_side + jnp.minimum(north_vel, 0.0) * north_side
    ) - 0.08 * wet_y * (north_side - south_side)
    interior = padded[:, :, 1:-1, 1:-1]
    moved = interior - (
        flux_x[:, :, 1:] - flux_x[:, :, :-1] + flux_y[:, :, :, 1:] - flux_y[:, :, :, :-1]
    )
    centre = pressure[:, 1:-1, 1:-1]
    grad_x = 0.5 * (
        wet_x[:, 1:] * (pressure[:, 2:, 1:-1] - centre)
        + wet_x[:, :-1] * (centre - pressure[:, :-2, 1:-1])
    )
    grad_y = 0.5 * (
        wet_y[:, :, 1:] * (pressure[:, 1:-1, 2:] - centre)
        + wet_y[:, :, :-1] * (centre - pressure[:, 1:-1, :-2])
    )
    east_new = moved[2] + 0.3 * coriolis * interior[3] - grad_x
    north_new = moved[3] - 0.3 * coriolis * interior[2] - grad_y
    wet_inner = wet_pad[:, 1:-1, 1:-1]
    return jnp.stack([moved[0], moved[1], east_new, north_new]) * wet_inner


def coupling_kernel(c_ref, ctop_ref, ratio_ref, inv_ref, u_ref, v_ref, ends_ref):
    levels = c_ref.shape[1]
    ctop = ctop_ref[...]
    ratio_prev = None
    vu_prev = None
    for k in range(levels):
        above = ctop if k == 0 else c_ref[:, k - 1]
        below = c_ref[:, k]
        if k == 0:
            divisor = 1.0 + above + below
        else:
            divisor = 1.0 + above * (1.0 - ratio_prev) + below
        inv = 1.0 / divisor
        ratio = below * inv
        vu = ctop * inv if k == 0 else above * vu_prev * inv
        ratio_ref[:, k] = ratio
        inv_ref[:, k] = inv
        u_ref[:, k] = vu
        ratio_prev, vu_prev = ratio, vu
    u_later = vu_prev
    v_later = ratio_prev
    pairs = c_ref.shape[0]
    ends_ref[pairs:2 * pairs] = u_later
    ends_ref[3 * pairs:4 * pairs] = v_later
    v_ref[:, levels - 1] = v_later
    for k in range(levels - 2, -1, -1):
        ratio = ratio_ref[:, k]
        u_later = u_ref[:, k] + ratio * u_later
        v_later = ratio * v_later
        u_ref[:, k] = u_later
        v_ref[:, k] = v_later
    ends_ref[0:pairs] = u_later
    ends_ref[2 * pairs:3 * pairs] = v_later


def field_kernel(f_ref, c_ref, ctop_ref, ratio_ref, inv_ref, y_ref, ends_ref):
    levels = f_ref.shape[1]
    fields = f_ref.shape[0]
    vy = None
    for k in range(levels):
        inv = jnp.repeat(inv_ref[:, k], 2, axis=0)
        rhs = f_ref[:, k]
        if k == 0:
            vy = rhs * inv
        else:
            above = jnp.repeat(c_ref[:, k - 1], 2, axis=0)
            vy = (rhs + above * vy) * inv
        y_ref[:, k] = vy
    y_later = vy
    ends_ref[fields:2 * fields] = y_later
    for k in range(levels - 2, -1, -1):
        ratio = jnp.repeat(ratio_ref[:, k], 2, axis=0)
        y_later = y_ref[:, k] + ratio * y_later
        y_ref[:, k] = y_later
    ends_ref[0:fields] = y_later


def _specs(lead, levels, bx, cols_y):
    return pl.BlockSpec((lead, levels, bx, cols_y), lambda i: (0, 0, i, 0))


def _plane_spec(lead, bx, cols_y):
    return pl.BlockSpec((lead, bx, cols_y), lambda i: (0, i, 0))


def coupling_solve(coupling, ctop):
    pairs, levels, cols_x, cols_y = coupling.shape
    bx = 8 if cols_x % 8 == 0 else cols_x
    cspec = _specs(pairs, levels, bx, cols_y)
    full = jax.ShapeDtypeStruct(coupling.shape, jnp.float32)
    return pl.pallas_call(
        coupling_kernel,
        grid=(cols_x // bx,),
        in_specs=[cspec, _plane_spec(pairs, bx, cols_y)],
        out_specs=[cspec, cspec, cspec, cspec, _plane_spec(4 * pairs, bx, cols_y)],
        out_shape=[full, full, full, full,
                   jax.ShapeDtypeStruct((4 * pairs, cols_x, cols_y), jnp.float32)],
    )(coupling, ctop)


def field_solve(forced, coupling, ctop, ratio, inv):
    fields, levels, cols_x, cols_y = forced.shape
    pairs = coupling.shape[0]
    bx = 8 if cols_x % 8 == 0 else cols_x
    fspec = _specs(fields, levels, bx, cols_y)
    cspec = _specs(pairs, levels, bx, cols_y)
    return pl.pallas_call(
        field_kernel,
        grid=(cols_x // bx,),
        in_specs=[fspec, cspec, _plane_spec(pairs, bx, cols_y), cspec, cspec],
        out_specs=[fspec, _plane_spec(2 * fields, bx, cols_y)],
        out_shape=[jax.ShapeDtypeStruct(forced.shape, jnp.float32),
                   jax.ShapeDtypeStruct((2 * fields, cols_x, cols_y), jnp.float32)],
    )(forced, coupling, ctop, ratio, inv)


def interface_values(y_ends, uv_ends, place, peers):
    fields = 4
    pairs = uv_ends.shape[1] // 4
    grouped = (peers, pairs, fields // pairs) + y_ends.shape[2:]
    y0 = y_ends[:, 0:fields].reshape(grouped)
    y1 = y_ends[:, fields:2 * fields].reshape(grouped)
    u0 = uv_ends[:, 0:pairs][:, :, None]
    u1 = uv_ends[:, pairs:2 * pairs][:, :, None]
    v0 = uv_ends[:, 2 * pairs:3 * pairs][:, :, None]
    v1 = uv_ends[:, 3 * pairs:4 * pairs][:, :, None]
    pt, qt, pb, qb = [], [], [], []
    for q in range(peers):
        if q == 0:
            pt_q, qt_q = y0[q], v0[q]
            pb_q, qb_q = y1[q], v1[q]
        else:
            inv = 1.0 / (1.0 - u0[q] * qb[-1])
            pt_q = (y0[q] + u0[q] * pb[-1]) * inv
            qt_q = v0[q] * inv
            pb_q = y1[q] + u1[q] * (pb[-1] + qb[-1] * pt_q)
            qb_q = v1[q] + u1[q] * qb[-1] * qt_q
        pt.append(pt_q)
        qt.append(qt_q)
        pb.append(pb_q)
        qb.append(qb_q)
    tops = [None] * peers
    bots = [None] * peers
    t_next = jnp.zeros_like(pt[0])
    for q in range(peers - 1, -1, -1):
        tops[q] = pt[q] + qt[q] * t_next
        bots[q] = pb[q] + qb[q] * t_next
        t_next = tops[q]
    above = jnp.zeros_like(pt[0])
    below = jnp.zeros_like(pt[0])
    for q in range(peers):
        if q >= 1:
            above = jnp.where(place == q, bots[q - 1], above)
        if q <= peers - 2:
            below = jnp.where(place == q, tops[q + 1], below)
    return above, below


def gather_by_permutes(part, axis, place, peers):
    received = [part]
    for hop in range(1, peers):
        shift = [(i, (i + hop) % peers) for i in range(peers)]
        received.append(lax.ppermute(part, axis, shift))
    rows = []
    for q in range(peers):
        row = received[0]
        for hop in range(1, peers):
            row = jnp.where((place - hop) % peers == q, received[hop], row)
        rows.append(row)
    return jnp.stack(rows)


def _density(t, s, w):
    return (-0.3 * t + 0.7 * s - 0.05 * t * t) * w


def _flux(vel, lo, hi, w):
    return 0.25 * (jnp.maximum(vel, 0.0) * lo + jnp.minimum(vel, 0.0) * hi) - 0.08 * w * (hi - lo)


def fused_kernel(st_ref, xw_ref, xe_ref, ys_ref, yn_ref,
                 dc_ref, de_ref, dw_ref, dn_ref, ds_ref,
                 dxw_ref, dxe_ref, dys_ref, dyn_ref,
                 sc_ref, sxw_ref, sxe_ref, sys_ref, syn_ref,
                 lane_ref, wind_ref, c_ref, inv_ref, ratio_ref,
                 y_ref, ends_ref):
    fields, levels, nx, ny = st_ref.shape
    row = lax.broadcasted_iota(jnp.int32, (nx, ny), 0)
    lane = lax.broadcasted_iota(jnp.int32, (nx, ny), 1)
    wall_n = lane_ref[0:1]
    wall_s = lane_ref[1:2]
    cor03 = lane_ref[2:3]
    d_c, d_e, d_w, d_n, d_s = dc_ref[...], de_ref[...], dw_ref[...], dn_ref[...], ds_ref[...]
    d_xw, d_xe, d_ys, d_yn = dxw_ref[...], dxe_ref[...], dys_ref[...], dyn_ref[...]

    def east(r, h):
        return jnp.where(row == nx - 1, h, pltpu.roll(r, nx - 1, 0))

    def west(r, h):
        return jnp.where(row == 0, h, pltpu.roll(r, 1, 0))

    def north(r, h):
        return jnp.where(lane == ny - 1, h, pltpu.roll(r, ny - 1, 1))

    def south(r, h):
        return jnp.where(lane == 0, h, pltpu.roll(r, 1, 1))

    def level(k, run, vy_prev):
        wc = (k < d_c).astype(jnp.float32)
        we = (k < d_e).astype(jnp.float32)
        ww = (k < d_w).astype(jnp.float32)
        wn = (k < d_n).astype(jnp.float32)
        ws = (k < d_s).astype(jnp.float32)
        wxw = (k < d_xw).astype(jnp.float32)
        wxe = (k < d_xe).astype(jnp.float32)
        wys = (k < d_ys).astype(jnp.float32)
        wyn = (k < d_yn).astype(jnp.float32)
        cen = [st_ref[f, k] for f in range(fields)]
        hxw = [xw_ref[f, pl.ds(k, 1), :] for f in range(fields)]
        hxe = [xe_ref[f, pl.ds(k, 1), :] for f in range(fields)]
        hys = [ys_ref[f, k] for f in range(fields)]
        hyn = [yn_ref[f, k] for f in range(fields)]
        run_c, run_xw, run_xe, run_ys, run_yn = run
        den_c = _density(cen[0], cen[1], wc)
        den_xw = _density(hxw[0], hxw[1], wxw)
        den_xe = _density(hxe[0], hxe[1], wxe)
        den_ys = _density(hys[0], hys[1], wys)
        den_yn = _density(hyn[0], hyn[1], wyn)
        run_c = run_c + den_c
        run_xw = run_xw + den_xw
        run_xe = run_xe + den_xe
        run_ys = run_ys + den_ys
        run_yn = run_yn + den_yn
        p_c = 0.03 * (sc_ref[...] + run_c - 0.5 * den_c)
        p_xw = 0.03 * (sxw_ref[...] + run_xw - 0.5 * den_xw)
        p_xe = 0.03 * (sxe_ref[...] + run_xe - 0.5 * den_xe)
        p_ys = 0.03 * (sys_ref[...] + run_ys - 0.5 * den_ys)
        p_yn = 0.03 * (syn_ref[...] + run_yn - 0.5 * den_yn)
        p_e = east(p_c, p_xe)
        p_w = west(p_c, p_xw)
        p_n = north(p_c, p_yn)
        p_s = south(p_c, p_ys)
        face_e = wc * we
        face_w = ww * wc
        face_n = wc * wn * wall_n
        face_s = ws * wc * wall_s
        nbr_e = [east(cen[f], hxe[f]) for f in range(fields)]
        nbr_w = [west(cen[f], hxw[f]) for f in range(fields)]
        nbr_n = [north(cen[f], hyn[f]) for f in range(fields)]
        nbr_s = [south(cen[f], hys[f]) for f in range(fields)]
        vel_e = 0.5 * (cen[2] + nbr_e[2]) * face_e
        vel_w = 0.5 * (nbr_w[2] + cen[2]) * face_w
        vel_n = 0.5 * (cen[3] + nbr_n[3]) * face_n
        vel_s = 0.5 * (nbr_s[3] + cen[3]) * face_s
        moved = []
        for f in range(fields):
            fe = _flux(vel_e, cen[f], nbr_e[f], face_e)
            fw = _flux(vel_w, nbr_w[f], cen[f], face_w)
            fn = _flux(vel_n, cen[f], nbr_n[f], face_n)
            fs = _flux(vel_s, nbr_s[f], cen[f], face_s)
            moved.append(cen[f] - (fe - fw + fn - fs))
        grad_x = 0.5 * (face_e * (p_e - p_c) + face_w * (p_c - p_w))
        grad_y = 0.5 * (face_n * (p_n - p_c) + face_s * (p_c - p_s))
        east_new = moved[2] + cor03 * cen[3] - grad_x
        north_new = moved[3] - cor03 * cen[2] - grad_y
        forced = [moved[0] * wc, moved[1] * wc, east_new * wc, north_new * wc]
        if isinstance(k, int) and k == 0:
            forced[2] = forced[2] + wind_ref[0] * wc
            forced[3] = forced[3] + wind_ref[1] * wc
        vy = []
        for f in range(fields):
            m = f // 2
            inv = inv_ref[m, k]
            if vy_prev is None:
                val = forced[f] * inv
            else:
                val = (forced[f] + c_ref[m, k - 1] * vy_prev[f]) * inv
            y_ref[f, k] = val
            vy.append(val)
        return (run_c, run_xw, run_xe, run_ys, run_yn), vy

    run0 = (jnp.zeros((nx, ny), jnp.float32), jnp.zeros((1, ny), jnp.float32),
            jnp.zeros((1, ny), jnp.float32), jnp.zeros((nx, 1), jnp.float32),
            jnp.zeros((nx, 1), jnp.float32))
    run, vy = level(0, run0, None)

    def step(k, carry):
        run, vy = carry
        run, vy = level(k, run, vy)
        return run, vy

    run, vy = lax.fori_loop(1, levels, step, (run, vy), unroll=2)
    for f in range(fields):
        ends_ref[fields + f] = vy[f]

    def back(j, later):
        k = levels - 2 - j
        out = []
        for f in range(fields):
            val = y_ref[f, k] + ratio_ref[f // 2, k] * later[f]
            y_ref[f, k] = val
            out.append(val)
        return out

    later = lax.fori_loop(0, levels - 1, back, vy, unroll=2)
    for f in range(fields):
        ends_ref[f] = later[f]


def fused_solve(*operands):
    st = operands[0]
    fields, levels, nx, ny = st.shape
    vmem = pl.BlockSpec(memory_space=pltpu.VMEM)
    return pl.pallas_call(
        fused_kernel,
        in_specs=[vmem] * len(operands),
        out_specs=[vmem, vmem],
        out_shape=[jax.ShapeDtypeStruct(st.shape, jnp.float32),
                   jax.ShapeDtypeStruct((2 * fields, nx, ny), jnp.float32)],
        compiler_params=pltpu.CompilerParams(vmem_limit_bytes=60 * 1024 * 1024),
    )(*operands)


def per_device(state, mixing, depth_levels, wind):
    fields, lev_count, col_x, col_y = state.shape
    total_x, total_y = depth_levels.shape
    peers_z = lax.axis_size("gz")
    place_z = lax.axis_index("gz")
    peers_x = lax.axis_size("gx")
    peers_y = lax.axis_size("gy")
    start_x = lax.axis_index("gx") * col_x
    start_y = lax.axis_index("gy") * col_y
    start_z = place_z * lev_count
    down_z = [(i, i + 1) for i in range(peers_z - 1)]
    mix_above = lax.ppermute(mixing[:, lev_count - 1], "gz", down_z)
    up_x = [(i, (i + 1) % peers_x) for i in range(peers_x)]
    dn_x = [(j, i) for i, j in up_x]
    up_y = [(i, (i + 1) % peers_y) for i in range(peers_y)]
    dn_y = [(j, i) for i, j in up_y]
    halo_xw = lax.ppermute(state[:, :, col_x - 1], "gx", up_x)
    halo_xe = lax.ppermute(state[:, :, 0], "gx", dn_x)
    halo_ys = lax.ppermute(state[:, :, :, col_y - 1], "gy", up_y)
    halo_yn = lax.ppermute(state[:, :, :, 0], "gy", dn_y)
    levels = start_z + jnp.arange(lev_count, dtype=jnp.int32)
    row_index = (start_x - 1 + jnp.arange(col_x + 2, dtype=jnp.int32)) % total_x
    col_index = (start_y - 1 + jnp.arange(col_y + 2, dtype=jnp.int32)) % total_y
    depth_pad = jnp.take(jnp.take(depth_levels, row_index, axis=0), col_index, axis=1) - start_z
    d_c = depth_pad[1:-1, 1:-1]
    d_e = depth_pad[2:, 1:-1]
    d_w = depth_pad[:-2, 1:-1]
    d_n = depth_pad[1:-1, 2:]
    d_s = depth_pad[1:-1, :-2]
    d_xw = depth_pad[0:1, 1:-1]
    d_xe = depth_pad[col_x + 1:, 1:-1]
    d_ys = depth_pad[1:-1, 0:1]
    d_yn = depth_pad[1:-1, col_y + 1:]
    local = jnp.arange(lev_count, dtype=jnp.int32)
    wet_here = (local[:, None, None] < d_c[None]).astype(jnp.float32)
    wet_next = ((local + 1)[:, None, None] < d_c[None]).astype(jnp.float32)
    coupling = mixing * (wet_here * wet_next)[None]
    wet_up = (-1 < d_c).astype(jnp.float32)
    ctop = mix_above * (wet_up * wet_here[0])[None]
    ctop = jnp.where(place_z > 0, ctop, 0.0)
    ratio, inv, u, v, uv_ends = coupling_solve(coupling, ctop)
    uv_all = lax.all_gather(uv_ends, "gz")
    lev3 = local[:, None, None]
    tot_c = jnp.sum(density_of(state, (lev3 < d_c[None]).astype(jnp.float32)), axis=0)
    lev2 = local[:, None]
    tot_xw = jnp.sum(density_of(halo_xw, (lev2 < d_xw[0][None]).astype(jnp.float32)), axis=0)
    tot_xe = jnp.sum(density_of(halo_xe, (lev2 < d_xe[0][None]).astype(jnp.float32)), axis=0)
    tot_ys = jnp.sum(density_of(halo_ys, (lev2 < d_ys[:, 0][None]).astype(jnp.float32)), axis=0)
    tot_yn = jnp.sum(density_of(halo_yn, (lev2 < d_yn[:, 0][None]).astype(jnp.float32)), axis=0)
    side = jnp.zeros((2, col_y), jnp.float32)
    side = side.at[0, :col_x].set(tot_ys).at[1, :col_x].set(tot_yn)
    pack = jnp.concatenate([tot_c, tot_xw[None], tot_xe[None], side], axis=0)
    shallower = jnp.zeros_like(pack)
    for hop in range(1, peers_z):
        pairs_z = [(i, i + hop) for i in range(peers_z - hop)]
        shallower = shallower + lax.ppermute(pack, "gz", pairs_z)
    s_c = shallower[:col_x]
    s_xw = shallower[col_x:col_x + 1]
    s_xe = shallower[col_x + 1:col_x + 2]
    s_ys = shallower[col_x + 2, :col_x][:, None]
    s_yn = shallower[col_x + 3, :col_x][:, None]
    face_row = start_y + jnp.arange(col_y, dtype=jnp.int32)
    wall_n = (face_row <= total_y - 2).astype(jnp.float32)
    wall_s = (face_row - 1 >= 0).astype(jnp.float32)
    coriolis = 0.5 + (face_row.astype(jnp.float32) + 0.5) / total_y
    lanes = jnp.stack([wall_n, wall_s, 0.3 * coriolis] + [jnp.zeros_like(wall_n)] * 5)
    wind_top = jnp.where(place_z == 0, wind, 0.0)
    y, y_ends = fused_solve(state, halo_xw, halo_xe, halo_ys[..., None], halo_yn[..., None],
                            d_c, d_e, d_w, d_n, d_s, d_xw, d_xe, d_ys, d_yn,
                            s_c, s_xw, s_xe, s_ys, s_yn, lanes, wind_top,
                            coupling, inv, ratio)
    y_all = gather_by_permutes(y_ends, "gz", place_z, peers_z)
    x_above, x_below = interface_values(y_all, uv_all, place_z, peers_z)
    pairs = u.shape[0]
    shape5 = (pairs, fields // pairs) + y.shape[1:]
    plane5 = (pairs, fields // pairs, 1, col_x, col_y)
    x_above = x_above.reshape(plane5)
    x_below = x_below.reshape(plane5)
    x = (y.reshape(shape5) + x_above.reshape(plane5) * u[:, None]
         + x_below.reshape(plane5) * v[:, None])
    return x.reshape(y.shape)


def solution(mesh):
    return jax.shard_map(
        per_device,
        mesh=mesh,
        in_specs=(P(None, "gz", "gx", "gy"), P(None, "gz", "gx", "gy"), P(), P(None, "gx", "gy")),
        out_specs=P(None, "gz", "gx", "gy"),
        check_vma=False,
    )
```

```python
import jax
import jax.numpy as jnp
from jax import lax
from jax.experimental import pallas as pl
from jax.experimental.pallas import tpu as pltpu
from jax.sharding import PartitionSpec as P


def padded_2(array, sides, width):
    for axis, dim in sides:
        peers, length = (lax.axis_size(axis), array.shape[dim])
        up = [(i, (i + 1) % peers) for i in range(peers)]
        down = [(j, i) for i, j in up]
        last = lax.slice_in_dim(array, length - width, length, axis=dim)
        initial = lax.slice_in_dim(array, 0, width, axis=dim)
        before = lax.ppermute(last, axis, up)
        after = lax.ppermute(initial, axis, down)
        array = jnp.concatenate([before, array, after], axis=dim)
    return array


def density_of(fields, wet_mask):
    return (-0.3 * fields[0] + 0.7 * fields[1] - 0.05 * fields[0] * fields[0]) * wet_mask


def advance(padded, wet_pad, pressure, wall_face, coriolis):
    wet_x = wet_pad[:, :-1, 1:-1] * wet_pad[:, 1:, 1:-1]
    wet_y = wet_pad[:, 1:-1, :-1] * wet_pad[:, 1:-1, 1:] * wall_face
    east_vel = 0.5 * (padded[2, :, :-1, 1:-1] + padded[2, :, 1:, 1:-1]) * wet_x
    north_vel = 0.5 * (padded[3, :, 1:-1, :-1] + padded[3, :, 1:-1, 1:]) * wet_y
    west_side = padded[:, :, :-1, 1:-1]
    east_side = padded[:, :, 1:, 1:-1]
    flux_x = 0.25 * (
        jnp.maximum(east_vel, 0.0) * west_side + jnp.minimum(east_vel, 0.0) * east_side
    ) - 0.08 * wet_x * (east_side - west_side)
    south_side = padded[:, :, 1:-1, :-1]
    north_side = padded[:, :, 1:-1, 1:]
    flux_y = 0.25 * (
        jnp.maximum(north_vel, 0.0) * south_side + jnp.minimum(north_vel, 0.0) * north_side
    ) - 0.08 * wet_y * (north_side - south_side)
    interior = padded[:, :, 1:-1, 1:-1]
    moved = interior - (
        flux_x[:, :, 1:] - flux_x[:, :, :-1] + flux_y[:, :, :, 1:] - flux_y[:, :, :, :-1]
    )
    centre = pressure[:, 1:-1, 1:-1]
    grad_x = 0.5 * (
        wet_x[:, 1:] * (pressure[:, 2:, 1:-1] - centre)
        + wet_x[:, :-1] * (centre - pressure[:, :-2, 1:-1])
    )
    grad_y = 0.5 * (
        wet_y[:, :, 1:] * (pressure[:, 1:-1, 2:] - centre)
        + wet_y[:, :, :-1] * (centre - pressure[:, 1:-1, :-2])
    )
    east_new = moved[2] + 0.3 * coriolis * interior[3] - grad_x
    north_new = moved[3] - 0.3 * coriolis * interior[2] - grad_y
    wet_inner = wet_pad[:, 1:-1, 1:-1]
    return jnp.stack([moved[0], moved[1], east_new, north_new]) * wet_inner


def coupling_kernel(c_ref, ctop_ref, ratio_ref, inv_ref, u_ref, v_ref, ends_ref):
    levels = c_ref.shape[1]
    ctop = ctop_ref[...]
    ratio_prev = None
    vu_prev = None
    for k in range(levels):
        above = ctop if k == 0 else c_ref[:, k - 1]
        below = c_ref[:, k]
        if k == 0:
            divisor = 1.0 + above + below
        else:
            divisor = 1.0 + above * (1.0 - ratio_prev) + below
        inv = 1.0 / divisor
        ratio = below * inv
        vu = ctop * inv if k == 0 else above * vu_prev * inv
        ratio_ref[:, k] = ratio
        inv_ref[:, k] = inv
        u_ref[:, k] = vu
        ratio_prev, vu_prev = ratio, vu
    u_later = vu_prev
    v_later = ratio_prev
    pairs = c_ref.shape[0]
    ends_ref[pairs:2 * pairs] = u_later
    ends_ref[3 * pairs:4 * pairs] = v_later
    v_ref[:, levels - 1] = v_later
    for k in range(levels - 2, -1, -1):
        ratio = ratio_ref[:, k]
        u_later = u_ref[:, k] + ratio * u_later
        v_later = ratio * v_later
        u_ref[:, k] = u_later
        v_ref[:, k] = v_later
    ends_ref[0:pairs] = u_later
    ends_ref[2 * pairs:3 * pairs] = v_later


def field_kernel(f_ref, c_ref, ctop_ref, ratio_ref, inv_ref, y_ref, ends_ref):
    levels = f_ref.shape[1]
    fields = f_ref.shape[0]
    vy = None
    for k in range(levels):
        inv = jnp.repeat(inv_ref[:, k], 2, axis=0)
        rhs = f_ref[:, k]
        if k == 0:
            vy = rhs * inv
        else:
            above = jnp.repeat(c_ref[:, k - 1], 2, axis=0)
            vy = (rhs + above * vy) * inv
        y_ref[:, k] = vy
    y_later = vy
    ends_ref[fields:2 * fields] = y_later
    for k in range(levels - 2, -1, -1):
        ratio = jnp.repeat(ratio_ref[:, k], 2, axis=0)
        y_later = y_ref[:, k] + ratio * y_later
        y_ref[:, k] = y_later
    ends_ref[0:fields] = y_later


def _specs(lead, levels, bx, cols_y):
    return pl.BlockSpec((lead, levels, bx, cols_y), lambda i: (0, 0, i, 0))


def _plane_spec(lead, bx, cols_y):
    return pl.BlockSpec((lead, bx, cols_y), lambda i: (0, i, 0))


def coupling_solve(coupling, ctop):
    pairs, levels, cols_x, cols_y = coupling.shape
    bx = 8 if cols_x % 8 == 0 else cols_x
    cspec = _specs(pairs, levels, bx, cols_y)
    full = jax.ShapeDtypeStruct(coupling.shape, jnp.float32)
    return pl.pallas_call(
        coupling_kernel,
        grid=(cols_x // bx,),
        in_specs=[cspec, _plane_spec(pairs, bx, cols_y)],
        out_specs=[cspec, cspec, cspec, cspec, _plane_spec(4 * pairs, bx, cols_y)],
        out_shape=[full, full, full, full,
                   jax.ShapeDtypeStruct((4 * pairs, cols_x, cols_y), jnp.float32)],
    )(coupling, ctop)


def field_solve(forced, coupling, ctop, ratio, inv):
    fields, levels, cols_x, cols_y = forced.shape
    pairs = coupling.shape[0]
    bx = 8 if cols_x % 8 == 0 else cols_x
    fspec = _specs(fields, levels, bx, cols_y)
    cspec = _specs(pairs, levels, bx, cols_y)
    return pl.pallas_call(
        field_kernel,
        grid=(cols_x // bx,),
        in_specs=[fspec, cspec, _plane_spec(pairs, bx, cols_y), cspec, cspec],
        out_specs=[fspec, _plane_spec(2 * fields, bx, cols_y)],
        out_shape=[jax.ShapeDtypeStruct(forced.shape, jnp.float32),
                   jax.ShapeDtypeStruct((2 * fields, cols_x, cols_y), jnp.float32)],
    )(forced, coupling, ctop, ratio, inv)


def interface_values(y_ends, uv_ends, place, peers):
    fields = 4
    y0 = y_ends[:, 0:fields]
    y1 = y_ends[:, fields:2 * fields]
    rest = jnp.repeat(uv_ends, 2, axis=1)
    u0 = rest[:, 0:4]
    u1 = rest[:, 4:8]
    v0 = rest[:, 8:12]
    v1 = rest[:, 12:16]
    pt, qt, pb, qb = [], [], [], []
    for q in range(peers):
        if q == 0:
            pt_q, qt_q = y0[q], v0[q]
            pb_q, qb_q = y1[q], v1[q]
        else:
            inv = 1.0 / (1.0 - u0[q] * qb[-1])
            pt_q = (y0[q] + u0[q] * pb[-1]) * inv
            qt_q = v0[q] * inv
            pb_q = y1[q] + u1[q] * (pb[-1] + qb[-1] * pt_q)
            qb_q = v1[q] + u1[q] * qb[-1] * qt_q
        pt.append(pt_q)
        qt.append(qt_q)
        pb.append(pb_q)
        qb.append(qb_q)
    tops = [None] * peers
    bots = [None] * peers
    t_next = jnp.zeros_like(pt[0])
    for q in range(peers - 1, -1, -1):
        tops[q] = pt[q] + qt[q] * t_next
        bots[q] = pb[q] + qb[q] * t_next
        t_next = tops[q]
    above = jnp.zeros_like(pt[0])
    below = jnp.zeros_like(pt[0])
    for q in range(peers):
        if q >= 1:
            above = jnp.where(place == q, bots[q - 1], above)
        if q <= peers - 2:
            below = jnp.where(place == q, tops[q + 1], below)
    return above, below


def gather_by_permutes(part, axis, place, peers):
    received = [part]
    for hop in range(1, peers):
        shift = [(i, (i + hop) % peers) for i in range(peers)]
        received.append(lax.ppermute(part, axis, shift))
    rows = []
    for q in range(peers):
        row = received[0]
        for hop in range(1, peers):
            row = jnp.where((place - hop) % peers == q, received[hop], row)
        rows.append(row)
    return jnp.stack(rows)


def _density(t, s, w):
    return (-0.3 * t + 0.7 * s - 0.05 * t * t) * w


def _flux(vel, lo, hi, w):
    return 0.25 * (jnp.maximum(vel, 0.0) * lo + jnp.minimum(vel, 0.0) * hi) - 0.08 * w * (hi - lo)


def fused_kernel(st_ref, xw_ref, xe_ref, ys_ref, yn_ref,
                 dc_ref, de_ref, dw_ref, dn_ref, ds_ref,
                 dxw_ref, dxe_ref, dys_ref, dyn_ref,
                 sc_ref, sxw_ref, sxe_ref, sys_ref, syn_ref,
                 lane_ref, wind_ref, c_ref, inv_ref, ratio_ref,
                 y_ref, ends_ref,
                 run_c_s, run_xw_s, run_xe_s, run_ys_s, run_yn_s, vy_s, cprev_s):
    fields, chunk, nx, ny = st_ref.shape
    levels = y_ref.shape[1]
    step_i = pl.program_id(0)
    row = lax.broadcasted_iota(jnp.int32, (nx, ny), 0)
    lane = lax.broadcasted_iota(jnp.int32, (nx, ny), 1)
    wall_n = lane_ref[0:1]
    wall_s = lane_ref[1:2]
    cor03 = lane_ref[2:3]
    d_c, d_e, d_w, d_n, d_s = dc_ref[...], de_ref[...], dw_ref[...], dn_ref[...], ds_ref[...]
    d_xw, d_xe, d_ys, d_yn = dxw_ref[...], dxe_ref[...], dys_ref[...], dyn_ref[...]

    @pl.when(step_i == 0)
    def _():
        run_c_s[...] = jnp.zeros_like(run_c_s)
        run_xw_s[...] = jnp.zeros_like(run_xw_s)
        run_xe_s[...] = jnp.zeros_like(run_xe_s)
        run_ys_s[...] = jnp.zeros_like(run_ys_s)
        run_yn_s[...] = jnp.zeros_like(run_yn_s)
        vy_s[...] = jnp.zeros_like(vy_s)
        cprev_s[...] = jnp.zeros_like(cprev_s)

    def east(r, h):
        return jnp.where(row == nx - 1, h, pltpu.roll(r, nx - 1, 0))

    def west(r, h):
        return jnp.where(row == 0, h, pltpu.roll(r, 1, 0))

    def north(r, h):
        return jnp.where(lane == ny - 1, h, pltpu.roll(r, ny - 1, 1))

    def south(r, h):
        return jnp.where(lane == 0, h, pltpu.roll(r, 1, 1))

    def level(kk, carry):
        run, vy_prev, c_prev = carry
        k = step_i * chunk + kk
        wc = (k < d_c).astype(jnp.float32)
        we = (k < d_e).astype(jnp.float32)
        ww = (k < d_w).astype(jnp.float32)
        wn = (k < d_n).astype(jnp.float32)
        ws = (k < d_s).astype(jnp.float32)
        wxw = (k < d_xw).astype(jnp.float32)
        wxe = (k < d_xe).astype(jnp.float32)
        wys = (k < d_ys).astype(jnp.float32)
        wyn = (k < d_yn).astype(jnp.float32)
        cen = [st_ref[f, kk] for f in range(fields)]
        hxw = [xw_ref[f, pl.ds(k, 1), :] for f in range(fields)]
        hxe = [xe_ref[f, pl.ds(k, 1), :] for f in range(fields)]
        hys = [ys_ref[f, kk] for f in range(fields)]
        hyn = [yn_ref[f, kk] for f in range(fields)]
        run_c, run_xw, run_xe, run_ys, run_yn = run
        den_c = _density(cen[0], cen[1], wc)
        den_xw = _density(hxw[0], hxw[1], wxw)
        den_xe = _density(hxe[0], hxe[1], wxe)
        den_ys = _density(hys[0], hys[1], wys)
        den_yn = _density(hyn[0], hyn[1], wyn)
        run_c = run_c + den_c
        run_xw = run_xw + den_xw
        run_xe = run_xe + den_xe
        run_ys = run_ys + den_ys
        run_yn = run_yn + den_yn
        p_c = 0.03 * (sc_ref[...] + run_c - 0.5 * den_c)
        p_xw = 0.03 * (sxw_ref[...] + run_xw - 0.5 * den_xw)
        p_xe = 0.03 * (sxe_ref[...] + run_xe - 0.5 * den_xe)
        p_ys = 0.03 * (sys_ref[...] + run_ys - 0.5 * den_ys)
        p_yn = 0.03 * (syn_ref[...] + run_yn - 0.5 * den_yn)
        p_e = east(p_c, p_xe)
        p_w = west(p_c, p_xw)
        p_n = north(p_c, p_yn)
        p_s = south(p_c, p_ys)
        face_e = wc * we
        face_w = ww * wc
        face_n = wc * wn * wall_n
        face_s = ws * wc * wall_s
        nbr_e = [east(cen[f], hxe[f]) for f in range(fields)]
        nbr_w = [west(cen[f], hxw[f]) for f in range(fields)]
        nbr_n = [north(cen[f], hyn[f]) for f in range(fields)]
        nbr_s = [south(cen[f], hys[f]) for f in range(fields)]
        vel_e = 0.5 * (cen[2] + nbr_e[2]) * face_e
        vel_w = 0.5 * (nbr_w[2] + cen[2]) * face_w
        vel_n = 0.5 * (cen[3] + nbr_n[3]) * face_n
        vel_s = 0.5 * (nbr_s[3] + cen[3]) * face_s
        moved = []
        for f in range(fields):
            fe = _flux(vel_e, cen[f], nbr_e[f], face_e)
            fw = _flux(vel_w, nbr_w[f], cen[f], face_w)
            fn = _flux(vel_n, cen[f], nbr_n[f], face_n)
            fs = _flux(vel_s, nbr_s[f], cen[f], face_s)
            moved.append(cen[f] - (fe - fw + fn - fs))
        grad_x = 0.5 * (face_e * (p_e - p_c) + face_w * (p_c - p_w))
        grad_y = 0.5 * (face_n * (p_n - p_c) + face_s * (p_c - p_s))
        east_new = moved[2] + cor03 * cen[3] - grad_x
        north_new = moved[3] - cor03 * cen[2] - grad_y
        top = (k == 0).astype(jnp.float32)
        forced = [moved[0] * wc, moved[1] * wc,
                  east_new * wc + wind_ref[0] * wc * top,
                  north_new * wc + wind_ref[1] * wc * top]
        vy = []
        for f in range(fields):
            m = f // 2
            val = (forced[f] + c_prev[m] * vy_prev[f]) * inv_ref[m, kk]
            y_ref[f, k] = val
            vy.append(val)
        c_here = jnp.stack([c_ref[0, kk], c_ref[1, kk]])
        return (run_c, run_xw, run_xe, run_ys, run_yn), jnp.stack(vy), c_here

    run = (run_c_s[...], run_xw_s[...], run_xe_s[...], run_ys_s[...], run_yn_s[...])
    carry = lax.fori_loop(0, chunk, level, (run, vy_s[...], cprev_s[...]), unroll=2)
    run, vy, c_prev = carry
    run_c_s[...], run_xw_s[...], run_xe_s[...], run_ys_s[...], run_yn_s[...] = run
    vy_s[...] = vy
    cprev_s[...] = c_prev

    @pl.when(step_i == pl.num_programs(0) - 1)
    def _():
        for f in range(fields):
            ends_ref[fields + f] = vy[f]

        def back(j, later):
            k = levels - 2 - j
            out = []
            for f in range(fields):
                val = y_ref[f, k] + ratio_ref[f // 2, k] * later[f]
                y_ref[f, k] = val
                out.append(val)
            return jnp.stack(out)

        later = lax.fori_loop(0, levels - 1, back, vy, unroll=2)
        for f in range(fields):
            ends_ref[f] = later[f]


def fused_solve(*operands):
    st = operands[0]
    fields, levels, nx, ny = st.shape
    pairs = operands[21].shape[0]
    chunk = 8 if levels % 8 == 0 else levels
    whole = [pl.BlockSpec(op.shape, (lambda i, n=op.ndim: (0,) * n)) for op in operands]
    by_level = lambda op: pl.BlockSpec((op.shape[0], chunk) + op.shape[2:], lambda i: (0, i, 0, 0))
    specs = list(whole)
    for idx in (0, 3, 4, 21, 22):
        specs[idx] = by_level(operands[idx])
    return pl.pallas_call(
        fused_kernel,
        grid=(levels // chunk,),
        in_specs=specs,
        out_specs=[pl.BlockSpec(st.shape, lambda i: (0, 0, 0, 0)),
                   pl.BlockSpec((2 * fields, nx, ny), lambda i: (0, 0, 0))],
        out_shape=[jax.ShapeDtypeStruct(st.shape, jnp.float32),
                   jax.ShapeDtypeStruct((2 * fields, nx, ny), jnp.float32)],
        scratch_shapes=[pltpu.VMEM((nx, ny), jnp.float32), pltpu.VMEM((1, ny), jnp.float32),
                        pltpu.VMEM((1, ny), jnp.float32), pltpu.VMEM((nx, 1), jnp.float32),
                        pltpu.VMEM((nx, 1), jnp.float32), pltpu.VMEM((fields, nx, ny), jnp.float32),
                        pltpu.VMEM((pairs, nx, ny), jnp.float32)],
        compiler_params=pltpu.CompilerParams(vmem_limit_bytes=60 * 1024 * 1024),
    )(*operands)


def per_device(state, mixing, depth_levels, wind):
    fields, lev_count, col_x, col_y = state.shape
    total_x, total_y = depth_levels.shape
    peers_z = lax.axis_size("gz")
    place_z = lax.axis_index("gz")
    peers_x = lax.axis_size("gx")
    peers_y = lax.axis_size("gy")
    start_x = lax.axis_index("gx") * col_x
    start_y = lax.axis_index("gy") * col_y
    start_z = place_z * lev_count
    down_z = [(i, i + 1) for i in range(peers_z - 1)]
    mix_above = lax.ppermute(mixing[:, lev_count - 1], "gz", down_z)
    up_x = [(i, (i + 1) % peers_x) for i in range(peers_x)]
    dn_x = [(j, i) for i, j in up_x]
    up_y = [(i, (i + 1) % peers_y) for i in range(peers_y)]
    dn_y = [(j, i) for i, j in up_y]
    halo_xw = lax.ppermute(state[:, :, col_x - 1], "gx", up_x)
    halo_xe = lax.ppermute(state[:, :, 0], "gx", dn_x)
    halo_ys = lax.ppermute(state[:, :, :, col_y - 1], "gy", up_y)
    halo_yn = lax.ppermute(state[:, :, :, 0], "gy", dn_y)
    levels = start_z + jnp.arange(lev_count, dtype=jnp.int32)
    row_index = (start_x - 1 + jnp.arange(col_x + 2, dtype=jnp.int32)) % total_x
    col_index = (start_y - 1 + jnp.arange(col_y + 2, dtype=jnp.int32)) % total_y
    depth_pad = jnp.take(jnp.take(depth_levels, row_index, axis=0), col_index, axis=1) - start_z
    d_c = depth_pad[1:-1, 1:-1]
    d_e = depth_pad[2:, 1:-1]
    d_w = depth_pad[:-2, 1:-1]
    d_n = depth_pad[1:-1, 2:]
    d_s = depth_pad[1:-1, :-2]
    d_xw = depth_pad[0:1, 1:-1]
    d_xe = depth_pad[col_x + 1:, 1:-1]
    d_ys = depth_pad[1:-1, 0:1]
    d_yn = depth_pad[1:-1, col_y + 1:]
    local = jnp.arange(lev_count, dtype=jnp.int32)
    wet_here = (local[:, None, None] < d_c[None]).astype(jnp.float32)
    wet_next = ((local + 1)[:, None, None] < d_c[None]).astype(jnp.float32)
    coupling = mixing * (wet_here * wet_next)[None]
    wet_up = (-1 < d_c).astype(jnp.float32)
    ctop = mix_above * (wet_up * wet_here[0])[None]
    ctop = jnp.where(place_z > 0, ctop, 0.0)
    ratio, inv, u, v, uv_ends = coupling_solve(coupling, ctop)
    uv_all = lax.all_gather(uv_ends, "gz")
    lev3 = local[:, None, None]
    tot_c = jnp.sum(density_of(state, (lev3 < d_c[None]).astype(jnp.float32)), axis=0)
    lev2 = local[:, None]
    tot_xw = jnp.sum(density_of(halo_xw, (lev2 < d_xw[0][None]).astype(jnp.float32)), axis=0)
    tot_xe = jnp.sum(density_of(halo_xe, (lev2 < d_xe[0][None]).astype(jnp.float32)), axis=0)
    tot_ys = jnp.sum(density_of(halo_ys, (lev2 < d_ys[:, 0][None]).astype(jnp.float32)), axis=0)
    tot_yn = jnp.sum(density_of(halo_yn, (lev2 < d_yn[:, 0][None]).astype(jnp.float32)), axis=0)
    side = jnp.zeros((2, col_y), jnp.float32)
    side = side.at[0, :col_x].set(tot_ys).at[1, :col_x].set(tot_yn)
    pack = jnp.concatenate([tot_c, tot_xw[None], tot_xe[None], side], axis=0)
    shallower = jnp.zeros_like(pack)
    for hop in range(1, peers_z):
        pairs_z = [(i, i + hop) for i in range(peers_z - hop)]
        shallower = shallower + lax.ppermute(pack, "gz", pairs_z)
    s_c = shallower[:col_x]
    s_xw = shallower[col_x:col_x + 1]
    s_xe = shallower[col_x + 1:col_x + 2]
    s_ys = shallower[col_x + 2, :col_x][:, None]
    s_yn = shallower[col_x + 3, :col_x][:, None]
    face_row = start_y + jnp.arange(col_y, dtype=jnp.int32)
    wall_n = (face_row <= total_y - 2).astype(jnp.float32)
    wall_s = (face_row - 1 >= 0).astype(jnp.float32)
    coriolis = 0.5 + (face_row.astype(jnp.float32) + 0.5) / total_y
    lanes = jnp.stack([wall_n, wall_s, 0.3 * coriolis] + [jnp.zeros_like(wall_n)] * 5)
    wind_top = jnp.where(place_z == 0, wind, 0.0)
    y, y_ends = fused_solve(state, halo_xw, halo_xe, halo_ys[..., None], halo_yn[..., None],
                            d_c, d_e, d_w, d_n, d_s, d_xw, d_xe, d_ys, d_yn,
                            s_c, s_xw, s_xe, s_ys, s_yn, lanes, wind_top,
                            coupling, inv, ratio)
    y_all = gather_by_permutes(y_ends, "gz", place_z, peers_z)
    x_above, x_below = interface_values(y_all, uv_all, place_z, peers_z)
    pairs = u.shape[0]
    shape5 = (pairs, fields // pairs) + y.shape[1:]
    plane5 = (pairs, fields // pairs, 1, col_x, col_y)
    x = (y.reshape(shape5) + x_above.reshape(plane5) * u[:, None]
         + x_below.reshape(plane5) * v[:, None])
    return x.reshape(y.shape)


def solution(mesh):
    return jax.shard_map(
        per_device,
        mesh=mesh,
        in_specs=(P(None, "gz", "gx", "gy"), P(None, "gz", "gx", "gy"), P(), P(None, "gx", "gy")),
        out_specs=P(None, "gz", "gx", "gy"),
        check_vma=False,
    )
```

```python
import jax
import jax.numpy as jnp
from jax import lax
from jax.experimental import pallas as pl
from jax.experimental.pallas import tpu as pltpu
from jax.sharding import PartitionSpec as P


def padded_2(array, sides, width):
    for axis, dim in sides:
        peers, length = (lax.axis_size(axis), array.shape[dim])
        up = [(i, (i + 1) % peers) for i in range(peers)]
        down = [(j, i) for i, j in up]
        last = lax.slice_in_dim(array, length - width, length, axis=dim)
        initial = lax.slice_in_dim(array, 0, width, axis=dim)
        before = lax.ppermute(last, axis, up)
        after = lax.ppermute(initial, axis, down)
        array = jnp.concatenate([before, array, after], axis=dim)
    return array


def density_of(fields, wet_mask):
    return (-0.3 * fields[0] + 0.7 * fields[1] - 0.05 * fields[0] * fields[0]) * wet_mask


def advance(padded, wet_pad, pressure, wall_face, coriolis):
    wet_x = wet_pad[:, :-1, 1:-1] * wet_pad[:, 1:, 1:-1]
    wet_y = wet_pad[:, 1:-1, :-1] * wet_pad[:, 1:-1, 1:] * wall_face
    east_vel = 0.5 * (padded[2, :, :-1, 1:-1] + padded[2, :, 1:, 1:-1]) * wet_x
    north_vel = 0.5 * (padded[3, :, 1:-1, :-1] + padded[3, :, 1:-1, 1:]) * wet_y
    west_side = padded[:, :, :-1, 1:-1]
    east_side = padded[:, :, 1:, 1:-1]
    flux_x = 0.25 * (
        jnp.maximum(east_vel, 0.0) * west_side + jnp.minimum(east_vel, 0.0) * east_side
    ) - 0.08 * wet_x * (east_side - west_side)
    south_side = padded[:, :, 1:-1, :-1]
    north_side = padded[:, :, 1:-1, 1:]
    flux_y = 0.25 * (
        jnp.maximum(north_vel, 0.0) * south_side + jnp.minimum(north_vel, 0.0) * north_side
    ) - 0.08 * wet_y * (north_side - south_side)
    interior = padded[:, :, 1:-1, 1:-1]
    moved = interior - (
        flux_x[:, :, 1:] - flux_x[:, :, :-1] + flux_y[:, :, :, 1:] - flux_y[:, :, :, :-1]
    )
    centre = pressure[:, 1:-1, 1:-1]
    grad_x = 0.5 * (
        wet_x[:, 1:] * (pressure[:, 2:, 1:-1] - centre)
        + wet_x[:, :-1] * (centre - pressure[:, :-2, 1:-1])
    )
    grad_y = 0.5 * (
        wet_y[:, :, 1:] * (pressure[:, 1:-1, 2:] - centre)
        + wet_y[:, :, :-1] * (centre - pressure[:, 1:-1, :-2])
    )
    east_new = moved[2] + 0.3 * coriolis * interior[3] - grad_x
    north_new = moved[3] - 0.3 * coriolis * interior[2] - grad_y
    wet_inner = wet_pad[:, 1:-1, 1:-1]
    return jnp.stack([moved[0], moved[1], east_new, north_new]) * wet_inner


def coupling_kernel(c_ref, ctop_ref, ratio_ref, inv_ref, u_ref, v_ref, ends_ref):
    levels = c_ref.shape[1]
    ctop = ctop_ref[...]
    ratio_prev = None
    vu_prev = None
    for k in range(levels):
        above = ctop if k == 0 else c_ref[:, k - 1]
        below = c_ref[:, k]
        if k == 0:
            divisor = 1.0 + above + below
        else:
            divisor = 1.0 + above * (1.0 - ratio_prev) + below
        inv = 1.0 / divisor
        ratio = below * inv
        vu = ctop * inv if k == 0 else above * vu_prev * inv
        ratio_ref[:, k] = ratio
        inv_ref[:, k] = inv
        u_ref[:, k] = vu
        ratio_prev, vu_prev = ratio, vu
    u_later = vu_prev
    v_later = ratio_prev
    pairs = c_ref.shape[0]
    per = ends_ref.shape[0] // (4 * pairs)
    for f in range(pairs * per):
        ends_ref[pairs * per + f] = u_later[f // per]
        ends_ref[3 * pairs * per + f] = v_later[f // per]
    v_ref[:, levels - 1] = v_later
    for k in range(levels - 2, -1, -1):
        ratio = ratio_ref[:, k]
        u_later = u_ref[:, k] + ratio * u_later
        v_later = ratio * v_later
        u_ref[:, k] = u_later
        v_ref[:, k] = v_later
    for f in range(pairs * per):
        ends_ref[f] = u_later[f // per]
        ends_ref[2 * pairs * per + f] = v_later[f // per]


def field_kernel(f_ref, c_ref, ctop_ref, ratio_ref, inv_ref, y_ref, ends_ref):
    levels = f_ref.shape[1]
    fields = f_ref.shape[0]
    vy = None
    for k in range(levels):
        inv = jnp.repeat(inv_ref[:, k], 2, axis=0)
        rhs = f_ref[:, k]
        if k == 0:
            vy = rhs * inv
        else:
            above = jnp.repeat(c_ref[:, k - 1], 2, axis=0)
            vy = (rhs + above * vy) * inv
        y_ref[:, k] = vy
    y_later = vy
    ends_ref[fields:2 * fields] = y_later
    for k in range(levels - 2, -1, -1):
        ratio = jnp.repeat(ratio_ref[:, k], 2, axis=0)
        y_later = y_ref[:, k] + ratio * y_later
        y_ref[:, k] = y_later
    ends_ref[0:fields] = y_later


def _specs(lead, levels, bx, cols_y):
    return pl.BlockSpec((lead, levels, bx, cols_y), lambda i: (0, 0, i, 0))


def _plane_spec(lead, bx, cols_y):
    return pl.BlockSpec((lead, bx, cols_y), lambda i: (0, i, 0))


def coupling_solve(coupling, ctop, fields):
    pairs, levels, cols_x, cols_y = coupling.shape
    bx = 8 if cols_x % 8 == 0 else cols_x
    cspec = _specs(pairs, levels, bx, cols_y)
    full = jax.ShapeDtypeStruct(coupling.shape, jnp.float32)
    return pl.pallas_call(
        coupling_kernel,
        grid=(cols_x // bx,),
        in_specs=[cspec, _plane_spec(pairs, bx, cols_y)],
        out_specs=[cspec, cspec, cspec, cspec, _plane_spec(4 * fields, bx, cols_y)],
        out_shape=[full, full, full, full,
                   jax.ShapeDtypeStruct((4 * fields, cols_x, cols_y), jnp.float32)],
    )(coupling, ctop)


def field_solve(forced, coupling, ctop, ratio, inv):
    fields, levels, cols_x, cols_y = forced.shape
    pairs = coupling.shape[0]
    bx = 8 if cols_x % 8 == 0 else cols_x
    fspec = _specs(fields, levels, bx, cols_y)
    cspec = _specs(pairs, levels, bx, cols_y)
    return pl.pallas_call(
        field_kernel,
        grid=(cols_x // bx,),
        in_specs=[fspec, cspec, _plane_spec(pairs, bx, cols_y), cspec, cspec],
        out_specs=[fspec, _plane_spec(2 * fields, bx, cols_y)],
        out_shape=[jax.ShapeDtypeStruct(forced.shape, jnp.float32),
                   jax.ShapeDtypeStruct((2 * fields, cols_x, cols_y), jnp.float32)],
    )(forced, coupling, ctop, ratio, inv)


def interface_values(y_ends, uv_ends, place, peers):
    fields = 4
    y0 = y_ends[:, 0:fields]
    y1 = y_ends[:, fields:2 * fields]
    rest = uv_ends
    u0 = rest[:, 0:4]
    u1 = rest[:, 4:8]
    v0 = rest[:, 8:12]
    v1 = rest[:, 12:16]
    pt, qt, pb, qb = [], [], [], []
    for q in range(peers):
        if q == 0:
            pt_q, qt_q = y0[q], v0[q]
            pb_q, qb_q = y1[q], v1[q]
        else:
            inv = 1.0 / (1.0 - u0[q] * qb[-1])
            pt_q = (y0[q] + u0[q] * pb[-1]) * inv
            qt_q = v0[q] * inv
            pb_q = y1[q] + u1[q] * (pb[-1] + qb[-1] * pt_q)
            qb_q = v1[q] + u1[q] * qb[-1] * qt_q
        pt.append(pt_q)
        qt.append(qt_q)
        pb.append(pb_q)
        qb.append(qb_q)
    tops = [None] * peers
    bots = [None] * peers
    t_next = jnp.zeros_like(pt[0])
    for q in range(peers - 1, -1, -1):
        tops[q] = pt[q] + qt[q] * t_next
        bots[q] = pb[q] + qb[q] * t_next
        t_next = tops[q]
    above = jnp.zeros_like(pt[0])
    below = jnp.zeros_like(pt[0])
    for q in range(peers):
        if q >= 1:
            above = jnp.where(place == q, bots[q - 1], above)
        if q <= peers - 2:
            below = jnp.where(place == q, tops[q + 1], below)
    return above, below


def gather_by_permutes(part, axis, place, peers):
    received = [part]
    for hop in range(1, peers):
        shift = [(i, (i + hop) % peers) for i in range(peers)]
        received.append(lax.ppermute(part, axis, shift))
    rows = []
    for q in range(peers):
        row = received[0]
        for hop in range(1, peers):
            row = jnp.where((place - hop) % peers == q, received[hop], row)
        rows.append(row)
    return jnp.stack(rows)


def _density(t, s, w):
    return (-0.3 * t + 0.7 * s - 0.05 * t * t) * w


def _flux(vel, lo, hi, w):
    return 0.25 * (jnp.maximum(vel, 0.0) * lo + jnp.minimum(vel, 0.0) * hi) - 0.08 * w * (hi - lo)


def fused_kernel(st_ref, xw_ref, xe_ref, ys_ref, yn_ref,
                 dc_ref, de_ref, dw_ref, dn_ref, ds_ref,
                 dxw_ref, dxe_ref, dys_ref, dyn_ref,
                 sc_ref, sxw_ref, sxe_ref, sys_ref, syn_ref,
                 lane_ref, wind_ref, c_ref, inv_ref, ratio_ref,
                 y_ref, ends_ref,
                 run_c_s, run_xw_s, run_xe_s, run_ys_s, run_yn_s, vy_s, cprev_s):
    fields, chunk, nx, ny = st_ref.shape
    levels = y_ref.shape[1]
    step_i = pl.program_id(0)
    row = lax.broadcasted_iota(jnp.int32, (nx, ny), 0)
    lane = lax.broadcasted_iota(jnp.int32, (nx, ny), 1)
    wall_n = lane_ref[0:1]
    wall_s = lane_ref[1:2]
    cor03 = lane_ref[2:3]
    d_c, d_e, d_w, d_n, d_s = dc_ref[...], de_ref[...], dw_ref[...], dn_ref[...], ds_ref[...]
    d_xw, d_xe, d_ys, d_yn = dxw_ref[...], dxe_ref[...], dys_ref[...], dyn_ref[...]

    @pl.when(step_i == 0)
    def _():
        run_c_s[...] = jnp.zeros_like(run_c_s)
        run_xw_s[...] = jnp.zeros_like(run_xw_s)
        run_xe_s[...] = jnp.zeros_like(run_xe_s)
        run_ys_s[...] = jnp.zeros_like(run_ys_s)
        run_yn_s[...] = jnp.zeros_like(run_yn_s)
        vy_s[...] = jnp.zeros_like(vy_s)
        cprev_s[...] = jnp.zeros_like(cprev_s)

    def east(r, h):
        return jnp.where(row == nx - 1, h, pltpu.roll(r, nx - 1, 0))

    def west(r, h):
        return jnp.where(row == 0, h, pltpu.roll(r, 1, 0))

    def north(r, h):
        return jnp.where(lane == ny - 1, h, pltpu.roll(r, ny - 1, 1))

    def south(r, h):
        return jnp.where(lane == 0, h, pltpu.roll(r, 1, 1))

    def level(kk, carry):
        run, vy_prev, c_prev = carry
        k = step_i * chunk + kk
        wc = (k < d_c).astype(jnp.float32)
        we = (k < d_e).astype(jnp.float32)
        ww = (k < d_w).astype(jnp.float32)
        wn = (k < d_n).astype(jnp.float32)
        ws = (k < d_s).astype(jnp.float32)
        wxw = (k < d_xw).astype(jnp.float32)
        wxe = (k < d_xe).astype(jnp.float32)
        wys = (k < d_ys).astype(jnp.float32)
        wyn = (k < d_yn).astype(jnp.float32)
        cen = [st_ref[f, kk] for f in range(fields)]
        hxw = [xw_ref[f, pl.ds(k, 1), :] for f in range(fields)]
        hxe = [xe_ref[f, pl.ds(k, 1), :] for f in range(fields)]
        hys = [ys_ref[f, kk] for f in range(fields)]
        hyn = [yn_ref[f, kk] for f in range(fields)]
        run_c, run_xw, run_xe, run_ys, run_yn = run
        den_c = _density(cen[0], cen[1], wc)
        den_xw = _density(hxw[0], hxw[1], wxw)
        den_xe = _density(hxe[0], hxe[1], wxe)
        den_ys = _density(hys[0], hys[1], wys)
        den_yn = _density(hyn[0], hyn[1], wyn)
        run_c = run_c + den_c
        run_xw = run_xw + den_xw
        run_xe = run_xe + den_xe
        run_ys = run_ys + den_ys
        run_yn = run_yn + den_yn
        p_c = 0.03 * (sc_ref[...] + run_c - 0.5 * den_c)
        p_xw = 0.03 * (sxw_ref[...] + run_xw - 0.5 * den_xw)
        p_xe = 0.03 * (sxe_ref[...] + run_xe - 0.5 * den_xe)
        p_ys = 0.03 * (sys_ref[...] + run_ys - 0.5 * den_ys)
        p_yn = 0.03 * (syn_ref[...] + run_yn - 0.5 * den_yn)
        p_e = east(p_c, p_xe)
        p_w = west(p_c, p_xw)
        p_n = north(p_c, p_yn)
        p_s = south(p_c, p_ys)
        face_e = wc * we
        face_w = ww * wc
        face_n = wc * wn * wall_n
        face_s = ws * wc * wall_s
        nbr_e = [east(cen[f], hxe[f]) for f in range(fields)]
        nbr_w = [west(cen[f], hxw[f]) for f in range(fields)]
        nbr_n = [north(cen[f], hyn[f]) for f in range(fields)]
        nbr_s = [south(cen[f], hys[f]) for f in range(fields)]
        vel_e = 0.5 * (cen[2] + nbr_e[2]) * face_e
        vel_w = 0.5 * (nbr_w[2] + cen[2]) * face_w
        vel_n = 0.5 * (cen[3] + nbr_n[3]) * face_n
        vel_s = 0.5 * (nbr_s[3] + cen[3]) * face_s
        moved = []
        for f in range(fields):
            fe = _flux(vel_e, cen[f], nbr_e[f], face_e)
            fw = _flux(vel_w, nbr_w[f], cen[f], face_w)
            fn = _flux(vel_n, cen[f], nbr_n[f], face_n)
            fs = _flux(vel_s, nbr_s[f], cen[f], face_s)
            moved.append(cen[f] - (fe - fw + fn - fs))
        grad_x = 0.5 * (face_e * (p_e - p_c) + face_w * (p_c - p_w))
        grad_y = 0.5 * (face_n * (p_n - p_c) + face_s * (p_c - p_s))
        east_new = moved[2] + cor03 * cen[3] - grad_x
        north_new = moved[3] - cor03 * cen[2] - grad_y
        top = (k == 0).astype(jnp.float32)
        forced = [moved[0] * wc, moved[1] * wc,
                  east_new * wc + wind_ref[0] * wc * top,
                  north_new * wc + wind_ref[1] * wc * top]
        vy = []
        for f in range(fields):
            m = f // 2
            val = (forced[f] + c_prev[m] * vy_prev[f]) * inv_ref[m, kk]
            y_ref[f, k] = val
            vy.append(val)
        c_here = jnp.stack([c_ref[0, kk], c_ref[1, kk]])
        return (run_c, run_xw, run_xe, run_ys, run_yn), jnp.stack(vy), c_here

    run = (run_c_s[...], run_xw_s[...], run_xe_s[...], run_ys_s[...], run_yn_s[...])
    carry = lax.fori_loop(0, chunk, level, (run, vy_s[...], cprev_s[...]), unroll=2)
    run, vy, c_prev = carry
    run_c_s[...], run_xw_s[...], run_xe_s[...], run_ys_s[...], run_yn_s[...] = run
    vy_s[...] = vy
    cprev_s[...] = c_prev

    @pl.when(step_i == pl.num_programs(0) - 1)
    def _():
        for f in range(fields):
            ends_ref[fields + f] = vy[f]

        def back(j, later):
            k = levels - 2 - j
            out = []
            for f in range(fields):
                val = y_ref[f, k] + ratio_ref[f // 2, k] * later[f]
                y_ref[f, k] = val
                out.append(val)
            return jnp.stack(out)

        later = lax.fori_loop(0, levels - 1, back, vy, unroll=2)
        for f in range(fields):
            ends_ref[f] = later[f]


def fused_solve(*operands):
    st = operands[0]
    fields, levels, nx, ny = st.shape
    pairs = operands[21].shape[0]
    chunk = 8 if levels % 8 == 0 else levels
    whole = [pl.BlockSpec(op.shape, (lambda i, n=op.ndim: (0,) * n)) for op in operands]
    by_level = lambda op: pl.BlockSpec((op.shape[0], chunk) + op.shape[2:], lambda i: (0, i, 0, 0))
    specs = list(whole)
    for idx in (0, 3, 4, 21, 22):
        specs[idx] = by_level(operands[idx])
    return pl.pallas_call(
        fused_kernel,
        grid=(levels // chunk,),
        in_specs=specs,
        out_specs=[pl.BlockSpec(st.shape, lambda i: (0, 0, 0, 0)),
                   pl.BlockSpec((2 * fields, nx, ny), lambda i: (0, 0, 0))],
        out_shape=[jax.ShapeDtypeStruct(st.shape, jnp.float32),
                   jax.ShapeDtypeStruct((2 * fields, nx, ny), jnp.float32)],
        scratch_shapes=[pltpu.VMEM((nx, ny), jnp.float32), pltpu.VMEM((1, ny), jnp.float32),
                        pltpu.VMEM((1, ny), jnp.float32), pltpu.VMEM((nx, 1), jnp.float32),
                        pltpu.VMEM((nx, 1), jnp.float32), pltpu.VMEM((fields, nx, ny), jnp.float32),
                        pltpu.VMEM((pairs, nx, ny), jnp.float32)],
        compiler_params=pltpu.CompilerParams(vmem_limit_bytes=60 * 1024 * 1024),
    )(*operands)


def per_device(state, mixing, depth_levels, wind):
    fields, lev_count, col_x, col_y = state.shape
    total_x, total_y = depth_levels.shape
    peers_z = lax.axis_size("gz")
    place_z = lax.axis_index("gz")
    peers_x = lax.axis_size("gx")
    peers_y = lax.axis_size("gy")
    start_x = lax.axis_index("gx") * col_x
    start_y = lax.axis_index("gy") * col_y
    start_z = place_z * lev_count
    down_z = [(i, i + 1) for i in range(peers_z - 1)]
    mix_above = lax.ppermute(mixing[:, lev_count - 1], "gz", down_z)
    up_x = [(i, (i + 1) % peers_x) for i in range(peers_x)]
    dn_x = [(j, i) for i, j in up_x]
    up_y = [(i, (i + 1) % peers_y) for i in range(peers_y)]
    dn_y = [(j, i) for i, j in up_y]
    halo_xw = lax.ppermute(state[:, :, col_x - 1], "gx", up_x)
    halo_xe = lax.ppermute(state[:, :, 0], "gx", dn_x)
    halo_ys = lax.ppermute(state[:, :, :, col_y - 1], "gy", up_y)
    halo_yn = lax.ppermute(state[:, :, :, 0], "gy", dn_y)
    levels = start_z + jnp.arange(lev_count, dtype=jnp.int32)
    row_index = (start_x - 1 + jnp.arange(col_x + 2, dtype=jnp.int32)) % total_x
    col_index = (start_y - 1 + jnp.arange(col_y + 2, dtype=jnp.int32)) % total_y
    depth_pad = jnp.take(jnp.take(depth_levels, row_index, axis=0), col_index, axis=1) - start_z
    d_c = depth_pad[1:-1, 1:-1]
    d_e = depth_pad[2:, 1:-1]
    d_w = depth_pad[:-2, 1:-1]
    d_n = depth_pad[1:-1, 2:]
    d_s = depth_pad[1:-1, :-2]
    d_xw = depth_pad[0:1, 1:-1]
    d_xe = depth_pad[col_x + 1:, 1:-1]
    d_ys = depth_pad[1:-1, 0:1]
    d_yn = depth_pad[1:-1, col_y + 1:]
    local = jnp.arange(lev_count, dtype=jnp.int32)
    wet_here = (local[:, None, None] < d_c[None]).astype(jnp.float32)
    wet_next = ((local + 1)[:, None, None] < d_c[None]).astype(jnp.float32)
    coupling = mixing * (wet_here * wet_next)[None]
    wet_up = (-1 < d_c).astype(jnp.float32)
    ctop = mix_above * (wet_up * wet_here[0])[None]
    ctop = jnp.where(place_z > 0, ctop, 0.0)
    ratio, inv, u, v, uv_ends = coupling_solve(coupling, ctop, fields)
    uv_all = lax.all_gather(uv_ends, "gz")
    lev3 = local[:, None, None]
    tot_c = jnp.sum(density_of(state, (lev3 < d_c[None]).astype(jnp.float32)), axis=0)
    lev2 = local[:, None]
    tot_xw = jnp.sum(density_of(halo_xw, (lev2 < d_xw[0][None]).astype(jnp.float32)), axis=0)
    tot_xe = jnp.sum(density_of(halo_xe, (lev2 < d_xe[0][None]).astype(jnp.float32)), axis=0)
    tot_ys = jnp.sum(density_of(halo_ys, (lev2 < d_ys[:, 0][None]).astype(jnp.float32)), axis=0)
    tot_yn = jnp.sum(density_of(halo_yn, (lev2 < d_yn[:, 0][None]).astype(jnp.float32)), axis=0)
    side = jnp.zeros((2, col_y), jnp.float32)
    side = side.at[0, :col_x].set(tot_ys).at[1, :col_x].set(tot_yn)
    pack = jnp.concatenate([tot_c, tot_xw[None], tot_xe[None], side], axis=0)
    shallower = jnp.zeros_like(pack)
    for hop in range(1, peers_z):
        pairs_z = [(i, i + hop) for i in range(peers_z - hop)]
        shallower = shallower + lax.ppermute(pack, "gz", pairs_z)
    s_c = shallower[:col_x]
    s_xw = shallower[col_x:col_x + 1]
    s_xe = shallower[col_x + 1:col_x + 2]
    s_ys = shallower[col_x + 2, :col_x][:, None]
    s_yn = shallower[col_x + 3, :col_x][:, None]
    face_row = start_y + jnp.arange(col_y, dtype=jnp.int32)
    wall_n = (face_row <= total_y - 2).astype(jnp.float32)
    wall_s = (face_row - 1 >= 0).astype(jnp.float32)
    coriolis = 0.5 + (face_row.astype(jnp.float32) + 0.5) / total_y
    lanes = jnp.stack([wall_n, wall_s, 0.3 * coriolis] + [jnp.zeros_like(wall_n)] * 5)
    wind_top = jnp.where(place_z == 0, wind, 0.0)
    y, y_ends = fused_solve(state, halo_xw, halo_xe, halo_ys[..., None], halo_yn[..., None],
                            d_c, d_e, d_w, d_n, d_s, d_xw, d_xe, d_ys, d_yn,
                            s_c, s_xw, s_xe, s_ys, s_yn, lanes, wind_top,
                            coupling, inv, ratio)
    y_all = gather_by_permutes(y_ends, "gz", place_z, peers_z)
    x_above, x_below = interface_values(y_all, uv_all, place_z, peers_z)
    pairs = u.shape[0]
    shape5 = (pairs, fields // pairs) + y.shape[1:]
    plane5 = (pairs, fields // pairs, 1, col_x, col_y)
    x = (y.reshape(shape5) + x_above.reshape(plane5) * u[:, None]
         + x_below.reshape(plane5) * v[:, None])
    return x.reshape(y.shape)


def solution(mesh):
    return jax.shard_map(
        per_device,
        mesh=mesh,
        in_specs=(P(None, "gz", "gx", "gy"), P(None, "gz", "gx", "gy"), P(), P(None, "gx", "gy")),
        out_specs=P(None, "gz", "gx", "gy"),
        check_vma=False,
    )
```

```python
import jax
import jax.numpy as jnp
from jax import lax
from jax.experimental import pallas as pl
from jax.experimental.pallas import tpu as pltpu
from jax.sharding import PartitionSpec as P


def padded_2(array, sides, width):
    for axis, dim in sides:
        peers, length = (lax.axis_size(axis), array.shape[dim])
        up = [(i, (i + 1) % peers) for i in range(peers)]
        down = [(j, i) for i, j in up]
        last = lax.slice_in_dim(array, length - width, length, axis=dim)
        initial = lax.slice_in_dim(array, 0, width, axis=dim)
        before = lax.ppermute(last, axis, up)
        after = lax.ppermute(initial, axis, down)
        array = jnp.concatenate([before, array, after], axis=dim)
    return array


def density_of(fields, wet_mask):
    return (-0.3 * fields[0] + 0.7 * fields[1] - 0.05 * fields[0] * fields[0]) * wet_mask


def advance(padded, wet_pad, pressure, wall_face, coriolis):
    wet_x = wet_pad[:, :-1, 1:-1] * wet_pad[:, 1:, 1:-1]
    wet_y = wet_pad[:, 1:-1, :-1] * wet_pad[:, 1:-1, 1:] * wall_face
    east_vel = 0.5 * (padded[2, :, :-1, 1:-1] + padded[2, :, 1:, 1:-1]) * wet_x
    north_vel = 0.5 * (padded[3, :, 1:-1, :-1] + padded[3, :, 1:-1, 1:]) * wet_y
    west_side = padded[:, :, :-1, 1:-1]
    east_side = padded[:, :, 1:, 1:-1]
    flux_x = 0.25 * (
        jnp.maximum(east_vel, 0.0) * west_side + jnp.minimum(east_vel, 0.0) * east_side
    ) - 0.08 * wet_x * (east_side - west_side)
    south_side = padded[:, :, 1:-1, :-1]
    north_side = padded[:, :, 1:-1, 1:]
    flux_y = 0.25 * (
        jnp.maximum(north_vel, 0.0) * south_side + jnp.minimum(north_vel, 0.0) * north_side
    ) - 0.08 * wet_y * (north_side - south_side)
    interior = padded[:, :, 1:-1, 1:-1]
    moved = interior - (
        flux_x[:, :, 1:] - flux_x[:, :, :-1] + flux_y[:, :, :, 1:] - flux_y[:, :, :, :-1]
    )
    centre = pressure[:, 1:-1, 1:-1]
    grad_x = 0.5 * (
        wet_x[:, 1:] * (pressure[:, 2:, 1:-1] - centre)
        + wet_x[:, :-1] * (centre - pressure[:, :-2, 1:-1])
    )
    grad_y = 0.5 * (
        wet_y[:, :, 1:] * (pressure[:, 1:-1, 2:] - centre)
        + wet_y[:, :, :-1] * (centre - pressure[:, 1:-1, :-2])
    )
    east_new = moved[2] + 0.3 * coriolis * interior[3] - grad_x
    north_new = moved[3] - 0.3 * coriolis * interior[2] - grad_y
    wet_inner = wet_pad[:, 1:-1, 1:-1]
    return jnp.stack([moved[0], moved[1], east_new, north_new]) * wet_inner


def coupling_kernel(c_ref, ctop_ref, ratio_ref, inv_ref, u_ref, v_ref, ends_ref):
    levels = c_ref.shape[1]
    ctop = ctop_ref[...]
    ratio_prev = None
    vu_prev = None
    for k in range(levels):
        above = ctop if k == 0 else c_ref[:, k - 1]
        below = c_ref[:, k]
        if k == 0:
            divisor = 1.0 + above + below
        else:
            divisor = 1.0 + above * (1.0 - ratio_prev) + below
        inv = 1.0 / divisor
        ratio = below * inv
        vu = ctop * inv if k == 0 else above * vu_prev * inv
        ratio_ref[:, k] = ratio
        inv_ref[:, k] = inv
        u_ref[:, k] = vu
        ratio_prev, vu_prev = ratio, vu
    u_later = vu_prev
    v_later = ratio_prev
    pairs = c_ref.shape[0]
    ends_ref[pairs:2 * pairs] = u_later
    ends_ref[3 * pairs:4 * pairs] = v_later
    v_ref[:, levels - 1] = v_later
    for k in range(levels - 2, -1, -1):
        ratio = ratio_ref[:, k]
        u_later = u_ref[:, k] + ratio * u_later
        v_later = ratio * v_later
        u_ref[:, k] = u_later
        v_ref[:, k] = v_later
    ends_ref[0:pairs] = u_later
    ends_ref[2 * pairs:3 * pairs] = v_later


def field_kernel(f_ref, c_ref, ctop_ref, ratio_ref, inv_ref, y_ref, ends_ref):
    levels = f_ref.shape[1]
    fields = f_ref.shape[0]
    vy = None
    for k in range(levels):
        inv = jnp.repeat(inv_ref[:, k], 2, axis=0)
        rhs = f_ref[:, k]
        if k == 0:
            vy = rhs * inv
        else:
            above = jnp.repeat(c_ref[:, k - 1], 2, axis=0)
            vy = (rhs + above * vy) * inv
        y_ref[:, k] = vy
    y_later = vy
    ends_ref[fields:2 * fields] = y_later
    for k in range(levels - 2, -1, -1):
        ratio = jnp.repeat(ratio_ref[:, k], 2, axis=0)
        y_later = y_ref[:, k] + ratio * y_later
        y_ref[:, k] = y_later
    ends_ref[0:fields] = y_later


def _specs(lead, levels, bx, cols_y):
    return pl.BlockSpec((lead, levels, bx, cols_y), lambda i: (0, 0, i, 0))


def _plane_spec(lead, bx, cols_y):
    return pl.BlockSpec((lead, bx, cols_y), lambda i: (0, i, 0))


def coupling_solve(coupling, ctop):
    pairs, levels, cols_x, cols_y = coupling.shape
    bx = 8 if cols_x % 8 == 0 else cols_x
    cspec = _specs(pairs, levels, bx, cols_y)
    full = jax.ShapeDtypeStruct(coupling.shape, jnp.float32)
    return pl.pallas_call(
        coupling_kernel,
        grid=(cols_x // bx,),
        in_specs=[cspec, _plane_spec(pairs, bx, cols_y)],
        out_specs=[cspec, cspec, cspec, cspec, _plane_spec(4 * pairs, bx, cols_y)],
        out_shape=[full, full, full, full,
                   jax.ShapeDtypeStruct((4 * pairs, cols_x, cols_y), jnp.float32)],
    )(coupling, ctop)


def field_solve(forced, coupling, ctop, ratio, inv):
    fields, levels, cols_x, cols_y = forced.shape
    pairs = coupling.shape[0]
    bx = 8 if cols_x % 8 == 0 else cols_x
    fspec = _specs(fields, levels, bx, cols_y)
    cspec = _specs(pairs, levels, bx, cols_y)
    return pl.pallas_call(
        field_kernel,
        grid=(cols_x // bx,),
        in_specs=[fspec, cspec, _plane_spec(pairs, bx, cols_y), cspec, cspec],
        out_specs=[fspec, _plane_spec(2 * fields, bx, cols_y)],
        out_shape=[jax.ShapeDtypeStruct(forced.shape, jnp.float32),
                   jax.ShapeDtypeStruct((2 * fields, cols_x, cols_y), jnp.float32)],
    )(forced, coupling, ctop, ratio, inv)


def interface_values(y_ends, uv_ends, place, peers):
    fields = 4
    y0 = y_ends[:, 0:fields]
    y1 = y_ends[:, fields:2 * fields]
    rest = jnp.repeat(uv_ends, 2, axis=1)
    u0 = rest[:, 0:4]
    u1 = rest[:, 4:8]
    v0 = rest[:, 8:12]
    v1 = rest[:, 12:16]
    pt, qt, pb, qb = [], [], [], []
    for q in range(peers):
        if q == 0:
            pt_q, qt_q = y0[q], v0[q]
            pb_q, qb_q = y1[q], v1[q]
        else:
            inv = 1.0 / (1.0 - u0[q] * qb[-1])
            pt_q = (y0[q] + u0[q] * pb[-1]) * inv
            qt_q = v0[q] * inv
            pb_q = y1[q] + u1[q] * (pb[-1] + qb[-1] * pt_q)
            qb_q = v1[q] + u1[q] * qb[-1] * qt_q
        pt.append(pt_q)
        qt.append(qt_q)
        pb.append(pb_q)
        qb.append(qb_q)
    tops = [None] * peers
    bots = [None] * peers
    t_next = jnp.zeros_like(pt[0])
    for q in range(peers - 1, -1, -1):
        tops[q] = pt[q] + qt[q] * t_next
        bots[q] = pb[q] + qb[q] * t_next
        t_next = tops[q]
    above = jnp.zeros_like(pt[0])
    below = jnp.zeros_like(pt[0])
    for q in range(peers):
        if q >= 1:
            above = jnp.where(place == q, bots[q - 1], above)
        if q <= peers - 2:
            below = jnp.where(place == q, tops[q + 1], below)
    return above, below


def gather_by_permutes(part, axis, place, peers):
    received = [part]
    for hop in range(1, peers):
        shift = [(i, (i + hop) % peers) for i in range(peers)]
        received.append(lax.ppermute(part, axis, shift))
    rows = []
    for q in range(peers):
        row = received[0]
        for hop in range(1, peers):
            row = jnp.where((place - hop) % peers == q, received[hop], row)
        rows.append(row)
    return jnp.stack(rows)


def _density(t, s, w):
    return (-0.3 * t + 0.7 * s - 0.05 * t * t) * w


def _flux(vel, lo, hi, w):
    return 0.25 * (jnp.maximum(vel, 0.0) * lo + jnp.minimum(vel, 0.0) * hi) - 0.08 * w * (hi - lo)


def fused_kernel(st_ref, xw_ref, xe_ref, ys_ref, yn_ref,
                 dc_ref, de_ref, dw_ref, dn_ref, ds_ref,
                 dxw_ref, dxe_ref, dys_ref, dyn_ref,
                 sc_ref, sxw_ref, sxe_ref, sys_ref, syn_ref,
                 lane_ref, wind_ref, c_ref, inv_ref, ratio_ref,
                 y_ref, ends_ref,
                 run_c_s, run_xw_s, run_xe_s, run_ys_s, run_yn_s, vy_s, cprev_s):
    fields, chunk, nx, ny = st_ref.shape
    levels = y_ref.shape[1]
    step_i = pl.program_id(0)
    row = lax.broadcasted_iota(jnp.int32, (nx, ny), 0)
    lane = lax.broadcasted_iota(jnp.int32, (nx, ny), 1)
    wall_n = lane_ref[0:1]
    wall_s = lane_ref[1:2]
    cor03 = lane_ref[2:3]
    d_c, d_e, d_w, d_n, d_s = dc_ref[...], de_ref[...], dw_ref[...], dn_ref[...], ds_ref[...]
    d_xw, d_xe, d_ys, d_yn = dxw_ref[...], dxe_ref[...], dys_ref[...], dyn_ref[...]

    @pl.when(step_i == 0)
    def _():
        run_c_s[...] = jnp.zeros_like(run_c_s)
        run_xw_s[...] = jnp.zeros_like(run_xw_s)
        run_xe_s[...] = jnp.zeros_like(run_xe_s)
        run_ys_s[...] = jnp.zeros_like(run_ys_s)
        run_yn_s[...] = jnp.zeros_like(run_yn_s)
        vy_s[...] = jnp.zeros_like(vy_s)
        cprev_s[...] = jnp.zeros_like(cprev_s)

    def east(r, h):
        return jnp.where(row == nx - 1, h, pltpu.roll(r, nx - 1, 0))

    def west(r, h):
        return jnp.where(row == 0, h, pltpu.roll(r, 1, 0))

    def north(r, h):
        return jnp.where(lane == ny - 1, h, pltpu.roll(r, ny - 1, 1))

    def south(r, h):
        return jnp.where(lane == 0, h, pltpu.roll(r, 1, 1))

    def level(kk, carry):
        run, vy_prev, c_prev = carry
        k = step_i * chunk + kk
        wc = (k < d_c).astype(jnp.float32)
        we = (k < d_e).astype(jnp.float32)
        ww = (k < d_w).astype(jnp.float32)
        wn = (k < d_n).astype(jnp.float32)
        ws = (k < d_s).astype(jnp.float32)
        wxw = (k < d_xw).astype(jnp.float32)
        wxe = (k < d_xe).astype(jnp.float32)
        wys = (k < d_ys).astype(jnp.float32)
        wyn = (k < d_yn).astype(jnp.float32)
        cen = [st_ref[f, kk] for f in range(fields)]
        hxw = [xw_ref[f, pl.ds(k, 1), :] for f in range(fields)]
        hxe = [xe_ref[f, pl.ds(k, 1), :] for f in range(fields)]
        hys = [ys_ref[f, kk] for f in range(fields)]
        hyn = [yn_ref[f, kk] for f in range(fields)]
        run_c, run_xw, run_xe, run_ys, run_yn = run
        den_c = _density(cen[0], cen[1], wc)
        den_xw = _density(hxw[0], hxw[1], wxw)
        den_xe = _density(hxe[0], hxe[1], wxe)
        den_ys = _density(hys[0], hys[1], wys)
        den_yn = _density(hyn[0], hyn[1], wyn)
        run_c = run_c + den_c
        run_xw = run_xw + den_xw
        run_xe = run_xe + den_xe
        run_ys = run_ys + den_ys
        run_yn = run_yn + den_yn
        p_c = 0.03 * (sc_ref[...] + run_c - 0.5 * den_c)
        p_xw = 0.03 * (sxw_ref[...] + run_xw - 0.5 * den_xw)
        p_xe = 0.03 * (sxe_ref[...] + run_xe - 0.5 * den_xe)
        p_ys = 0.03 * (sys_ref[...] + run_ys - 0.5 * den_ys)
        p_yn = 0.03 * (syn_ref[...] + run_yn - 0.5 * den_yn)
        p_e = east(p_c, p_xe)
        p_w = west(p_c, p_xw)
        p_n = north(p_c, p_yn)
        p_s = south(p_c, p_ys)
        face_e = wc * we
        face_w = ww * wc
        face_n = wc * wn * wall_n
        face_s = ws * wc * wall_s
        nbr_e = [east(cen[f], hxe[f]) for f in range(fields)]
        nbr_w = [west(cen[f], hxw[f]) for f in range(fields)]
        nbr_n = [north(cen[f], hyn[f]) for f in range(fields)]
        nbr_s = [south(cen[f], hys[f]) for f in range(fields)]
        vel_e = 0.5 * (cen[2] + nbr_e[2]) * face_e
        vel_w = 0.5 * (nbr_w[2] + cen[2]) * face_w
        vel_n = 0.5 * (cen[3] + nbr_n[3]) * face_n
        vel_s = 0.5 * (nbr_s[3] + cen[3]) * face_s
        moved = []
        for f in range(fields):
            fe = _flux(vel_e, cen[f], nbr_e[f], face_e)
            fw = _flux(vel_w, nbr_w[f], cen[f], face_w)
            fn = _flux(vel_n, cen[f], nbr_n[f], face_n)
            fs = _flux(vel_s, nbr_s[f], cen[f], face_s)
            moved.append(cen[f] - (fe - fw + fn - fs))
        grad_x = 0.5 * (face_e * (p_e - p_c) + face_w * (p_c - p_w))
        grad_y = 0.5 * (face_n * (p_n - p_c) + face_s * (p_c - p_s))
        east_new = moved[2] + cor03 * cen[3] - grad_x
        north_new = moved[3] - cor03 * cen[2] - grad_y
        top = (k == 0).astype(jnp.float32)
        forced = [moved[0] * wc, moved[1] * wc,
                  east_new * wc + wind_ref[0] * wc * top,
                  north_new * wc + wind_ref[1] * wc * top]
        vy = []
        for f in range(fields):
            m = f // 2
            val = (forced[f] + c_prev[m] * vy_prev[f]) * inv_ref[m, kk]
            y_ref[f, k] = val
            vy.append(val)
        c_here = jnp.stack([c_ref[0, kk], c_ref[1, kk]])
        return (run_c, run_xw, run_xe, run_ys, run_yn), jnp.stack(vy), c_here

    run = (run_c_s[...], run_xw_s[...], run_xe_s[...], run_ys_s[...], run_yn_s[...])
    carry = lax.fori_loop(0, chunk, level, (run, vy_s[...], cprev_s[...]), unroll=4)
    run, vy, c_prev = carry
    run_c_s[...], run_xw_s[...], run_xe_s[...], run_ys_s[...], run_yn_s[...] = run
    vy_s[...] = vy
    cprev_s[...] = c_prev

    @pl.when(step_i == pl.num_programs(0) - 1)
    def _():
        for f in range(fields):
            ends_ref[fields + f] = vy[f]

        def back(j, later):
            k = levels - 2 - j
            out = []
            for f in range(fields):
                val = y_ref[f, k] + ratio_ref[f // 2, k] * later[f]
                y_ref[f, k] = val
                out.append(val)
            return jnp.stack(out)

        later = lax.fori_loop(0, levels - 1, back, vy, unroll=2)
        for f in range(fields):
            ends_ref[f] = later[f]


def fused_solve(*operands):
    st = operands[0]
    fields, levels, nx, ny = st.shape
    pairs = operands[21].shape[0]
    chunk = 8 if levels % 8 == 0 else levels
    whole = [pl.BlockSpec(op.shape, (lambda i, n=op.ndim: (0,) * n)) for op in operands]
    by_level = lambda op: pl.BlockSpec((op.shape[0], chunk) + op.shape[2:], lambda i: (0, i, 0, 0))
    specs = list(whole)
    for idx in (0, 3, 4, 21, 22):
        specs[idx] = by_level(operands[idx])
    return pl.pallas_call(
        fused_kernel,
        grid=(levels // chunk,),
        in_specs=specs,
        out_specs=[pl.BlockSpec(st.shape, lambda i: (0, 0, 0, 0)),
                   pl.BlockSpec((2 * fields, nx, ny), lambda i: (0, 0, 0))],
        out_shape=[jax.ShapeDtypeStruct(st.shape, jnp.float32),
                   jax.ShapeDtypeStruct((2 * fields, nx, ny), jnp.float32)],
        scratch_shapes=[pltpu.VMEM((nx, ny), jnp.float32), pltpu.VMEM((1, ny), jnp.float32),
                        pltpu.VMEM((1, ny), jnp.float32), pltpu.VMEM((nx, 1), jnp.float32),
                        pltpu.VMEM((nx, 1), jnp.float32), pltpu.VMEM((fields, nx, ny), jnp.float32),
                        pltpu.VMEM((pairs, nx, ny), jnp.float32)],
        compiler_params=pltpu.CompilerParams(vmem_limit_bytes=60 * 1024 * 1024),
    )(*operands)


def per_device(state, mixing, depth_levels, wind):
    fields, lev_count, col_x, col_y = state.shape
    total_x, total_y = depth_levels.shape
    peers_z = lax.axis_size("gz")
    place_z = lax.axis_index("gz")
    peers_x = lax.axis_size("gx")
    peers_y = lax.axis_size("gy")
    start_x = lax.axis_index("gx") * col_x
    start_y = lax.axis_index("gy") * col_y
    start_z = place_z * lev_count
    down_z = [(i, i + 1) for i in range(peers_z - 1)]
    mix_above = lax.ppermute(mixing[:, lev_count - 1], "gz", down_z)
    up_x = [(i, (i + 1) % peers_x) for i in range(peers_x)]
    dn_x = [(j, i) for i, j in up_x]
    up_y = [(i, (i + 1) % peers_y) for i in range(peers_y)]
    dn_y = [(j, i) for i, j in up_y]
    halo_xw = lax.ppermute(state[:, :, col_x - 1], "gx", up_x)
    halo_xe = lax.ppermute(state[:, :, 0], "gx", dn_x)
    halo_ys = lax.ppermute(state[:, :, :, col_y - 1], "gy", up_y)
    halo_yn = lax.ppermute(state[:, :, :, 0], "gy", dn_y)
    levels = start_z + jnp.arange(lev_count, dtype=jnp.int32)
    row_index = (start_x - 1 + jnp.arange(col_x + 2, dtype=jnp.int32)) % total_x
    col_index = (start_y - 1 + jnp.arange(col_y + 2, dtype=jnp.int32)) % total_y
    depth_pad = jnp.take(jnp.take(depth_levels, row_index, axis=0), col_index, axis=1) - start_z
    d_c = depth_pad[1:-1, 1:-1]
    d_e = depth_pad[2:, 1:-1]
    d_w = depth_pad[:-2, 1:-1]
    d_n = depth_pad[1:-1, 2:]
    d_s = depth_pad[1:-1, :-2]
    d_xw = depth_pad[0:1, 1:-1]
    d_xe = depth_pad[col_x + 1:, 1:-1]
    d_ys = depth_pad[1:-1, 0:1]
    d_yn = depth_pad[1:-1, col_y + 1:]
    local = jnp.arange(lev_count, dtype=jnp.int32)
    wet_here = (local[:, None, None] < d_c[None]).astype(jnp.float32)
    wet_next = ((local + 1)[:, None, None] < d_c[None]).astype(jnp.float32)
    coupling = mixing * (wet_here * wet_next)[None]
    wet_up = (-1 < d_c).astype(jnp.float32)
    ctop = mix_above * (wet_up * wet_here[0])[None]
    ctop = jnp.where(place_z > 0, ctop, 0.0)
    ratio, inv, u, v, uv_ends = coupling_solve(coupling, ctop)
    uv_all = lax.all_gather(uv_ends, "gz")
    lev3 = local[:, None, None]
    tot_c = jnp.sum(density_of(state, (lev3 < d_c[None]).astype(jnp.float32)), axis=0)
    lev2 = local[:, None]
    tot_xw = jnp.sum(density_of(halo_xw, (lev2 < d_xw[0][None]).astype(jnp.float32)), axis=0)
    tot_xe = jnp.sum(density_of(halo_xe, (lev2 < d_xe[0][None]).astype(jnp.float32)), axis=0)
    tot_ys = jnp.sum(density_of(halo_ys, (lev2 < d_ys[:, 0][None]).astype(jnp.float32)), axis=0)
    tot_yn = jnp.sum(density_of(halo_yn, (lev2 < d_yn[:, 0][None]).astype(jnp.float32)), axis=0)
    side = jnp.zeros((2, col_y), jnp.float32)
    side = side.at[0, :col_x].set(tot_ys).at[1, :col_x].set(tot_yn)
    pack = jnp.concatenate([tot_c, tot_xw[None], tot_xe[None], side], axis=0)
    shallower = jnp.zeros_like(pack)
    for hop in range(1, peers_z):
        pairs_z = [(i, i + hop) for i in range(peers_z - hop)]
        shallower = shallower + lax.ppermute(pack, "gz", pairs_z)
    s_c = shallower[:col_x]
    s_xw = shallower[col_x:col_x + 1]
    s_xe = shallower[col_x + 1:col_x + 2]
    s_ys = shallower[col_x + 2, :col_x][:, None]
    s_yn = shallower[col_x + 3, :col_x][:, None]
    face_row = start_y + jnp.arange(col_y, dtype=jnp.int32)
    wall_n = (face_row <= total_y - 2).astype(jnp.float32)
    wall_s = (face_row - 1 >= 0).astype(jnp.float32)
    coriolis = 0.5 + (face_row.astype(jnp.float32) + 0.5) / total_y
    lanes = jnp.stack([wall_n, wall_s, 0.3 * coriolis] + [jnp.zeros_like(wall_n)] * 5)
    wind_top = jnp.where(place_z == 0, wind, 0.0)
    y, y_ends = fused_solve(state, halo_xw, halo_xe, halo_ys[..., None], halo_yn[..., None],
                            d_c, d_e, d_w, d_n, d_s, d_xw, d_xe, d_ys, d_yn,
                            s_c, s_xw, s_xe, s_ys, s_yn, lanes, wind_top,
                            coupling, inv, ratio)
    y_all = gather_by_permutes(y_ends, "gz", place_z, peers_z)
    x_above, x_below = interface_values(y_all, uv_all, place_z, peers_z)
    pairs = u.shape[0]
    shape5 = (pairs, fields // pairs) + y.shape[1:]
    plane5 = (pairs, fields // pairs, 1, col_x, col_y)
    x = (y.reshape(shape5) + x_above.reshape(plane5) * u[:, None]
         + x_below.reshape(plane5) * v[:, None])
    return x.reshape(y.shape)


def solution(mesh):
    return jax.shard_map(
        per_device,
        mesh=mesh,
        in_specs=(P(None, "gz", "gx", "gy"), P(None, "gz", "gx", "gy"), P(), P(None, "gx", "gy")),
        out_specs=P(None, "gz", "gx", "gy"),
        check_vma=False,
    )
```

```python
import jax
import jax.numpy as jnp
from jax import lax
from jax.experimental import pallas as pl
from jax.experimental.pallas import tpu as pltpu
from jax.sharding import PartitionSpec as P


def padded_2(array, sides, width):
    for axis, dim in sides:
        peers, length = (lax.axis_size(axis), array.shape[dim])
        up = [(i, (i + 1) % peers) for i in range(peers)]
        down = [(j, i) for i, j in up]
        last = lax.slice_in_dim(array, length - width, length, axis=dim)
        initial = lax.slice_in_dim(array, 0, width, axis=dim)
        before = lax.ppermute(last, axis, up)
        after = lax.ppermute(initial, axis, down)
        array = jnp.concatenate([before, array, after], axis=dim)
    return array


def density_of(fields, wet_mask):
    return (-0.3 * fields[0] + 0.7 * fields[1] - 0.05 * fields[0] * fields[0]) * wet_mask


def advance(padded, wet_pad, pressure, wall_face, coriolis):
    wet_x = wet_pad[:, :-1, 1:-1] * wet_pad[:, 1:, 1:-1]
    wet_y = wet_pad[:, 1:-1, :-1] * wet_pad[:, 1:-1, 1:] * wall_face
    east_vel = 0.5 * (padded[2, :, :-1, 1:-1] + padded[2, :, 1:, 1:-1]) * wet_x
    north_vel = 0.5 * (padded[3, :, 1:-1, :-1] + padded[3, :, 1:-1, 1:]) * wet_y
    west_side = padded[:, :, :-1, 1:-1]
    east_side = padded[:, :, 1:, 1:-1]
    flux_x = 0.25 * (
        jnp.maximum(east_vel, 0.0) * west_side + jnp.minimum(east_vel, 0.0) * east_side
    ) - 0.08 * wet_x * (east_side - west_side)
    south_side = padded[:, :, 1:-1, :-1]
    north_side = padded[:, :, 1:-1, 1:]
    flux_y = 0.25 * (
        jnp.maximum(north_vel, 0.0) * south_side + jnp.minimum(north_vel, 0.0) * north_side
    ) - 0.08 * wet_y * (north_side - south_side)
    interior = padded[:, :, 1:-1, 1:-1]
    moved = interior - (
        flux_x[:, :, 1:] - flux_x[:, :, :-1] + flux_y[:, :, :, 1:] - flux_y[:, :, :, :-1]
    )
    centre = pressure[:, 1:-1, 1:-1]
    grad_x = 0.5 * (
        wet_x[:, 1:] * (pressure[:, 2:, 1:-1] - centre)
        + wet_x[:, :-1] * (centre - pressure[:, :-2, 1:-1])
    )
    grad_y = 0.5 * (
        wet_y[:, :, 1:] * (pressure[:, 1:-1, 2:] - centre)
        + wet_y[:, :, :-1] * (centre - pressure[:, 1:-1, :-2])
    )
    east_new = moved[2] + 0.3 * coriolis * interior[3] - grad_x
    north_new = moved[3] - 0.3 * coriolis * interior[2] - grad_y
    wet_inner = wet_pad[:, 1:-1, 1:-1]
    return jnp.stack([moved[0], moved[1], east_new, north_new]) * wet_inner


def coupling_kernel(c_ref, ctop_ref, ratio_ref, inv_ref, u_ref, v_ref, ends_ref):
    levels = c_ref.shape[1]
    ctop = ctop_ref[...]
    ratio_prev = None
    vu_prev = None
    for k in range(levels):
        above = ctop if k == 0 else c_ref[:, k - 1]
        below = c_ref[:, k]
        if k == 0:
            divisor = 1.0 + above + below
        else:
            divisor = 1.0 + above * (1.0 - ratio_prev) + below
        inv = 1.0 / divisor
        ratio = below * inv
        vu = ctop * inv if k == 0 else above * vu_prev * inv
        ratio_ref[:, k] = ratio
        inv_ref[:, k] = inv
        u_ref[:, k] = vu
        ratio_prev, vu_prev = ratio, vu
    u_later = vu_prev
    v_later = ratio_prev
    pairs = c_ref.shape[0]
    ends_ref[pairs:2 * pairs] = u_later
    ends_ref[3 * pairs:4 * pairs] = v_later
    v_ref[:, levels - 1] = v_later
    for k in range(levels - 2, -1, -1):
        ratio = ratio_ref[:, k]
        u_later = u_ref[:, k] + ratio * u_later
        v_later = ratio * v_later
        u_ref[:, k] = u_later
        v_ref[:, k] = v_later
    ends_ref[0:pairs] = u_later
    ends_ref[2 * pairs:3 * pairs] = v_later


def field_kernel(f_ref, c_ref, ctop_ref, ratio_ref, inv_ref, y_ref, ends_ref):
    levels = f_ref.shape[1]
    fields = f_ref.shape[0]
    vy = None
    for k in range(levels):
        inv = jnp.repeat(inv_ref[:, k], 2, axis=0)
        rhs = f_ref[:, k]
        if k == 0:
            vy = rhs * inv
        else:
            above = jnp.repeat(c_ref[:, k - 1], 2, axis=0)
            vy = (rhs + above * vy) * inv
        y_ref[:, k] = vy
    y_later = vy
    ends_ref[fields:2 * fields] = y_later
    for k in range(levels - 2, -1, -1):
        ratio = jnp.repeat(ratio_ref[:, k], 2, axis=0)
        y_later = y_ref[:, k] + ratio * y_later
        y_ref[:, k] = y_later
    ends_ref[0:fields] = y_later


def _specs(lead, levels, bx, cols_y):
    return pl.BlockSpec((lead, levels, bx, cols_y), lambda i: (0, 0, i, 0))


def _plane_spec(lead, bx, cols_y):
    return pl.BlockSpec((lead, bx, cols_y), lambda i: (0, i, 0))


def coupling_solve(coupling, ctop):
    pairs, levels, cols_x, cols_y = coupling.shape
    bx = 16 if cols_x % 16 == 0 else cols_x
    cspec = _specs(pairs, levels, bx, cols_y)
    full = jax.ShapeDtypeStruct(coupling.shape, jnp.float32)
    return pl.pallas_call(
        coupling_kernel,
        grid=(cols_x // bx,),
        in_specs=[cspec, _plane_spec(pairs, bx, cols_y)],
        out_specs=[cspec, cspec, cspec, cspec, _plane_spec(4 * pairs, bx, cols_y)],
        out_shape=[full, full, full, full,
                   jax.ShapeDtypeStruct((4 * pairs, cols_x, cols_y), jnp.float32)],
    )(coupling, ctop)


def field_solve(forced, coupling, ctop, ratio, inv):
    fields, levels, cols_x, cols_y = forced.shape
    pairs = coupling.shape[0]
    bx = 8 if cols_x % 8 == 0 else cols_x
    fspec = _specs(fields, levels, bx, cols_y)
    cspec = _specs(pairs, levels, bx, cols_y)
    return pl.pallas_call(
        field_kernel,
        grid=(cols_x // bx,),
        in_specs=[fspec, cspec, _plane_spec(pairs, bx, cols_y), cspec, cspec],
        out_specs=[fspec, _plane_spec(2 * fields, bx, cols_y)],
        out_shape=[jax.ShapeDtypeStruct(forced.shape, jnp.float32),
                   jax.ShapeDtypeStruct((2 * fields, cols_x, cols_y), jnp.float32)],
    )(forced, coupling, ctop, ratio, inv)


def interface_values(y_ends, uv_ends, place, peers):
    fields = 4
    y0 = y_ends[:, 0:fields]
    y1 = y_ends[:, fields:2 * fields]
    rest = jnp.repeat(uv_ends, 2, axis=1)
    u0 = rest[:, 0:4]
    u1 = rest[:, 4:8]
    v0 = rest[:, 8:12]
    v1 = rest[:, 12:16]
    pt, qt, pb, qb = [], [], [], []
    for q in range(peers):
        if q == 0:
            pt_q, qt_q = y0[q], v0[q]
            pb_q, qb_q = y1[q], v1[q]
        else:
            inv = 1.0 / (1.0 - u0[q] * qb[-1])
            pt_q = (y0[q] + u0[q] * pb[-1]) * inv
            qt_q = v0[q] * inv
            pb_q = y1[q] + u1[q] * (pb[-1] + qb[-1] * pt_q)
            qb_q = v1[q] + u1[q] * qb[-1] * qt_q
        pt.append(pt_q)
        qt.append(qt_q)
        pb.append(pb_q)
        qb.append(qb_q)
    tops = [None] * peers
    bots = [None] * peers
    t_next = jnp.zeros_like(pt[0])
    for q in range(peers - 1, -1, -1):
        tops[q] = pt[q] + qt[q] * t_next
        bots[q] = pb[q] + qb[q] * t_next
        t_next = tops[q]
    above = jnp.zeros_like(pt[0])
    below = jnp.zeros_like(pt[0])
    for q in range(peers):
        if q >= 1:
            above = jnp.where(place == q, bots[q - 1], above)
        if q <= peers - 2:
            below = jnp.where(place == q, tops[q + 1], below)
    return above, below


def gather_by_permutes(part, axis, place, peers):
    received = [part]
    for hop in range(1, peers):
        shift = [(i, (i + hop) % peers) for i in range(peers)]
        received.append(lax.ppermute(part, axis, shift))
    rows = []
    for q in range(peers):
        row = received[0]
        for hop in range(1, peers):
            row = jnp.where((place - hop) % peers == q, received[hop], row)
        rows.append(row)
    return jnp.stack(rows)


def _density(t, s, w):
    return (-0.3 * t + 0.7 * s - 0.05 * t * t) * w


def _flux(vel, lo, hi, w):
    return 0.25 * (jnp.maximum(vel, 0.0) * lo + jnp.minimum(vel, 0.0) * hi) - 0.08 * w * (hi - lo)


def fused_kernel(st_ref, xw_ref, xe_ref, ys_ref, yn_ref,
                 dc_ref, de_ref, dw_ref, dn_ref, ds_ref,
                 dxw_ref, dxe_ref, dys_ref, dyn_ref,
                 sc_ref, sxw_ref, sxe_ref, sys_ref, syn_ref,
                 lane_ref, wind_ref, c_ref, inv_ref, ratio_ref,
                 y_ref, ends_ref,
                 run_c_s, run_xw_s, run_xe_s, run_ys_s, run_yn_s, vy_s, cprev_s):
    fields, chunk, nx, ny = st_ref.shape
    levels = y_ref.shape[1]
    step_i = pl.program_id(0)
    row = lax.broadcasted_iota(jnp.int32, (nx, ny), 0)
    lane = lax.broadcasted_iota(jnp.int32, (nx, ny), 1)
    wall_n = lane_ref[0:1]
    wall_s = lane_ref[1:2]
    cor03 = lane_ref[2:3]
    d_c, d_e, d_w, d_n, d_s = dc_ref[...], de_ref[...], dw_ref[...], dn_ref[...], ds_ref[...]
    d_xw, d_xe, d_ys, d_yn = dxw_ref[...], dxe_ref[...], dys_ref[...], dyn_ref[...]

    @pl.when(step_i == 0)
    def _():
        run_c_s[...] = jnp.zeros_like(run_c_s)
        run_xw_s[...] = jnp.zeros_like(run_xw_s)
        run_xe_s[...] = jnp.zeros_like(run_xe_s)
        run_ys_s[...] = jnp.zeros_like(run_ys_s)
        run_yn_s[...] = jnp.zeros_like(run_yn_s)
        vy_s[...] = jnp.zeros_like(vy_s)
        cprev_s[...] = jnp.zeros_like(cprev_s)

    def east(r, h):
        return jnp.where(row == nx - 1, h, pltpu.roll(r, nx - 1, 0))

    def west(r, h):
        return jnp.where(row == 0, h, pltpu.roll(r, 1, 0))

    def north(r, h):
        return jnp.where(lane == ny - 1, h, pltpu.roll(r, ny - 1, 1))

    def south(r, h):
        return jnp.where(lane == 0, h, pltpu.roll(r, 1, 1))

    def level(kk, carry):
        run, vy_prev, c_prev = carry
        k = step_i * chunk + kk
        wc = (k < d_c).astype(jnp.float32)
        we = (k < d_e).astype(jnp.float32)
        ww = (k < d_w).astype(jnp.float32)
        wn = (k < d_n).astype(jnp.float32)
        ws = (k < d_s).astype(jnp.float32)
        wxw = (k < d_xw).astype(jnp.float32)
        wxe = (k < d_xe).astype(jnp.float32)
        wys = (k < d_ys).astype(jnp.float32)
        wyn = (k < d_yn).astype(jnp.float32)
        cen = [st_ref[f, kk] for f in range(fields)]
        hxw = [xw_ref[f, pl.ds(k, 1), :] for f in range(fields)]
        hxe = [xe_ref[f, pl.ds(k, 1), :] for f in range(fields)]
        hys = [ys_ref[f, kk] for f in range(fields)]
        hyn = [yn_ref[f, kk] for f in range(fields)]
        run_c, run_xw, run_xe, run_ys, run_yn = run
        den_c = _density(cen[0], cen[1], wc)
        den_xw = _density(hxw[0], hxw[1], wxw)
        den_xe = _density(hxe[0], hxe[1], wxe)
        den_ys = _density(hys[0], hys[1], wys)
        den_yn = _density(hyn[0], hyn[1], wyn)
        run_c = run_c + den_c
        run_xw = run_xw + den_xw
        run_xe = run_xe + den_xe
        run_ys = run_ys + den_ys
        run_yn = run_yn + den_yn
        p_c = 0.03 * (sc_ref[...] + run_c - 0.5 * den_c)
        p_xw = 0.03 * (sxw_ref[...] + run_xw - 0.5 * den_xw)
        p_xe = 0.03 * (sxe_ref[...] + run_xe - 0.5 * den_xe)
        p_ys = 0.03 * (sys_ref[...] + run_ys - 0.5 * den_ys)
        p_yn = 0.03 * (syn_ref[...] + run_yn - 0.5 * den_yn)
        p_e = east(p_c, p_xe)
        p_w = west(p_c, p_xw)
        p_n = north(p_c, p_yn)
        p_s = south(p_c, p_ys)
        face_e = wc * we
        face_w = ww * wc
        face_n = wc * wn * wall_n
        face_s = ws * wc * wall_s
        nbr_e = [east(cen[f], hxe[f]) for f in range(fields)]
        nbr_w = [west(cen[f], hxw[f]) for f in range(fields)]
        nbr_n = [north(cen[f], hyn[f]) for f in range(fields)]
        nbr_s = [south(cen[f], hys[f]) for f in range(fields)]
        vel_e = 0.5 * (cen[2] + nbr_e[2]) * face_e
        vel_w = 0.5 * (nbr_w[2] + cen[2]) * face_w
        vel_n = 0.5 * (cen[3] + nbr_n[3]) * face_n
        vel_s = 0.5 * (nbr_s[3] + cen[3]) * face_s
        moved = []
        for f in range(fields):
            fe = _flux(vel_e, cen[f], nbr_e[f], face_e)
            fw = _flux(vel_w, nbr_w[f], cen[f], face_w)
            fn = _flux(vel_n, cen[f], nbr_n[f], face_n)
            fs = _flux(vel_s, nbr_s[f], cen[f], face_s)
            moved.append(cen[f] - (fe - fw + fn - fs))
        grad_x = 0.5 * (face_e * (p_e - p_c) + face_w * (p_c - p_w))
        grad_y = 0.5 * (face_n * (p_n - p_c) + face_s * (p_c - p_s))
        east_new = moved[2] + cor03 * cen[3] - grad_x
        north_new = moved[3] - cor03 * cen[2] - grad_y
        top = (k == 0).astype(jnp.float32)
        forced = [moved[0] * wc, moved[1] * wc,
                  east_new * wc + wind_ref[0] * wc * top,
                  north_new * wc + wind_ref[1] * wc * top]
        vy = []
        for f in range(fields):
            m = f // 2
            val = (forced[f] + c_prev[m] * vy_prev[f]) * inv_ref[m, kk]
            y_ref[f, k] = val
            vy.append(val)
        c_here = jnp.stack([c_ref[0, kk], c_ref[1, kk]])
        return (run_c, run_xw, run_xe, run_ys, run_yn), jnp.stack(vy), c_here

    run = (run_c_s[...], run_xw_s[...], run_xe_s[...], run_ys_s[...], run_yn_s[...])
    carry = lax.fori_loop(0, chunk, level, (run, vy_s[...], cprev_s[...]), unroll=4)
    run, vy, c_prev = carry
    run_c_s[...], run_xw_s[...], run_xe_s[...], run_ys_s[...], run_yn_s[...] = run
    vy_s[...] = vy
    cprev_s[...] = c_prev

    @pl.when(step_i == pl.num_programs(0) - 1)
    def _():
        for f in range(fields):
            ends_ref[fields + f] = vy[f]

        def back(j, later):
            k = levels - 2 - j
            out = []
            for f in range(fields):
                val = y_ref[f, k] + ratio_ref[f // 2, k] * later[f]
                y_ref[f, k] = val
                out.append(val)
            return jnp.stack(out)

        later = lax.fori_loop(0, levels - 1, back, vy, unroll=2)
        for f in range(fields):
            ends_ref[f] = later[f]


def fused_solve(*operands):
    st = operands[0]
    fields, levels, nx, ny = st.shape
    pairs = operands[21].shape[0]
    chunk = 8 if levels % 8 == 0 else levels
    whole = [pl.BlockSpec(op.shape, (lambda i, n=op.ndim: (0,) * n)) for op in operands]
    by_level = lambda op: pl.BlockSpec((op.shape[0], chunk) + op.shape[2:], lambda i: (0, i, 0, 0))
    specs = list(whole)
    for idx in (0, 3, 4, 21, 22):
        specs[idx] = by_level(operands[idx])
    return pl.pallas_call(
        fused_kernel,
        grid=(levels // chunk,),
        in_specs=specs,
        out_specs=[pl.BlockSpec(st.shape, lambda i: (0, 0, 0, 0)),
                   pl.BlockSpec((2 * fields, nx, ny), lambda i: (0, 0, 0))],
        out_shape=[jax.ShapeDtypeStruct(st.shape, jnp.float32),
                   jax.ShapeDtypeStruct((2 * fields, nx, ny), jnp.float32)],
        scratch_shapes=[pltpu.VMEM((nx, ny), jnp.float32), pltpu.VMEM((1, ny), jnp.float32),
                        pltpu.VMEM((1, ny), jnp.float32), pltpu.VMEM((nx, 1), jnp.float32),
                        pltpu.VMEM((nx, 1), jnp.float32), pltpu.VMEM((fields, nx, ny), jnp.float32),
                        pltpu.VMEM((pairs, nx, ny), jnp.float32)],
        compiler_params=pltpu.CompilerParams(vmem_limit_bytes=60 * 1024 * 1024),
    )(*operands)


def per_device(state, mixing, depth_levels, wind):
    fields, lev_count, col_x, col_y = state.shape
    total_x, total_y = depth_levels.shape
    peers_z = lax.axis_size("gz")
    place_z = lax.axis_index("gz")
    peers_x = lax.axis_size("gx")
    peers_y = lax.axis_size("gy")
    start_x = lax.axis_index("gx") * col_x
    start_y = lax.axis_index("gy") * col_y
    start_z = place_z * lev_count
    down_z = [(i, i + 1) for i in range(peers_z - 1)]
    mix_above = lax.ppermute(mixing[:, lev_count - 1], "gz", down_z)
    up_x = [(i, (i + 1) % peers_x) for i in range(peers_x)]
    dn_x = [(j, i) for i, j in up_x]
    up_y = [(i, (i + 1) % peers_y) for i in range(peers_y)]
    dn_y = [(j, i) for i, j in up_y]
    halo_xw = lax.ppermute(state[:, :, col_x - 1], "gx", up_x)
    halo_xe = lax.ppermute(state[:, :, 0], "gx", dn_x)
    halo_ys = lax.ppermute(state[:, :, :, col_y - 1], "gy", up_y)
    halo_yn = lax.ppermute(state[:, :, :, 0], "gy", dn_y)
    levels = start_z + jnp.arange(lev_count, dtype=jnp.int32)
    row_index = (start_x - 1 + jnp.arange(col_x + 2, dtype=jnp.int32)) % total_x
    col_index = (start_y - 1 + jnp.arange(col_y + 2, dtype=jnp.int32)) % total_y
    depth_pad = jnp.take(jnp.take(depth_levels, row_index, axis=0), col_index, axis=1) - start_z
    d_c = depth_pad[1:-1, 1:-1]
    d_e = depth_pad[2:, 1:-1]
    d_w = depth_pad[:-2, 1:-1]
    d_n = depth_pad[1:-1, 2:]
    d_s = depth_pad[1:-1, :-2]
    d_xw = depth_pad[0:1, 1:-1]
    d_xe = depth_pad[col_x + 1:, 1:-1]
    d_ys = depth_pad[1:-1, 0:1]
    d_yn = depth_pad[1:-1, col_y + 1:]
    local = jnp.arange(lev_count, dtype=jnp.int32)
    wet_here = (local[:, None, None] < d_c[None]).astype(jnp.float32)
    wet_next = ((local + 1)[:, None, None] < d_c[None]).astype(jnp.float32)
    coupling = mixing * (wet_here * wet_next)[None]
    wet_up = (-1 < d_c).astype(jnp.float32)
    ctop = mix_above * (wet_up * wet_here[0])[None]
    ctop = jnp.where(place_z > 0, ctop, 0.0)
    ratio, inv, u, v, uv_ends = coupling_solve(coupling, ctop)
    uv_all = lax.all_gather(uv_ends, "gz")
    lev3 = local[:, None, None]
    tot_c = jnp.sum(density_of(state, (lev3 < d_c[None]).astype(jnp.float32)), axis=0)
    lev2 = local[:, None]
    tot_xw = jnp.sum(density_of(halo_xw, (lev2 < d_xw[0][None]).astype(jnp.float32)), axis=0)
    tot_xe = jnp.sum(density_of(halo_xe, (lev2 < d_xe[0][None]).astype(jnp.float32)), axis=0)
    tot_ys = jnp.sum(density_of(halo_ys, (lev2 < d_ys[:, 0][None]).astype(jnp.float32)), axis=0)
    tot_yn = jnp.sum(density_of(halo_yn, (lev2 < d_yn[:, 0][None]).astype(jnp.float32)), axis=0)
    side = jnp.zeros((2, col_y), jnp.float32)
    side = side.at[0, :col_x].set(tot_ys).at[1, :col_x].set(tot_yn)
    pack = jnp.concatenate([tot_c, tot_xw[None], tot_xe[None], side], axis=0)
    shallower = jnp.zeros_like(pack)
    for hop in range(1, peers_z):
        pairs_z = [(i, i + hop) for i in range(peers_z - hop)]
        shallower = shallower + lax.ppermute(pack, "gz", pairs_z)
    s_c = shallower[:col_x]
    s_xw = shallower[col_x:col_x + 1]
    s_xe = shallower[col_x + 1:col_x + 2]
    s_ys = shallower[col_x + 2, :col_x][:, None]
    s_yn = shallower[col_x + 3, :col_x][:, None]
    face_row = start_y + jnp.arange(col_y, dtype=jnp.int32)
    wall_n = (face_row <= total_y - 2).astype(jnp.float32)
    wall_s = (face_row - 1 >= 0).astype(jnp.float32)
    coriolis = 0.5 + (face_row.astype(jnp.float32) + 0.5) / total_y
    lanes = jnp.stack([wall_n, wall_s, 0.3 * coriolis] + [jnp.zeros_like(wall_n)] * 5)
    wind_top = jnp.where(place_z == 0, wind, 0.0)
    y, y_ends = fused_solve(state, halo_xw, halo_xe, halo_ys[..., None], halo_yn[..., None],
                            d_c, d_e, d_w, d_n, d_s, d_xw, d_xe, d_ys, d_yn,
                            s_c, s_xw, s_xe, s_ys, s_yn, lanes, wind_top,
                            coupling, inv, ratio)
    y_all = gather_by_permutes(y_ends, "gz", place_z, peers_z)
    x_above, x_below = interface_values(y_all, uv_all, place_z, peers_z)
    pairs = u.shape[0]
    shape5 = (pairs, fields // pairs) + y.shape[1:]
    plane5 = (pairs, fields // pairs, 1, col_x, col_y)
    x = (y.reshape(shape5) + x_above.reshape(plane5) * u[:, None]
         + x_below.reshape(plane5) * v[:, None])
    return x.reshape(y.shape)


def solution(mesh):
    return jax.shard_map(
        per_device,
        mesh=mesh,
        in_specs=(P(None, "gz", "gx", "gy"), P(None, "gz", "gx", "gy"), P(), P(None, "gx", "gy")),
        out_specs=P(None, "gz", "gx", "gy"),
        check_vma=False,
    )
```

```python
import jax
import jax.numpy as jnp
from jax import lax
from jax.experimental import pallas as pl
from jax.experimental.pallas import tpu as pltpu
from jax.sharding import PartitionSpec as P


def padded_2(array, sides, width):
    for axis, dim in sides:
        peers, length = (lax.axis_size(axis), array.shape[dim])
        up = [(i, (i + 1) % peers) for i in range(peers)]
        down = [(j, i) for i, j in up]
        last = lax.slice_in_dim(array, length - width, length, axis=dim)
        initial = lax.slice_in_dim(array, 0, width, axis=dim)
        before = lax.ppermute(last, axis, up)
        after = lax.ppermute(initial, axis, down)
        array = jnp.concatenate([before, array, after], axis=dim)
    return array


def density_of(fields, wet_mask):
    return (-0.3 * fields[0] + 0.7 * fields[1] - 0.05 * fields[0] * fields[0]) * wet_mask


def advance(padded, wet_pad, pressure, wall_face, coriolis):
    wet_x = wet_pad[:, :-1, 1:-1] * wet_pad[:, 1:, 1:-1]
    wet_y = wet_pad[:, 1:-1, :-1] * wet_pad[:, 1:-1, 1:] * wall_face
    east_vel = 0.5 * (padded[2, :, :-1, 1:-1] + padded[2, :, 1:, 1:-1]) * wet_x
    north_vel = 0.5 * (padded[3, :, 1:-1, :-1] + padded[3, :, 1:-1, 1:]) * wet_y
    west_side = padded[:, :, :-1, 1:-1]
    east_side = padded[:, :, 1:, 1:-1]
    flux_x = 0.25 * (
        jnp.maximum(east_vel, 0.0) * west_side + jnp.minimum(east_vel, 0.0) * east_side
    ) - 0.08 * wet_x * (east_side - west_side)
    south_side = padded[:, :, 1:-1, :-1]
    north_side = padded[:, :, 1:-1, 1:]
    flux_y = 0.25 * (
        jnp.maximum(north_vel, 0.0) * south_side + jnp.minimum(north_vel, 0.0) * north_side
    ) - 0.08 * wet_y * (north_side - south_side)
    interior = padded[:, :, 1:-1, 1:-1]
    moved = interior - (
        flux_x[:, :, 1:] - flux_x[:, :, :-1] + flux_y[:, :, :, 1:] - flux_y[:, :, :, :-1]
    )
    centre = pressure[:, 1:-1, 1:-1]
    grad_x = 0.5 * (
        wet_x[:, 1:] * (pressure[:, 2:, 1:-1] - centre)
        + wet_x[:, :-1] * (centre - pressure[:, :-2, 1:-1])
    )
    grad_y = 0.5 * (
        wet_y[:, :, 1:] * (pressure[:, 1:-1, 2:] - centre)
        + wet_y[:, :, :-1] * (centre - pressure[:, 1:-1, :-2])
    )
    east_new = moved[2] + 0.3 * coriolis * interior[3] - grad_x
    north_new = moved[3] - 0.3 * coriolis * interior[2] - grad_y
    wet_inner = wet_pad[:, 1:-1, 1:-1]
    return jnp.stack([moved[0], moved[1], east_new, north_new]) * wet_inner


def coupling_kernel(c_ref, ctop_ref, ratio_ref, inv_ref, u_ref, v_ref, ends_ref):
    levels = c_ref.shape[1]
    ctop = ctop_ref[...]
    ratio_prev = None
    vu_prev = None
    for k in range(levels):
        above = ctop if k == 0 else c_ref[:, k - 1]
        below = c_ref[:, k]
        if k == 0:
            divisor = 1.0 + above + below
        else:
            divisor = 1.0 + above * (1.0 - ratio_prev) + below
        inv = 1.0 / divisor
        ratio = below * inv
        vu = ctop * inv if k == 0 else above * vu_prev * inv
        ratio_ref[:, k] = ratio
        inv_ref[:, k] = inv
        u_ref[:, k] = vu
        ratio_prev, vu_prev = ratio, vu
    u_later = vu_prev
    v_later = ratio_prev
    pairs = c_ref.shape[0]
    ends_ref[pairs:2 * pairs] = u_later
    ends_ref[3 * pairs:4 * pairs] = v_later
    v_ref[:, levels - 1] = v_later
    for k in range(levels - 2, -1, -1):
        ratio = ratio_ref[:, k]
        u_later = u_ref[:, k] + ratio * u_later
        v_later = ratio * v_later
        u_ref[:, k] = u_later
        v_ref[:, k] = v_later
    ends_ref[0:pairs] = u_later
    ends_ref[2 * pairs:3 * pairs] = v_later


def field_kernel(f_ref, c_ref, ctop_ref, ratio_ref, inv_ref, y_ref, ends_ref):
    levels = f_ref.shape[1]
    fields = f_ref.shape[0]
    vy = None
    for k in range(levels):
        inv = jnp.repeat(inv_ref[:, k], 2, axis=0)
        rhs = f_ref[:, k]
        if k == 0:
            vy = rhs * inv
        else:
            above = jnp.repeat(c_ref[:, k - 1], 2, axis=0)
            vy = (rhs + above * vy) * inv
        y_ref[:, k] = vy
    y_later = vy
    ends_ref[fields:2 * fields] = y_later
    for k in range(levels - 2, -1, -1):
        ratio = jnp.repeat(ratio_ref[:, k], 2, axis=0)
        y_later = y_ref[:, k] + ratio * y_later
        y_ref[:, k] = y_later
    ends_ref[0:fields] = y_later


def _specs(lead, levels, bx, cols_y):
    return pl.BlockSpec((lead, levels, bx, cols_y), lambda i: (0, 0, i, 0))


def _plane_spec(lead, bx, cols_y):
    return pl.BlockSpec((lead, bx, cols_y), lambda i: (0, i, 0))


def coupling_solve(coupling, ctop):
    pairs, levels, cols_x, cols_y = coupling.shape
    bx = 16 if cols_x % 16 == 0 else cols_x
    cspec = _specs(pairs, levels, bx, cols_y)
    full = jax.ShapeDtypeStruct(coupling.shape, jnp.float32)
    return pl.pallas_call(
        coupling_kernel,
        grid=(cols_x // bx,),
        in_specs=[cspec, _plane_spec(pairs, bx, cols_y)],
        out_specs=[cspec, cspec, cspec, cspec, _plane_spec(4 * pairs, bx, cols_y)],
        out_shape=[full, full, full, full,
                   jax.ShapeDtypeStruct((4 * pairs, cols_x, cols_y), jnp.float32)],
    )(coupling, ctop)


def field_solve(forced, coupling, ctop, ratio, inv):
    fields, levels, cols_x, cols_y = forced.shape
    pairs = coupling.shape[0]
    bx = 8 if cols_x % 8 == 0 else cols_x
    fspec = _specs(fields, levels, bx, cols_y)
    cspec = _specs(pairs, levels, bx, cols_y)
    return pl.pallas_call(
        field_kernel,
        grid=(cols_x // bx,),
        in_specs=[fspec, cspec, _plane_spec(pairs, bx, cols_y), cspec, cspec],
        out_specs=[fspec, _plane_spec(2 * fields, bx, cols_y)],
        out_shape=[jax.ShapeDtypeStruct(forced.shape, jnp.float32),
                   jax.ShapeDtypeStruct((2 * fields, cols_x, cols_y), jnp.float32)],
    )(forced, coupling, ctop, ratio, inv)


def interface_values(y_ends, uv_ends, place, peers):
    fields = 4
    y0 = y_ends[:, 0:fields]
    y1 = y_ends[:, fields:2 * fields]
    rest = jnp.repeat(uv_ends, 2, axis=1)
    u0 = rest[:, 0:4]
    u1 = rest[:, 4:8]
    v0 = rest[:, 8:12]
    v1 = rest[:, 12:16]
    pt, qt, pb, qb = [], [], [], []
    for q in range(peers):
        if q == 0:
            pt_q, qt_q = y0[q], v0[q]
            pb_q, qb_q = y1[q], v1[q]
        else:
            inv = 1.0 / (1.0 - u0[q] * qb[-1])
            pt_q = (y0[q] + u0[q] * pb[-1]) * inv
            qt_q = v0[q] * inv
            pb_q = y1[q] + u1[q] * (pb[-1] + qb[-1] * pt_q)
            qb_q = v1[q] + u1[q] * qb[-1] * qt_q
        pt.append(pt_q)
        qt.append(qt_q)
        pb.append(pb_q)
        qb.append(qb_q)
    tops = [None] * peers
    bots = [None] * peers
    t_next = jnp.zeros_like(pt[0])
    for q in range(peers - 1, -1, -1):
        tops[q] = pt[q] + qt[q] * t_next
        bots[q] = pb[q] + qb[q] * t_next
        t_next = tops[q]
    above = jnp.zeros_like(pt[0])
    below = jnp.zeros_like(pt[0])
    for q in range(peers):
        if q >= 1:
            above = jnp.where(place == q, bots[q - 1], above)
        if q <= peers - 2:
            below = jnp.where(place == q, tops[q + 1], below)
    return above, below


def gather_by_permutes(part, axis, place, peers):
    received = [part]
    for hop in range(1, peers):
        shift = [(i, (i + hop) % peers) for i in range(peers)]
        received.append(lax.ppermute(part, axis, shift))
    rows = []
    for q in range(peers):
        row = received[0]
        for hop in range(1, peers):
            row = jnp.where((place - hop) % peers == q, received[hop], row)
        rows.append(row)
    return jnp.stack(rows)


def _density(t, s, w):
    return (-0.3 * t + 0.7 * s - 0.05 * t * t) * w


def _flux(vel, lo, hi, w):
    return 0.25 * (jnp.maximum(vel, 0.0) * lo + jnp.minimum(vel, 0.0) * hi) - 0.08 * w * (hi - lo)


def fused_kernel(st_ref, xw_ref, xe_ref, ys_ref, yn_ref,
                 dc_ref, de_ref, dw_ref, dn_ref, ds_ref,
                 dxw_ref, dxe_ref, dys_ref, dyn_ref,
                 sc_ref, sxw_ref, sxe_ref, sys_ref, syn_ref,
                 lane_ref, wind_ref, c_ref, inv_ref, ratio_ref,
                 y_ref, ends_ref,
                 run_c_s, run_xw_s, run_xe_s, run_ys_s, run_yn_s, vy_s, cprev_s):
    fields, chunk, nx, ny = st_ref.shape
    levels = y_ref.shape[1]
    step_i = pl.program_id(0)
    row = lax.broadcasted_iota(jnp.int32, (nx, ny), 0)
    lane = lax.broadcasted_iota(jnp.int32, (nx, ny), 1)
    wall_n = lane_ref[0:1]
    wall_s = lane_ref[1:2]
    cor03 = lane_ref[2:3]
    d_c, d_e, d_w, d_n, d_s = dc_ref[...], de_ref[...], dw_ref[...], dn_ref[...], ds_ref[...]
    d_xw, d_xe, d_ys, d_yn = dxw_ref[...], dxe_ref[...], dys_ref[...], dyn_ref[...]

    @pl.when(step_i == 0)
    def _():
        run_c_s[...] = jnp.zeros_like(run_c_s)
        run_xw_s[...] = jnp.zeros_like(run_xw_s)
        run_xe_s[...] = jnp.zeros_like(run_xe_s)
        run_ys_s[...] = jnp.zeros_like(run_ys_s)
        run_yn_s[...] = jnp.zeros_like(run_yn_s)
        vy_s[...] = jnp.zeros_like(vy_s)
        cprev_s[...] = jnp.zeros_like(cprev_s)

    def east(r, h):
        return jnp.where(row == nx - 1, h, pltpu.roll(r, nx - 1, 0))

    def west(r, h):
        return jnp.where(row == 0, h, pltpu.roll(r, 1, 0))

    def north(r, h):
        return jnp.where(lane == ny - 1, h, pltpu.roll(r, ny - 1, 1))

    def south(r, h):
        return jnp.where(lane == 0, h, pltpu.roll(r, 1, 1))

    def level(kk, carry):
        run, vy_prev, c_prev = carry
        k = step_i * chunk + kk
        wc = (k < d_c).astype(jnp.float32)
        we = (k < d_e).astype(jnp.float32)
        ww = (k < d_w).astype(jnp.float32)
        wn = (k < d_n).astype(jnp.float32)
        ws = (k < d_s).astype(jnp.float32)
        wxw = (k < d_xw).astype(jnp.float32)
        wxe = (k < d_xe).astype(jnp.float32)
        wys = (k < d_ys).astype(jnp.float32)
        wyn = (k < d_yn).astype(jnp.float32)
        cen = [st_ref[f, kk] for f in range(fields)]
        hxw = [xw_ref[f, pl.ds(k, 1), :] for f in range(fields)]
        hxe = [xe_ref[f, pl.ds(k, 1), :] for f in range(fields)]
        hys = [ys_ref[f, kk] for f in range(fields)]
        hyn = [yn_ref[f, kk] for f in range(fields)]
        run_c, run_xw, run_xe, run_ys, run_yn = run
        den_c = _density(cen[0], cen[1], wc)
        den_xw = _density(hxw[0], hxw[1], wxw)
        den_xe = _density(hxe[0], hxe[1], wxe)
        den_ys = _density(hys[0], hys[1], wys)
        den_yn = _density(hyn[0], hyn[1], wyn)
        run_c = run_c + den_c
        run_xw = run_xw + den_xw
        run_xe = run_xe + den_xe
        run_ys = run_ys + den_ys
        run_yn = run_yn + den_yn
        p_c = 0.03 * (sc_ref[...] + run_c - 0.5 * den_c)
        p_xw = 0.03 * (sxw_ref[...] + run_xw - 0.5 * den_xw)
        p_xe = 0.03 * (sxe_ref[...] + run_xe - 0.5 * den_xe)
        p_ys = 0.03 * (sys_ref[...] + run_ys - 0.5 * den_ys)
        p_yn = 0.03 * (syn_ref[...] + run_yn - 0.5 * den_yn)
        p_e = east(p_c, p_xe)
        p_w = west(p_c, p_xw)
        p_n = north(p_c, p_yn)
        p_s = south(p_c, p_ys)
        face_e = wc * we
        face_w = ww * wc
        face_n = wc * wn * wall_n
        face_s = ws * wc * wall_s
        nbr_e = [east(cen[f], hxe[f]) for f in range(fields)]
        nbr_w = [west(cen[f], hxw[f]) for f in range(fields)]
        nbr_n = [north(cen[f], hyn[f]) for f in range(fields)]
        nbr_s = [south(cen[f], hys[f]) for f in range(fields)]
        vel_e = 0.5 * (cen[2] + nbr_e[2]) * face_e
        vel_w = 0.5 * (nbr_w[2] + cen[2]) * face_w
        vel_n = 0.5 * (cen[3] + nbr_n[3]) * face_n
        vel_s = 0.5 * (nbr_s[3] + cen[3]) * face_s
        moved = []
        for f in range(fields):
            fe = _flux(vel_e, cen[f], nbr_e[f], face_e)
            fw = _flux(vel_w, nbr_w[f], cen[f], face_w)
            fn = _flux(vel_n, cen[f], nbr_n[f], face_n)
            fs = _flux(vel_s, nbr_s[f], cen[f], face_s)
            moved.append(cen[f] - (fe - fw + fn - fs))
        grad_x = 0.5 * (face_e * (p_e - p_c) + face_w * (p_c - p_w))
        grad_y = 0.5 * (face_n * (p_n - p_c) + face_s * (p_c - p_s))
        east_new = moved[2] + cor03 * cen[3] - grad_x
        north_new = moved[3] - cor03 * cen[2] - grad_y
        top = (k == 0).astype(jnp.float32)
        forced = [moved[0] * wc, moved[1] * wc,
                  east_new * wc + wind_ref[0] * wc * top,
                  north_new * wc + wind_ref[1] * wc * top]
        vy = []
        for f in range(fields):
            m = f // 2
            val = (forced[f] + c_prev[m] * vy_prev[f]) * inv_ref[m, kk]
            y_ref[f, k] = val
            vy.append(val)
        c_here = jnp.stack([c_ref[0, kk], c_ref[1, kk]])
        return (run_c, run_xw, run_xe, run_ys, run_yn), jnp.stack(vy), c_here

    run = (run_c_s[...], run_xw_s[...], run_xe_s[...], run_ys_s[...], run_yn_s[...])
    carry = lax.fori_loop(0, chunk, level, (run, vy_s[...], cprev_s[...]), unroll=chunk)
    run, vy, c_prev = carry
    run_c_s[...], run_xw_s[...], run_xe_s[...], run_ys_s[...], run_yn_s[...] = run
    vy_s[...] = vy
    cprev_s[...] = c_prev

    @pl.when(step_i == pl.num_programs(0) - 1)
    def _():
        for f in range(fields):
            ends_ref[fields + f] = vy[f]

        def back(j, later):
            k = levels - 2 - j
            out = []
            for f in range(fields):
                val = y_ref[f, k] + ratio_ref[f // 2, k] * later[f]
                y_ref[f, k] = val
                out.append(val)
            return jnp.stack(out)

        later = lax.fori_loop(0, levels - 1, back, vy, unroll=2)
        for f in range(fields):
            ends_ref[f] = later[f]


def fused_solve(*operands):
    st = operands[0]
    fields, levels, nx, ny = st.shape
    pairs = operands[21].shape[0]
    chunk = 8 if levels % 8 == 0 else levels
    whole = [pl.BlockSpec(op.shape, (lambda i, n=op.ndim: (0,) * n)) for op in operands]
    by_level = lambda op: pl.BlockSpec((op.shape[0], chunk) + op.shape[2:], lambda i: (0, i, 0, 0))
    specs = list(whole)
    for idx in (0, 3, 4, 21, 22):
        specs[idx] = by_level(operands[idx])
    return pl.pallas_call(
        fused_kernel,
        grid=(levels // chunk,),
        in_specs=specs,
        out_specs=[pl.BlockSpec(st.shape, lambda i: (0, 0, 0, 0)),
                   pl.BlockSpec((2 * fields, nx, ny), lambda i: (0, 0, 0))],
        out_shape=[jax.ShapeDtypeStruct(st.shape, jnp.float32),
                   jax.ShapeDtypeStruct((2 * fields, nx, ny), jnp.float32)],
        scratch_shapes=[pltpu.VMEM((nx, ny), jnp.float32), pltpu.VMEM((1, ny), jnp.float32),
                        pltpu.VMEM((1, ny), jnp.float32), pltpu.VMEM((nx, 1), jnp.float32),
                        pltpu.VMEM((nx, 1), jnp.float32), pltpu.VMEM((fields, nx, ny), jnp.float32),
                        pltpu.VMEM((pairs, nx, ny), jnp.float32)],
        compiler_params=pltpu.CompilerParams(vmem_limit_bytes=60 * 1024 * 1024),
    )(*operands)


def per_device(state, mixing, depth_levels, wind):
    fields, lev_count, col_x, col_y = state.shape
    total_x, total_y = depth_levels.shape
    peers_z = lax.axis_size("gz")
    place_z = lax.axis_index("gz")
    peers_x = lax.axis_size("gx")
    peers_y = lax.axis_size("gy")
    start_x = lax.axis_index("gx") * col_x
    start_y = lax.axis_index("gy") * col_y
    start_z = place_z * lev_count
    down_z = [(i, i + 1) for i in range(peers_z - 1)]
    mix_above = lax.ppermute(mixing[:, lev_count - 1], "gz", down_z)
    up_x = [(i, (i + 1) % peers_x) for i in range(peers_x)]
    dn_x = [(j, i) for i, j in up_x]
    up_y = [(i, (i + 1) % peers_y) for i in range(peers_y)]
    dn_y = [(j, i) for i, j in up_y]
    halo_xw = lax.ppermute(state[:, :, col_x - 1], "gx", up_x)
    halo_xe = lax.ppermute(state[:, :, 0], "gx", dn_x)
    halo_ys = lax.ppermute(state[:, :, :, col_y - 1], "gy", up_y)
    halo_yn = lax.ppermute(state[:, :, :, 0], "gy", dn_y)
    levels = start_z + jnp.arange(lev_count, dtype=jnp.int32)
    row_index = (start_x - 1 + jnp.arange(col_x + 2, dtype=jnp.int32)) % total_x
    col_index = (start_y - 1 + jnp.arange(col_y + 2, dtype=jnp.int32)) % total_y
    depth_pad = jnp.take(jnp.take(depth_levels, row_index, axis=0), col_index, axis=1) - start_z
    d_c = depth_pad[1:-1, 1:-1]
    d_e = depth_pad[2:, 1:-1]
    d_w = depth_pad[:-2, 1:-1]
    d_n = depth_pad[1:-1, 2:]
    d_s = depth_pad[1:-1, :-2]
    d_xw = depth_pad[0:1, 1:-1]
    d_xe = depth_pad[col_x + 1:, 1:-1]
    d_ys = depth_pad[1:-1, 0:1]
    d_yn = depth_pad[1:-1, col_y + 1:]
    local = jnp.arange(lev_count, dtype=jnp.int32)
    wet_here = (local[:, None, None] < d_c[None]).astype(jnp.float32)
    wet_next = ((local + 1)[:, None, None] < d_c[None]).astype(jnp.float32)
    coupling = mixing * (wet_here * wet_next)[None]
    wet_up = (-1 < d_c).astype(jnp.float32)
    ctop = mix_above * (wet_up * wet_here[0])[None]
    ctop = jnp.where(place_z > 0, ctop, 0.0)
    ratio, inv, u, v, uv_ends = coupling_solve(coupling, ctop)
    uv_all = lax.all_gather(uv_ends, "gz")
    lev3 = local[:, None, None]
    tot_c = jnp.sum(density_of(state, (lev3 < d_c[None]).astype(jnp.float32)), axis=0)
    lev2 = local[:, None]
    tot_xw = jnp.sum(density_of(halo_xw, (lev2 < d_xw[0][None]).astype(jnp.float32)), axis=0)
    tot_xe = jnp.sum(density_of(halo_xe, (lev2 < d_xe[0][None]).astype(jnp.float32)), axis=0)
    tot_ys = jnp.sum(density_of(halo_ys, (lev2 < d_ys[:, 0][None]).astype(jnp.float32)), axis=0)
    tot_yn = jnp.sum(density_of(halo_yn, (lev2 < d_yn[:, 0][None]).astype(jnp.float32)), axis=0)
    side = jnp.zeros((2, col_y), jnp.float32)
    side = side.at[0, :col_x].set(tot_ys).at[1, :col_x].set(tot_yn)
    pack = jnp.concatenate([tot_c, tot_xw[None], tot_xe[None], side], axis=0)
    shallower = jnp.zeros_like(pack)
    for hop in range(1, peers_z):
        pairs_z = [(i, i + hop) for i in range(peers_z - hop)]
        shallower = shallower + lax.ppermute(pack, "gz", pairs_z)
    s_c = shallower[:col_x]
    s_xw = shallower[col_x:col_x + 1]
    s_xe = shallower[col_x + 1:col_x + 2]
    s_ys = shallower[col_x + 2, :col_x][:, None]
    s_yn = shallower[col_x + 3, :col_x][:, None]
    face_row = start_y + jnp.arange(col_y, dtype=jnp.int32)
    wall_n = (face_row <= total_y - 2).astype(jnp.float32)
    wall_s = (face_row - 1 >= 0).astype(jnp.float32)
    coriolis = 0.5 + (face_row.astype(jnp.float32) + 0.5) / total_y
    lanes = jnp.stack([wall_n, wall_s, 0.3 * coriolis] + [jnp.zeros_like(wall_n)] * 5)
    wind_top = jnp.where(place_z == 0, wind, 0.0)
    y, y_ends = fused_solve(state, halo_xw, halo_xe, halo_ys[..., None], halo_yn[..., None],
                            d_c, d_e, d_w, d_n, d_s, d_xw, d_xe, d_ys, d_yn,
                            s_c, s_xw, s_xe, s_ys, s_yn, lanes, wind_top,
                            coupling, inv, ratio)
    y_all = gather_by_permutes(y_ends, "gz", place_z, peers_z)
    x_above, x_below = interface_values(y_all, uv_all, place_z, peers_z)
    pairs = u.shape[0]
    shape5 = (pairs, fields // pairs) + y.shape[1:]
    plane5 = (pairs, fields // pairs, 1, col_x, col_y)
    x = (y.reshape(shape5) + x_above.reshape(plane5) * u[:, None]
         + x_below.reshape(plane5) * v[:, None])
    return x.reshape(y.shape)


def solution(mesh):
    return jax.shard_map(
        per_device,
        mesh=mesh,
        in_specs=(P(None, "gz", "gx", "gy"), P(None, "gz", "gx", "gy"), P(), P(None, "gx", "gy")),
        out_specs=P(None, "gz", "gx", "gy"),
        check_vma=False,
    )
```

```python
import jax
import jax.numpy as jnp
from jax import lax
from jax.experimental import pallas as pl
from jax.experimental.pallas import tpu as pltpu
from jax.sharding import PartitionSpec as P


def padded_2(array, sides, width):
    for axis, dim in sides:
        peers, length = (lax.axis_size(axis), array.shape[dim])
        up = [(i, (i + 1) % peers) for i in range(peers)]
        down = [(j, i) for i, j in up]
        last = lax.slice_in_dim(array, length - width, length, axis=dim)
        initial = lax.slice_in_dim(array, 0, width, axis=dim)
        before = lax.ppermute(last, axis, up)
        after = lax.ppermute(initial, axis, down)
        array = jnp.concatenate([before, array, after], axis=dim)
    return array


def density_of(fields, wet_mask):
    return (-0.3 * fields[0] + 0.7 * fields[1] - 0.05 * fields[0] * fields[0]) * wet_mask


def advance(padded, wet_pad, pressure, wall_face, coriolis):
    wet_x = wet_pad[:, :-1, 1:-1] * wet_pad[:, 1:, 1:-1]
    wet_y = wet_pad[:, 1:-1, :-1] * wet_pad[:, 1:-1, 1:] * wall_face
    east_vel = 0.5 * (padded[2, :, :-1, 1:-1] + padded[2, :, 1:, 1:-1]) * wet_x
    north_vel = 0.5 * (padded[3, :, 1:-1, :-1] + padded[3, :, 1:-1, 1:]) * wet_y
    west_side = padded[:, :, :-1, 1:-1]
    east_side = padded[:, :, 1:, 1:-1]
    flux_x = 0.25 * (
        jnp.maximum(east_vel, 0.0) * west_side + jnp.minimum(east_vel, 0.0) * east_side
    ) - 0.08 * wet_x * (east_side - west_side)
    south_side = padded[:, :, 1:-1, :-1]
    north_side = padded[:, :, 1:-1, 1:]
    flux_y = 0.25 * (
        jnp.maximum(north_vel, 0.0) * south_side + jnp.minimum(north_vel, 0.0) * north_side
    ) - 0.08 * wet_y * (north_side - south_side)
    interior = padded[:, :, 1:-1, 1:-1]
    moved = interior - (
        flux_x[:, :, 1:] - flux_x[:, :, :-1] + flux_y[:, :, :, 1:] - flux_y[:, :, :, :-1]
    )
    centre = pressure[:, 1:-1, 1:-1]
    grad_x = 0.5 * (
        wet_x[:, 1:] * (pressure[:, 2:, 1:-1] - centre)
        + wet_x[:, :-1] * (centre - pressure[:, :-2, 1:-1])
    )
    grad_y = 0.5 * (
        wet_y[:, :, 1:] * (pressure[:, 1:-1, 2:] - centre)
        + wet_y[:, :, :-1] * (centre - pressure[:, 1:-1, :-2])
    )
    east_new = moved[2] + 0.3 * coriolis * interior[3] - grad_x
    north_new = moved[3] - 0.3 * coriolis * interior[2] - grad_y
    wet_inner = wet_pad[:, 1:-1, 1:-1]
    return jnp.stack([moved[0], moved[1], east_new, north_new]) * wet_inner


def coupling_kernel(c_ref, ctop_ref, ratio_ref, inv_ref, u_ref, v_ref, ends_ref):
    levels = c_ref.shape[1]
    ctop = ctop_ref[...]
    ratio_prev = None
    vu_prev = None
    for k in range(levels):
        above = ctop if k == 0 else c_ref[:, k - 1]
        below = c_ref[:, k]
        if k == 0:
            divisor = 1.0 + above + below
        else:
            divisor = 1.0 + above * (1.0 - ratio_prev) + below
        inv = 1.0 / divisor
        ratio = below * inv
        vu = ctop * inv if k == 0 else above * vu_prev * inv
        ratio_ref[:, k] = ratio
        inv_ref[:, k] = inv
        u_ref[:, k] = vu
        ratio_prev, vu_prev = ratio, vu
    u_later = vu_prev
    v_later = ratio_prev
    pairs = c_ref.shape[0]
    ends_ref[pairs:2 * pairs] = u_later
    ends_ref[3 * pairs:4 * pairs] = v_later
    v_ref[:, levels - 1] = v_later
    for k in range(levels - 2, -1, -1):
        ratio = ratio_ref[:, k]
        u_later = u_ref[:, k] + ratio * u_later
        v_later = ratio * v_later
        u_ref[:, k] = u_later
        v_ref[:, k] = v_later
    ends_ref[0:pairs] = u_later
    ends_ref[2 * pairs:3 * pairs] = v_later


def field_kernel(f_ref, c_ref, ctop_ref, ratio_ref, inv_ref, y_ref, ends_ref):
    levels = f_ref.shape[1]
    fields = f_ref.shape[0]
    vy = None
    for k in range(levels):
        inv = jnp.repeat(inv_ref[:, k], 2, axis=0)
        rhs = f_ref[:, k]
        if k == 0:
            vy = rhs * inv
        else:
            above = jnp.repeat(c_ref[:, k - 1], 2, axis=0)
            vy = (rhs + above * vy) * inv
        y_ref[:, k] = vy
    y_later = vy
    ends_ref[fields:2 * fields] = y_later
    for k in range(levels - 2, -1, -1):
        ratio = jnp.repeat(ratio_ref[:, k], 2, axis=0)
        y_later = y_ref[:, k] + ratio * y_later
        y_ref[:, k] = y_later
    ends_ref[0:fields] = y_later


def _specs(lead, levels, bx, cols_y):
    return pl.BlockSpec((lead, levels, bx, cols_y), lambda i: (0, 0, i, 0))


def _plane_spec(lead, bx, cols_y):
    return pl.BlockSpec((lead, bx, cols_y), lambda i: (0, i, 0))


def coupling_solve(coupling, ctop):
    pairs, levels, cols_x, cols_y = coupling.shape
    bx = 16 if cols_x % 16 == 0 else cols_x
    cspec = _specs(pairs, levels, bx, cols_y)
    full = jax.ShapeDtypeStruct(coupling.shape, jnp.float32)
    return pl.pallas_call(
        coupling_kernel,
        grid=(cols_x // bx,),
        in_specs=[cspec, _plane_spec(pairs, bx, cols_y)],
        out_specs=[cspec, cspec, cspec, cspec, _plane_spec(4 * pairs, bx, cols_y)],
        out_shape=[full, full, full, full,
                   jax.ShapeDtypeStruct((4 * pairs, cols_x, cols_y), jnp.float32)],
    )(coupling, ctop)


def field_solve(forced, coupling, ctop, ratio, inv):
    fields, levels, cols_x, cols_y = forced.shape
    pairs = coupling.shape[0]
    bx = 8 if cols_x % 8 == 0 else cols_x
    fspec = _specs(fields, levels, bx, cols_y)
    cspec = _specs(pairs, levels, bx, cols_y)
    return pl.pallas_call(
        field_kernel,
        grid=(cols_x // bx,),
        in_specs=[fspec, cspec, _plane_spec(pairs, bx, cols_y), cspec, cspec],
        out_specs=[fspec, _plane_spec(2 * fields, bx, cols_y)],
        out_shape=[jax.ShapeDtypeStruct(forced.shape, jnp.float32),
                   jax.ShapeDtypeStruct((2 * fields, cols_x, cols_y), jnp.float32)],
    )(forced, coupling, ctop, ratio, inv)


def interface_values(y_ends, uv_ends, place, peers):
    fields = 4
    y0 = y_ends[:, 0:fields]
    y1 = y_ends[:, fields:2 * fields]
    rest = jnp.repeat(uv_ends, 2, axis=1)
    u0 = rest[:, 0:4]
    u1 = rest[:, 4:8]
    v0 = rest[:, 8:12]
    v1 = rest[:, 12:16]
    pt, qt, pb, qb = [], [], [], []
    for q in range(peers):
        if q == 0:
            pt_q, qt_q = y0[q], v0[q]
            pb_q, qb_q = y1[q], v1[q]
        else:
            inv = 1.0 / (1.0 - u0[q] * qb[-1])
            pt_q = (y0[q] + u0[q] * pb[-1]) * inv
            qt_q = v0[q] * inv
            pb_q = y1[q] + u1[q] * (pb[-1] + qb[-1] * pt_q)
            qb_q = v1[q] + u1[q] * qb[-1] * qt_q
        pt.append(pt_q)
        qt.append(qt_q)
        pb.append(pb_q)
        qb.append(qb_q)
    tops = [None] * peers
    bots = [None] * peers
    t_next = jnp.zeros_like(pt[0])
    for q in range(peers - 1, -1, -1):
        tops[q] = pt[q] + qt[q] * t_next
        bots[q] = pb[q] + qb[q] * t_next
        t_next = tops[q]
    above = jnp.zeros_like(pt[0])
    below = jnp.zeros_like(pt[0])
    for q in range(peers):
        if q >= 1:
            above = jnp.where(place == q, bots[q - 1], above)
        if q <= peers - 2:
            below = jnp.where(place == q, tops[q + 1], below)
    return above, below


def gather_by_permutes(part, axis, place, peers):
    received = [part]
    for hop in range(1, peers):
        shift = [(i, (i + hop) % peers) for i in range(peers)]
        received.append(lax.ppermute(part, axis, shift))
    rows = []
    for q in range(peers):
        row = received[0]
        for hop in range(1, peers):
            row = jnp.where((place - hop) % peers == q, received[hop], row)
        rows.append(row)
    return jnp.stack(rows)


def _density(t, s, w):
    return (-0.3 * t + 0.7 * s - 0.05 * t * t) * w


def _flux(vel, lo, hi, w):
    return 0.25 * (jnp.maximum(vel, 0.0) * lo + jnp.minimum(vel, 0.0) * hi) - 0.08 * w * (hi - lo)


def fused_kernel(st_ref, xw_ref, xe_ref, ys_ref, yn_ref,
                 dc_ref, de_ref, dw_ref, dn_ref, ds_ref,
                 dxw_ref, dxe_ref, dys_ref, dyn_ref,
                 sc_ref, sxw_ref, sxe_ref, sys_ref, syn_ref,
                 lane_ref, wind_ref, c_ref, inv_ref, ratio_ref,
                 y_ref, ends_ref,
                 run_c_s, run_xw_s, run_xe_s, run_ys_s, run_yn_s, vy_s, cprev_s):
    fields, chunk, nx, ny = st_ref.shape
    levels = y_ref.shape[1]
    step_i = pl.program_id(0)
    row = lax.broadcasted_iota(jnp.int32, (nx, ny), 0)
    lane = lax.broadcasted_iota(jnp.int32, (nx, ny), 1)
    wall_n = lane_ref[0:1]
    wall_s = lane_ref[1:2]
    cor03 = lane_ref[2:3]
    d_c, d_e, d_w, d_n, d_s = dc_ref[...], de_ref[...], dw_ref[...], dn_ref[...], ds_ref[...]
    d_xw, d_xe, d_ys, d_yn = dxw_ref[...], dxe_ref[...], dys_ref[...], dyn_ref[...]

    @pl.when(step_i == 0)
    def _():
        run_c_s[...] = jnp.zeros_like(run_c_s)
        run_xw_s[...] = jnp.zeros_like(run_xw_s)
        run_xe_s[...] = jnp.zeros_like(run_xe_s)
        run_ys_s[...] = jnp.zeros_like(run_ys_s)
        run_yn_s[...] = jnp.zeros_like(run_yn_s)
        vy_s[...] = jnp.zeros_like(vy_s)
        cprev_s[...] = jnp.zeros_like(cprev_s)

    def east(r, h):
        return jnp.where(row == nx - 1, h, pltpu.roll(r, nx - 1, 0))

    def west(r, h):
        return jnp.where(row == 0, h, pltpu.roll(r, 1, 0))

    def north(r, h):
        return jnp.where(lane == ny - 1, h, pltpu.roll(r, ny - 1, 1))

    def south(r, h):
        return jnp.where(lane == 0, h, pltpu.roll(r, 1, 1))

    def level(kk, carry):
        run, vy_prev, c_prev = carry
        k = step_i * chunk + kk
        wc = (k < d_c).astype(jnp.float32)
        we = (k < d_e).astype(jnp.float32)
        ww = (k < d_w).astype(jnp.float32)
        wn = (k < d_n).astype(jnp.float32)
        ws = (k < d_s).astype(jnp.float32)
        wxw = (k < d_xw).astype(jnp.float32)
        wxe = (k < d_xe).astype(jnp.float32)
        wys = (k < d_ys).astype(jnp.float32)
        wyn = (k < d_yn).astype(jnp.float32)
        cen = [st_ref[f, kk] for f in range(fields)]
        hxw = [xw_ref[f, pl.ds(k, 1), :] for f in range(fields)]
        hxe = [xe_ref[f, pl.ds(k, 1), :] for f in range(fields)]
        hys = [ys_ref[f, kk] for f in range(fields)]
        hyn = [yn_ref[f, kk] for f in range(fields)]
        run_c, run_xw, run_xe, run_ys, run_yn = run
        den_c = _density(cen[0], cen[1], wc)
        den_xw = _density(hxw[0], hxw[1], wxw)
        den_xe = _density(hxe[0], hxe[1], wxe)
        den_ys = _density(hys[0], hys[1], wys)
        den_yn = _density(hyn[0], hyn[1], wyn)
        run_c = run_c + den_c
        run_xw = run_xw + den_xw
        run_xe = run_xe + den_xe
        run_ys = run_ys + den_ys
        run_yn = run_yn + den_yn
        p_c = 0.03 * (sc_ref[...] + run_c - 0.5 * den_c)
        p_xw = 0.03 * (sxw_ref[...] + run_xw - 0.5 * den_xw)
        p_xe = 0.03 * (sxe_ref[...] + run_xe - 0.5 * den_xe)
        p_ys = 0.03 * (sys_ref[...] + run_ys - 0.5 * den_ys)
        p_yn = 0.03 * (syn_ref[...] + run_yn - 0.5 * den_yn)
        p_e = east(p_c, p_xe)
        p_w = west(p_c, p_xw)
        p_n = north(p_c, p_yn)
        p_s = south(p_c, p_ys)
        face_e = wc * we
        face_w = ww * wc
        face_n = wc * wn * wall_n
        face_s = ws * wc * wall_s
        nbr_e = [east(cen[f], hxe[f]) for f in range(fields)]
        nbr_w = [west(cen[f], hxw[f]) for f in range(fields)]
        nbr_n = [north(cen[f], hyn[f]) for f in range(fields)]
        nbr_s = [south(cen[f], hys[f]) for f in range(fields)]
        vel_e = 0.5 * (cen[2] + nbr_e[2]) * face_e
        vel_w = 0.5 * (nbr_w[2] + cen[2]) * face_w
        vel_n = 0.5 * (cen[3] + nbr_n[3]) * face_n
        vel_s = 0.5 * (nbr_s[3] + cen[3]) * face_s
        moved = []
        for f in range(fields):
            fe = _flux(vel_e, cen[f], nbr_e[f], face_e)
            fw = _flux(vel_w, nbr_w[f], cen[f], face_w)
            fn = _flux(vel_n, cen[f], nbr_n[f], face_n)
            fs = _flux(vel_s, nbr_s[f], cen[f], face_s)
            moved.append(cen[f] - (fe - fw + fn - fs))
        grad_x = 0.5 * (face_e * (p_e - p_c) + face_w * (p_c - p_w))
        grad_y = 0.5 * (face_n * (p_n - p_c) + face_s * (p_c - p_s))
        east_new = moved[2] + cor03 * cen[3] - grad_x
        north_new = moved[3] - cor03 * cen[2] - grad_y
        top = (k == 0).astype(jnp.float32)
        forced = [moved[0] * wc, moved[1] * wc,
                  east_new * wc + wind_ref[0] * wc * top,
                  north_new * wc + wind_ref[1] * wc * top]
        vy = []
        for f in range(fields):
            m = f // 2
            val = (forced[f] + c_prev[m] * vy_prev[f]) * inv_ref[m, kk]
            y_ref[f, k] = val
            vy.append(val)
        c_here = jnp.stack([c_ref[0, kk], c_ref[1, kk]])
        return (run_c, run_xw, run_xe, run_ys, run_yn), jnp.stack(vy), c_here

    run = (run_c_s[...], run_xw_s[...], run_xe_s[...], run_ys_s[...], run_yn_s[...])
    carry = lax.fori_loop(0, chunk, level, (run, vy_s[...], cprev_s[...]), unroll=chunk)
    run, vy, c_prev = carry
    run_c_s[...], run_xw_s[...], run_xe_s[...], run_ys_s[...], run_yn_s[...] = run
    vy_s[...] = vy
    cprev_s[...] = c_prev

    @pl.when(step_i == pl.num_programs(0) - 1)
    def _():
        for f in range(fields):
            ends_ref[fields + f] = vy[f]

        def back(j, later):
            k = levels - 2 - j
            out = []
            for f in range(fields):
                val = y_ref[f, k] + ratio_ref[f // 2, k] * later[f]
                y_ref[f, k] = val
                out.append(val)
            return jnp.stack(out)

        later = lax.fori_loop(0, levels - 1, back, vy, unroll=levels - 1)
        for f in range(fields):
            ends_ref[f] = later[f]


def fused_solve(*operands):
    st = operands[0]
    fields, levels, nx, ny = st.shape
    pairs = operands[21].shape[0]
    chunk = 8 if levels % 8 == 0 else levels
    whole = [pl.BlockSpec(op.shape, (lambda i, n=op.ndim: (0,) * n)) for op in operands]
    by_level = lambda op: pl.BlockSpec((op.shape[0], chunk) + op.shape[2:], lambda i: (0, i, 0, 0))
    specs = list(whole)
    for idx in (0, 3, 4, 21, 22):
        specs[idx] = by_level(operands[idx])
    return pl.pallas_call(
        fused_kernel,
        grid=(levels // chunk,),
        in_specs=specs,
        out_specs=[pl.BlockSpec(st.shape, lambda i: (0, 0, 0, 0)),
                   pl.BlockSpec((2 * fields, nx, ny), lambda i: (0, 0, 0))],
        out_shape=[jax.ShapeDtypeStruct(st.shape, jnp.float32),
                   jax.ShapeDtypeStruct((2 * fields, nx, ny), jnp.float32)],
        scratch_shapes=[pltpu.VMEM((nx, ny), jnp.float32), pltpu.VMEM((1, ny), jnp.float32),
                        pltpu.VMEM((1, ny), jnp.float32), pltpu.VMEM((nx, 1), jnp.float32),
                        pltpu.VMEM((nx, 1), jnp.float32), pltpu.VMEM((fields, nx, ny), jnp.float32),
                        pltpu.VMEM((pairs, nx, ny), jnp.float32)],
        compiler_params=pltpu.CompilerParams(vmem_limit_bytes=60 * 1024 * 1024),
    )(*operands)


def per_device(state, mixing, depth_levels, wind):
    fields, lev_count, col_x, col_y = state.shape
    total_x, total_y = depth_levels.shape
    peers_z = lax.axis_size("gz")
    place_z = lax.axis_index("gz")
    peers_x = lax.axis_size("gx")
    peers_y = lax.axis_size("gy")
    start_x = lax.axis_index("gx") * col_x
    start_y = lax.axis_index("gy") * col_y
    start_z = place_z * lev_count
    down_z = [(i, i + 1) for i in range(peers_z - 1)]
    mix_above = lax.ppermute(mixing[:, lev_count - 1], "gz", down_z)
    up_x = [(i, (i + 1) % peers_x) for i in range(peers_x)]
    dn_x = [(j, i) for i, j in up_x]
    up_y = [(i, (i + 1) % peers_y) for i in range(peers_y)]
    dn_y = [(j, i) for i, j in up_y]
    halo_xw = lax.ppermute(state[:, :, col_x - 1], "gx", up_x)
    halo_xe = lax.ppermute(state[:, :, 0], "gx", dn_x)
    halo_ys = lax.ppermute(state[:, :, :, col_y - 1], "gy", up_y)
    halo_yn = lax.ppermute(state[:, :, :, 0], "gy", dn_y)
    levels = start_z + jnp.arange(lev_count, dtype=jnp.int32)
    row_index = (start_x - 1 + jnp.arange(col_x + 2, dtype=jnp.int32)) % total_x
    col_index = (start_y - 1 + jnp.arange(col_y + 2, dtype=jnp.int32)) % total_y
    depth_pad = jnp.take(jnp.take(depth_levels, row_index, axis=0), col_index, axis=1) - start_z
    d_c = depth_pad[1:-1, 1:-1]
    d_e = depth_pad[2:, 1:-1]
    d_w = depth_pad[:-2, 1:-1]
    d_n = depth_pad[1:-1, 2:]
    d_s = depth_pad[1:-1, :-2]
    d_xw = depth_pad[0:1, 1:-1]
    d_xe = depth_pad[col_x + 1:, 1:-1]
    d_ys = depth_pad[1:-1, 0:1]
    d_yn = depth_pad[1:-1, col_y + 1:]
    local = jnp.arange(lev_count, dtype=jnp.int32)
    wet_here = (local[:, None, None] < d_c[None]).astype(jnp.float32)
    wet_next = ((local + 1)[:, None, None] < d_c[None]).astype(jnp.float32)
    coupling = mixing * (wet_here * wet_next)[None]
    wet_up = (-1 < d_c).astype(jnp.float32)
    ctop = mix_above * (wet_up * wet_here[0])[None]
    ctop = jnp.where(place_z > 0, ctop, 0.0)
    ratio, inv, u, v, uv_ends = coupling_solve(coupling, ctop)
    uv_all = lax.all_gather(uv_ends, "gz")
    lev3 = local[:, None, None]
    tot_c = jnp.sum(density_of(state, (lev3 < d_c[None]).astype(jnp.float32)), axis=0)
    lev2 = local[:, None]
    tot_xw = jnp.sum(density_of(halo_xw, (lev2 < d_xw[0][None]).astype(jnp.float32)), axis=0)
    tot_xe = jnp.sum(density_of(halo_xe, (lev2 < d_xe[0][None]).astype(jnp.float32)), axis=0)
    tot_ys = jnp.sum(density_of(halo_ys, (lev2 < d_ys[:, 0][None]).astype(jnp.float32)), axis=0)
    tot_yn = jnp.sum(density_of(halo_yn, (lev2 < d_yn[:, 0][None]).astype(jnp.float32)), axis=0)
    side = jnp.zeros((2, col_y), jnp.float32)
    side = side.at[0, :col_x].set(tot_ys).at[1, :col_x].set(tot_yn)
    pack = jnp.concatenate([tot_c, tot_xw[None], tot_xe[None], side], axis=0)
    shallower = jnp.zeros_like(pack)
    for hop in range(1, peers_z):
        pairs_z = [(i, i + hop) for i in range(peers_z - hop)]
        shallower = shallower + lax.ppermute(pack, "gz", pairs_z)
    s_c = shallower[:col_x]
    s_xw = shallower[col_x:col_x + 1]
    s_xe = shallower[col_x + 1:col_x + 2]
    s_ys = shallower[col_x + 2, :col_x][:, None]
    s_yn = shallower[col_x + 3, :col_x][:, None]
    face_row = start_y + jnp.arange(col_y, dtype=jnp.int32)
    wall_n = (face_row <= total_y - 2).astype(jnp.float32)
    wall_s = (face_row - 1 >= 0).astype(jnp.float32)
    coriolis = 0.5 + (face_row.astype(jnp.float32) + 0.5) / total_y
    lanes = jnp.stack([wall_n, wall_s, 0.3 * coriolis] + [jnp.zeros_like(wall_n)] * 5)
    wind_top = jnp.where(place_z == 0, wind, 0.0)
    y, y_ends = fused_solve(state, halo_xw, halo_xe, halo_ys[..., None], halo_yn[..., None],
                            d_c, d_e, d_w, d_n, d_s, d_xw, d_xe, d_ys, d_yn,
                            s_c, s_xw, s_xe, s_ys, s_yn, lanes, wind_top,
                            coupling, inv, ratio)
    y_all = gather_by_permutes(y_ends, "gz", place_z, peers_z)
    x_above, x_below = interface_values(y_all, uv_all, place_z, peers_z)
    pairs = u.shape[0]
    shape5 = (pairs, fields // pairs) + y.shape[1:]
    plane5 = (pairs, fields // pairs, 1, col_x, col_y)
    x = (y.reshape(shape5) + x_above.reshape(plane5) * u[:, None]
         + x_below.reshape(plane5) * v[:, None])
    return x.reshape(y.shape)


def solution(mesh):
    return jax.shard_map(
        per_device,
        mesh=mesh,
        in_specs=(P(None, "gz", "gx", "gy"), P(None, "gz", "gx", "gy"), P(), P(None, "gx", "gy")),
        out_specs=P(None, "gz", "gx", "gy"),
        check_vma=False,
    )
```

```python
import jax
import jax.numpy as jnp
from jax import lax
from jax.experimental import pallas as pl
from jax.experimental.pallas import tpu as pltpu
from jax.sharding import PartitionSpec as P


def padded_2(array, sides, width):
    for axis, dim in sides:
        peers, length = (lax.axis_size(axis), array.shape[dim])
        up = [(i, (i + 1) % peers) for i in range(peers)]
        down = [(j, i) for i, j in up]
        last = lax.slice_in_dim(array, length - width, length, axis=dim)
        initial = lax.slice_in_dim(array, 0, width, axis=dim)
        before = lax.ppermute(last, axis, up)
        after = lax.ppermute(initial, axis, down)
        array = jnp.concatenate([before, array, after], axis=dim)
    return array


def density_of(fields, wet_mask):
    return (-0.3 * fields[0] + 0.7 * fields[1] - 0.05 * fields[0] * fields[0]) * wet_mask


def advance(padded, wet_pad, pressure, wall_face, coriolis):
    wet_x = wet_pad[:, :-1, 1:-1] * wet_pad[:, 1:, 1:-1]
    wet_y = wet_pad[:, 1:-1, :-1] * wet_pad[:, 1:-1, 1:] * wall_face
    east_vel = 0.5 * (padded[2, :, :-1, 1:-1] + padded[2, :, 1:, 1:-1]) * wet_x
    north_vel = 0.5 * (padded[3, :, 1:-1, :-1] + padded[3, :, 1:-1, 1:]) * wet_y
    west_side = padded[:, :, :-1, 1:-1]
    east_side = padded[:, :, 1:, 1:-1]
    flux_x = 0.25 * (
        jnp.maximum(east_vel, 0.0) * west_side + jnp.minimum(east_vel, 0.0) * east_side
    ) - 0.08 * wet_x * (east_side - west_side)
    south_side = padded[:, :, 1:-1, :-1]
    north_side = padded[:, :, 1:-1, 1:]
    flux_y = 0.25 * (
        jnp.maximum(north_vel, 0.0) * south_side + jnp.minimum(north_vel, 0.0) * north_side
    ) - 0.08 * wet_y * (north_side - south_side)
    interior = padded[:, :, 1:-1, 1:-1]
    moved = interior - (
        flux_x[:, :, 1:] - flux_x[:, :, :-1] + flux_y[:, :, :, 1:] - flux_y[:, :, :, :-1]
    )
    centre = pressure[:, 1:-1, 1:-1]
    grad_x = 0.5 * (
        wet_x[:, 1:] * (pressure[:, 2:, 1:-1] - centre)
        + wet_x[:, :-1] * (centre - pressure[:, :-2, 1:-1])
    )
    grad_y = 0.5 * (
        wet_y[:, :, 1:] * (pressure[:, 1:-1, 2:] - centre)
        + wet_y[:, :, :-1] * (centre - pressure[:, 1:-1, :-2])
    )
    east_new = moved[2] + 0.3 * coriolis * interior[3] - grad_x
    north_new = moved[3] - 0.3 * coriolis * interior[2] - grad_y
    wet_inner = wet_pad[:, 1:-1, 1:-1]
    return jnp.stack([moved[0], moved[1], east_new, north_new]) * wet_inner


def coupling_kernel(c_ref, ctop_ref, ratio_ref, inv_ref, u_ref, v_ref, ends_ref):
    levels = c_ref.shape[1]
    ctop = ctop_ref[...]
    ratio_prev = None
    vu_prev = None
    for k in range(levels):
        above = ctop if k == 0 else c_ref[:, k - 1]
        below = c_ref[:, k]
        if k == 0:
            divisor = 1.0 + above + below
        else:
            divisor = 1.0 + above * (1.0 - ratio_prev) + below
        inv = 1.0 / divisor
        ratio = below * inv
        vu = ctop * inv if k == 0 else above * vu_prev * inv
        ratio_ref[:, k] = ratio
        inv_ref[:, k] = inv
        u_ref[:, k] = vu
        ratio_prev, vu_prev = ratio, vu
    u_later = vu_prev
    v_later = ratio_prev
    pairs = c_ref.shape[0]
    ends_ref[pairs:2 * pairs] = u_later
    ends_ref[3 * pairs:4 * pairs] = v_later
    v_ref[:, levels - 1] = v_later
    for k in range(levels - 2, -1, -1):
        ratio = ratio_ref[:, k]
        u_later = u_ref[:, k] + ratio * u_later
        v_later = ratio * v_later
        u_ref[:, k] = u_later
        v_ref[:, k] = v_later
    ends_ref[0:pairs] = u_later
    ends_ref[2 * pairs:3 * pairs] = v_later


def field_kernel(f_ref, c_ref, ctop_ref, ratio_ref, inv_ref, y_ref, ends_ref):
    levels = f_ref.shape[1]
    fields = f_ref.shape[0]
    vy = None
    for k in range(levels):
        inv = jnp.repeat(inv_ref[:, k], 2, axis=0)
        rhs = f_ref[:, k]
        if k == 0:
            vy = rhs * inv
        else:
            above = jnp.repeat(c_ref[:, k - 1], 2, axis=0)
            vy = (rhs + above * vy) * inv
        y_ref[:, k] = vy
    y_later = vy
    ends_ref[fields:2 * fields] = y_later
    for k in range(levels - 2, -1, -1):
        ratio = jnp.repeat(ratio_ref[:, k], 2, axis=0)
        y_later = y_ref[:, k] + ratio * y_later
        y_ref[:, k] = y_later
    ends_ref[0:fields] = y_later


def _specs(lead, levels, bx, cols_y):
    return pl.BlockSpec((lead, levels, bx, cols_y), lambda i: (0, 0, i, 0))


def _plane_spec(lead, bx, cols_y):
    return pl.BlockSpec((lead, bx, cols_y), lambda i: (0, i, 0))


def coupling_solve(coupling, ctop):
    pairs, levels, cols_x, cols_y = coupling.shape
    bx = cols_x
    cspec = _specs(pairs, levels, bx, cols_y)
    full = jax.ShapeDtypeStruct(coupling.shape, jnp.float32)
    return pl.pallas_call(
        coupling_kernel,
        grid=(cols_x // bx,),
        in_specs=[cspec, _plane_spec(pairs, bx, cols_y)],
        out_specs=[cspec, cspec, cspec, cspec, _plane_spec(4 * pairs, bx, cols_y)],
        out_shape=[full, full, full, full,
                   jax.ShapeDtypeStruct((4 * pairs, cols_x, cols_y), jnp.float32)],
    )(coupling, ctop)


def field_solve(forced, coupling, ctop, ratio, inv):
    fields, levels, cols_x, cols_y = forced.shape
    pairs = coupling.shape[0]
    bx = 8 if cols_x % 8 == 0 else cols_x
    fspec = _specs(fields, levels, bx, cols_y)
    cspec = _specs(pairs, levels, bx, cols_y)
    return pl.pallas_call(
        field_kernel,
        grid=(cols_x // bx,),
        in_specs=[fspec, cspec, _plane_spec(pairs, bx, cols_y), cspec, cspec],
        out_specs=[fspec, _plane_spec(2 * fields, bx, cols_y)],
        out_shape=[jax.ShapeDtypeStruct(forced.shape, jnp.float32),
                   jax.ShapeDtypeStruct((2 * fields, cols_x, cols_y), jnp.float32)],
    )(forced, coupling, ctop, ratio, inv)


def interface_values(y_ends, uv_ends, place, peers):
    fields = 4
    y0 = y_ends[:, 0:fields]
    y1 = y_ends[:, fields:2 * fields]
    rest = jnp.repeat(uv_ends, 2, axis=1)
    u0 = rest[:, 0:4]
    u1 = rest[:, 4:8]
    v0 = rest[:, 8:12]
    v1 = rest[:, 12:16]
    pt, qt, pb, qb = [], [], [], []
    for q in range(peers):
        if q == 0:
            pt_q, qt_q = y0[q], v0[q]
            pb_q, qb_q = y1[q], v1[q]
        else:
            inv = 1.0 / (1.0 - u0[q] * qb[-1])
            pt_q = (y0[q] + u0[q] * pb[-1]) * inv
            qt_q = v0[q] * inv
            pb_q = y1[q] + u1[q] * (pb[-1] + qb[-1] * pt_q)
            qb_q = v1[q] + u1[q] * qb[-1] * qt_q
        pt.append(pt_q)
        qt.append(qt_q)
        pb.append(pb_q)
        qb.append(qb_q)
    tops = [None] * peers
    bots = [None] * peers
    t_next = jnp.zeros_like(pt[0])
    for q in range(peers - 1, -1, -1):
        tops[q] = pt[q] + qt[q] * t_next
        bots[q] = pb[q] + qb[q] * t_next
        t_next = tops[q]
    above = jnp.zeros_like(pt[0])
    below = jnp.zeros_like(pt[0])
    for q in range(peers):
        if q >= 1:
            above = jnp.where(place == q, bots[q - 1], above)
        if q <= peers - 2:
            below = jnp.where(place == q, tops[q + 1], below)
    return above, below


def gather_by_permutes(part, axis, place, peers):
    received = [part]
    for hop in range(1, peers):
        shift = [(i, (i + hop) % peers) for i in range(peers)]
        received.append(lax.ppermute(part, axis, shift))
    rows = []
    for q in range(peers):
        row = received[0]
        for hop in range(1, peers):
            row = jnp.where((place - hop) % peers == q, received[hop], row)
        rows.append(row)
    return jnp.stack(rows)


def _density(t, s, w):
    return (-0.3 * t + 0.7 * s - 0.05 * t * t) * w


def _flux(vel, lo, hi, w):
    return 0.25 * (jnp.maximum(vel, 0.0) * lo + jnp.minimum(vel, 0.0) * hi) - 0.08 * w * (hi - lo)


def fused_kernel(st_ref, xw_ref, xe_ref, ys_ref, yn_ref,
                 dc_ref, de_ref, dw_ref, dn_ref, ds_ref,
                 dxw_ref, dxe_ref, dys_ref, dyn_ref,
                 sc_ref, sxw_ref, sxe_ref, sys_ref, syn_ref,
                 lane_ref, wind_ref, c_ref, inv_ref, ratio_ref,
                 y_ref, ends_ref,
                 run_c_s, run_xw_s, run_xe_s, run_ys_s, run_yn_s, vy_s, cprev_s):
    fields, chunk, nx, ny = st_ref.shape
    levels = y_ref.shape[1]
    step_i = pl.program_id(0)
    row = lax.broadcasted_iota(jnp.int32, (nx, ny), 0)
    lane = lax.broadcasted_iota(jnp.int32, (nx, ny), 1)
    wall_n = lane_ref[0:1]
    wall_s = lane_ref[1:2]
    cor03 = lane_ref[2:3]
    d_c, d_e, d_w, d_n, d_s = dc_ref[...], de_ref[...], dw_ref[...], dn_ref[...], ds_ref[...]
    d_xw, d_xe, d_ys, d_yn = dxw_ref[...], dxe_ref[...], dys_ref[...], dyn_ref[...]

    @pl.when(step_i == 0)
    def _():
        run_c_s[...] = jnp.zeros_like(run_c_s)
        run_xw_s[...] = jnp.zeros_like(run_xw_s)
        run_xe_s[...] = jnp.zeros_like(run_xe_s)
        run_ys_s[...] = jnp.zeros_like(run_ys_s)
        run_yn_s[...] = jnp.zeros_like(run_yn_s)
        vy_s[...] = jnp.zeros_like(vy_s)
        cprev_s[...] = jnp.zeros_like(cprev_s)

    def east(r, h):
        return jnp.where(row == nx - 1, h, pltpu.roll(r, nx - 1, 0))

    def west(r, h):
        return jnp.where(row == 0, h, pltpu.roll(r, 1, 0))

    def north(r, h):
        return jnp.where(lane == ny - 1, h, pltpu.roll(r, ny - 1, 1))

    def south(r, h):
        return jnp.where(lane == 0, h, pltpu.roll(r, 1, 1))

    def level(kk, carry):
        run, vy_prev, c_prev = carry
        k = step_i * chunk + kk
        wc = (k < d_c).astype(jnp.float32)
        we = (k < d_e).astype(jnp.float32)
        ww = (k < d_w).astype(jnp.float32)
        wn = (k < d_n).astype(jnp.float32)
        ws = (k < d_s).astype(jnp.float32)
        wxw = (k < d_xw).astype(jnp.float32)
        wxe = (k < d_xe).astype(jnp.float32)
        wys = (k < d_ys).astype(jnp.float32)
        wyn = (k < d_yn).astype(jnp.float32)
        cen = [st_ref[f, kk] for f in range(fields)]
        hxw = [xw_ref[f, pl.ds(k, 1), :] for f in range(fields)]
        hxe = [xe_ref[f, pl.ds(k, 1), :] for f in range(fields)]
        hys = [ys_ref[f, kk] for f in range(fields)]
        hyn = [yn_ref[f, kk] for f in range(fields)]
        run_c, run_xw, run_xe, run_ys, run_yn = run
        den_c = _density(cen[0], cen[1], wc)
        den_xw = _density(hxw[0], hxw[1], wxw)
        den_xe = _density(hxe[0], hxe[1], wxe)
        den_ys = _density(hys[0], hys[1], wys)
        den_yn = _density(hyn[0], hyn[1], wyn)
        run_c = run_c + den_c
        run_xw = run_xw + den_xw
        run_xe = run_xe + den_xe
        run_ys = run_ys + den_ys
        run_yn = run_yn + den_yn
        p_c = 0.03 * (sc_ref[...] + run_c - 0.5 * den_c)
        p_xw = 0.03 * (sxw_ref[...] + run_xw - 0.5 * den_xw)
        p_xe = 0.03 * (sxe_ref[...] + run_xe - 0.5 * den_xe)
        p_ys = 0.03 * (sys_ref[...] + run_ys - 0.5 * den_ys)
        p_yn = 0.03 * (syn_ref[...] + run_yn - 0.5 * den_yn)
        p_e = east(p_c, p_xe)
        p_w = west(p_c, p_xw)
        p_n = north(p_c, p_yn)
        p_s = south(p_c, p_ys)
        face_e = wc * we
        face_w = ww * wc
        face_n = wc * wn * wall_n
        face_s = ws * wc * wall_s
        nbr_e = [east(cen[f], hxe[f]) for f in range(fields)]
        nbr_w = [west(cen[f], hxw[f]) for f in range(fields)]
        nbr_n = [north(cen[f], hyn[f]) for f in range(fields)]
        nbr_s = [south(cen[f], hys[f]) for f in range(fields)]
        vel_e = 0.5 * (cen[2] + nbr_e[2]) * face_e
        vel_w = 0.5 * (nbr_w[2] + cen[2]) * face_w
        vel_n = 0.5 * (cen[3] + nbr_n[3]) * face_n
        vel_s = 0.5 * (nbr_s[3] + cen[3]) * face_s
        moved = []
        for f in range(fields):
            fe = _flux(vel_e, cen[f], nbr_e[f], face_e)
            fw = _flux(vel_w, nbr_w[f], cen[f], face_w)
            fn = _flux(vel_n, cen[f], nbr_n[f], face_n)
            fs = _flux(vel_s, nbr_s[f], cen[f], face_s)
            moved.append(cen[f] - (fe - fw + fn - fs))
        grad_x = 0.5 * (face_e * (p_e - p_c) + face_w * (p_c - p_w))
        grad_y = 0.5 * (face_n * (p_n - p_c) + face_s * (p_c - p_s))
        east_new = moved[2] + cor03 * cen[3] - grad_x
        north_new = moved[3] - cor03 * cen[2] - grad_y
        top = (k == 0).astype(jnp.float32)
        forced = [moved[0] * wc, moved[1] * wc,
                  east_new * wc + wind_ref[0] * wc * top,
                  north_new * wc + wind_ref[1] * wc * top]
        vy = []
        for f in range(fields):
            m = f // 2
            val = (forced[f] + c_prev[m] * vy_prev[f]) * inv_ref[m, kk]
            y_ref[f, k] = val
            vy.append(val)
        c_here = jnp.stack([c_ref[0, kk], c_ref[1, kk]])
        return (run_c, run_xw, run_xe, run_ys, run_yn), jnp.stack(vy), c_here

    run = (run_c_s[...], run_xw_s[...], run_xe_s[...], run_ys_s[...], run_yn_s[...])
    carry = lax.fori_loop(0, chunk, level, (run, vy_s[...], cprev_s[...]), unroll=chunk)
    run, vy, c_prev = carry
    run_c_s[...], run_xw_s[...], run_xe_s[...], run_ys_s[...], run_yn_s[...] = run
    vy_s[...] = vy
    cprev_s[...] = c_prev

    @pl.when(step_i == pl.num_programs(0) - 1)
    def _():
        for f in range(fields):
            ends_ref[fields + f] = vy[f]

        def back(j, later):
            k = levels - 2 - j
            out = []
            for f in range(fields):
                val = y_ref[f, k] + ratio_ref[f // 2, k] * later[f]
                y_ref[f, k] = val
                out.append(val)
            return jnp.stack(out)

        later = lax.fori_loop(0, levels - 1, back, vy, unroll=2)
        for f in range(fields):
            ends_ref[f] = later[f]


def fused_solve(*operands):
    st = operands[0]
    fields, levels, nx, ny = st.shape
    pairs = operands[21].shape[0]
    chunk = 8 if levels % 8 == 0 else levels
    whole = [pl.BlockSpec(op.shape, (lambda i, n=op.ndim: (0,) * n)) for op in operands]
    by_level = lambda op: pl.BlockSpec((op.shape[0], chunk) + op.shape[2:], lambda i: (0, i, 0, 0))
    specs = list(whole)
    for idx in (0, 3, 4, 21, 22):
        specs[idx] = by_level(operands[idx])
    return pl.pallas_call(
        fused_kernel,
        grid=(levels // chunk,),
        in_specs=specs,
        out_specs=[pl.BlockSpec(st.shape, lambda i: (0, 0, 0, 0)),
                   pl.BlockSpec((2 * fields, nx, ny), lambda i: (0, 0, 0))],
        out_shape=[jax.ShapeDtypeStruct(st.shape, jnp.float32),
                   jax.ShapeDtypeStruct((2 * fields, nx, ny), jnp.float32)],
        scratch_shapes=[pltpu.VMEM((nx, ny), jnp.float32), pltpu.VMEM((1, ny), jnp.float32),
                        pltpu.VMEM((1, ny), jnp.float32), pltpu.VMEM((nx, 1), jnp.float32),
                        pltpu.VMEM((nx, 1), jnp.float32), pltpu.VMEM((fields, nx, ny), jnp.float32),
                        pltpu.VMEM((pairs, nx, ny), jnp.float32)],
        compiler_params=pltpu.CompilerParams(vmem_limit_bytes=60 * 1024 * 1024),
    )(*operands)


def per_device(state, mixing, depth_levels, wind):
    fields, lev_count, col_x, col_y = state.shape
    total_x, total_y = depth_levels.shape
    peers_z = lax.axis_size("gz")
    place_z = lax.axis_index("gz")
    peers_x = lax.axis_size("gx")
    peers_y = lax.axis_size("gy")
    start_x = lax.axis_index("gx") * col_x
    start_y = lax.axis_index("gy") * col_y
    start_z = place_z * lev_count
    down_z = [(i, i + 1) for i in range(peers_z - 1)]
    mix_above = lax.ppermute(mixing[:, lev_count - 1], "gz", down_z)
    up_x = [(i, (i + 1) % peers_x) for i in range(peers_x)]
    dn_x = [(j, i) for i, j in up_x]
    up_y = [(i, (i + 1) % peers_y) for i in range(peers_y)]
    dn_y = [(j, i) for i, j in up_y]
    halo_xw = lax.ppermute(state[:, :, col_x - 1], "gx", up_x)
    halo_xe = lax.ppermute(state[:, :, 0], "gx", dn_x)
    halo_ys = lax.ppermute(state[:, :, :, col_y - 1], "gy", up_y)
    halo_yn = lax.ppermute(state[:, :, :, 0], "gy", dn_y)
    levels = start_z + jnp.arange(lev_count, dtype=jnp.int32)
    row_index = (start_x - 1 + jnp.arange(col_x + 2, dtype=jnp.int32)) % total_x
    col_index = (start_y - 1 + jnp.arange(col_y + 2, dtype=jnp.int32)) % total_y
    depth_pad = jnp.take(jnp.take(depth_levels, row_index, axis=0), col_index, axis=1) - start_z
    d_c = depth_pad[1:-1, 1:-1]
    d_e = depth_pad[2:, 1:-1]
    d_w = depth_pad[:-2, 1:-1]
    d_n = depth_pad[1:-1, 2:]
    d_s = depth_pad[1:-1, :-2]
    d_xw = depth_pad[0:1, 1:-1]
    d_xe = depth_pad[col_x + 1:, 1:-1]
    d_ys = depth_pad[1:-1, 0:1]
    d_yn = depth_pad[1:-1, col_y + 1:]
    local = jnp.arange(lev_count, dtype=jnp.int32)
    wet_here = (local[:, None, None] < d_c[None]).astype(jnp.float32)
    wet_next = ((local + 1)[:, None, None] < d_c[None]).astype(jnp.float32)
    coupling = mixing * (wet_here * wet_next)[None]
    wet_up = (-1 < d_c).astype(jnp.float32)
    ctop = mix_above * (wet_up * wet_here[0])[None]
    ctop = jnp.where(place_z > 0, ctop, 0.0)
    ratio, inv, u, v, uv_ends = coupling_solve(coupling, ctop)
    uv_all = lax.all_gather(uv_ends, "gz")
    lev3 = local[:, None, None]
    tot_c = jnp.sum(density_of(state, (lev3 < d_c[None]).astype(jnp.float32)), axis=0)
    lev2 = local[:, None]
    tot_xw = jnp.sum(density_of(halo_xw, (lev2 < d_xw[0][None]).astype(jnp.float32)), axis=0)
    tot_xe = jnp.sum(density_of(halo_xe, (lev2 < d_xe[0][None]).astype(jnp.float32)), axis=0)
    tot_ys = jnp.sum(density_of(halo_ys, (lev2 < d_ys[:, 0][None]).astype(jnp.float32)), axis=0)
    tot_yn = jnp.sum(density_of(halo_yn, (lev2 < d_yn[:, 0][None]).astype(jnp.float32)), axis=0)
    side = jnp.zeros((2, col_y), jnp.float32)
    side = side.at[0, :col_x].set(tot_ys).at[1, :col_x].set(tot_yn)
    pack = jnp.concatenate([tot_c, tot_xw[None], tot_xe[None], side], axis=0)
    shallower = jnp.zeros_like(pack)
    for hop in range(1, peers_z):
        pairs_z = [(i, i + hop) for i in range(peers_z - hop)]
        shallower = shallower + lax.ppermute(pack, "gz", pairs_z)
    s_c = shallower[:col_x]
    s_xw = shallower[col_x:col_x + 1]
    s_xe = shallower[col_x + 1:col_x + 2]
    s_ys = shallower[col_x + 2, :col_x][:, None]
    s_yn = shallower[col_x + 3, :col_x][:, None]
    face_row = start_y + jnp.arange(col_y, dtype=jnp.int32)
    wall_n = (face_row <= total_y - 2).astype(jnp.float32)
    wall_s = (face_row - 1 >= 0).astype(jnp.float32)
    coriolis = 0.5 + (face_row.astype(jnp.float32) + 0.5) / total_y
    lanes = jnp.stack([wall_n, wall_s, 0.3 * coriolis] + [jnp.zeros_like(wall_n)] * 5)
    wind_top = jnp.where(place_z == 0, wind, 0.0)
    y, y_ends = fused_solve(state, halo_xw, halo_xe, halo_ys[..., None], halo_yn[..., None],
                            d_c, d_e, d_w, d_n, d_s, d_xw, d_xe, d_ys, d_yn,
                            s_c, s_xw, s_xe, s_ys, s_yn, lanes, wind_top,
                            coupling, inv, ratio)
    y_all = gather_by_permutes(y_ends, "gz", place_z, peers_z)
    x_above, x_below = interface_values(y_all, uv_all, place_z, peers_z)
    pairs = u.shape[0]
    shape5 = (pairs, fields // pairs) + y.shape[1:]
    plane5 = (pairs, fields // pairs, 1, col_x, col_y)
    x = (y.reshape(shape5) + x_above.reshape(plane5) * u[:, None]
         + x_below.reshape(plane5) * v[:, None])
    return x.reshape(y.shape)


def solution(mesh):
    return jax.shard_map(
        per_device,
        mesh=mesh,
        in_specs=(P(None, "gz", "gx", "gy"), P(None, "gz", "gx", "gy"), P(), P(None, "gx", "gy")),
        out_specs=P(None, "gz", "gx", "gy"),
        check_vma=False,
    )
```

```python
import jax
import jax.numpy as jnp
from jax import lax
from jax.experimental import pallas as pl
from jax.experimental.pallas import tpu as pltpu
from jax.sharding import PartitionSpec as P


def padded_2(array, sides, width):
    for axis, dim in sides:
        peers, length = (lax.axis_size(axis), array.shape[dim])
        up = [(i, (i + 1) % peers) for i in range(peers)]
        down = [(j, i) for i, j in up]
        last = lax.slice_in_dim(array, length - width, length, axis=dim)
        initial = lax.slice_in_dim(array, 0, width, axis=dim)
        before = lax.ppermute(last, axis, up)
        after = lax.ppermute(initial, axis, down)
        array = jnp.concatenate([before, array, after], axis=dim)
    return array


def density_of(fields, wet_mask):
    return (-0.3 * fields[0] + 0.7 * fields[1] - 0.05 * fields[0] * fields[0]) * wet_mask


def advance(padded, wet_pad, pressure, wall_face, coriolis):
    wet_x = wet_pad[:, :-1, 1:-1] * wet_pad[:, 1:, 1:-1]
    wet_y = wet_pad[:, 1:-1, :-1] * wet_pad[:, 1:-1, 1:] * wall_face
    east_vel = 0.5 * (padded[2, :, :-1, 1:-1] + padded[2, :, 1:, 1:-1]) * wet_x
    north_vel = 0.5 * (padded[3, :, 1:-1, :-1] + padded[3, :, 1:-1, 1:]) * wet_y
    west_side = padded[:, :, :-1, 1:-1]
    east_side = padded[:, :, 1:, 1:-1]
    flux_x = 0.25 * (
        jnp.maximum(east_vel, 0.0) * west_side + jnp.minimum(east_vel, 0.0) * east_side
    ) - 0.08 * wet_x * (east_side - west_side)
    south_side = padded[:, :, 1:-1, :-1]
    north_side = padded[:, :, 1:-1, 1:]
    flux_y = 0.25 * (
        jnp.maximum(north_vel, 0.0) * south_side + jnp.minimum(north_vel, 0.0) * north_side
    ) - 0.08 * wet_y * (north_side - south_side)
    interior = padded[:, :, 1:-1, 1:-1]
    moved = interior - (
        flux_x[:, :, 1:] - flux_x[:, :, :-1] + flux_y[:, :, :, 1:] - flux_y[:, :, :, :-1]
    )
    centre = pressure[:, 1:-1, 1:-1]
    grad_x = 0.5 * (
        wet_x[:, 1:] * (pressure[:, 2:, 1:-1] - centre)
        + wet_x[:, :-1] * (centre - pressure[:, :-2, 1:-1])
    )
    grad_y = 0.5 * (
        wet_y[:, :, 1:] * (pressure[:, 1:-1, 2:] - centre)
        + wet_y[:, :, :-1] * (centre - pressure[:, 1:-1, :-2])
    )
    east_new = moved[2] + 0.3 * coriolis * interior[3] - grad_x
    north_new = moved[3] - 0.3 * coriolis * interior[2] - grad_y
    wet_inner = wet_pad[:, 1:-1, 1:-1]
    return jnp.stack([moved[0], moved[1], east_new, north_new]) * wet_inner


def coupling_kernel(c_ref, ctop_ref, ratio_ref, inv_ref, u_ref, v_ref, ends_ref):
    levels = c_ref.shape[1]
    ctop = ctop_ref[...]
    ratio_prev = None
    vu_prev = None
    for k in range(levels):
        above = ctop if k == 0 else c_ref[:, k - 1]
        below = c_ref[:, k]
        if k == 0:
            divisor = 1.0 + above + below
        else:
            divisor = 1.0 + above * (1.0 - ratio_prev) + below
        inv = 1.0 / divisor
        ratio = below * inv
        vu = ctop * inv if k == 0 else above * vu_prev * inv
        ratio_ref[:, k] = ratio
        inv_ref[:, k] = inv
        u_ref[:, k] = vu
        ratio_prev, vu_prev = ratio, vu
    u_later = vu_prev
    v_later = ratio_prev
    pairs = c_ref.shape[0]
    ends_ref[pairs:2 * pairs] = u_later
    ends_ref[3 * pairs:4 * pairs] = v_later
    v_ref[:, levels - 1] = v_later
    for k in range(levels - 2, -1, -1):
        ratio = ratio_ref[:, k]
        u_later = u_ref[:, k] + ratio * u_later
        v_later = ratio * v_later
        u_ref[:, k] = u_later
        v_ref[:, k] = v_later
    ends_ref[0:pairs] = u_later
    ends_ref[2 * pairs:3 * pairs] = v_later


def field_kernel(f_ref, c_ref, ctop_ref, ratio_ref, inv_ref, y_ref, ends_ref):
    levels = f_ref.shape[1]
    fields = f_ref.shape[0]
    vy = None
    for k in range(levels):
        inv = jnp.repeat(inv_ref[:, k], 2, axis=0)
        rhs = f_ref[:, k]
        if k == 0:
            vy = rhs * inv
        else:
            above = jnp.repeat(c_ref[:, k - 1], 2, axis=0)
            vy = (rhs + above * vy) * inv
        y_ref[:, k] = vy
    y_later = vy
    ends_ref[fields:2 * fields] = y_later
    for k in range(levels - 2, -1, -1):
        ratio = jnp.repeat(ratio_ref[:, k], 2, axis=0)
        y_later = y_ref[:, k] + ratio * y_later
        y_ref[:, k] = y_later
    ends_ref[0:fields] = y_later


def _specs(lead, levels, bx, cols_y):
    return pl.BlockSpec((lead, levels, bx, cols_y), lambda i: (0, 0, i, 0))


def _plane_spec(lead, bx, cols_y):
    return pl.BlockSpec((lead, bx, cols_y), lambda i: (0, i, 0))


def coupling_solve(coupling, ctop):
    pairs, levels, cols_x, cols_y = coupling.shape
    bx = 16 if cols_x % 16 == 0 else cols_x
    cspec = _specs(pairs, levels, bx, cols_y)
    full = jax.ShapeDtypeStruct(coupling.shape, jnp.float32)
    return pl.pallas_call(
        coupling_kernel,
        grid=(cols_x // bx,),
        in_specs=[cspec, _plane_spec(pairs, bx, cols_y)],
        out_specs=[cspec, cspec, cspec, cspec, _plane_spec(4 * pairs, bx, cols_y)],
        out_shape=[full, full, full, full,
                   jax.ShapeDtypeStruct((4 * pairs, cols_x, cols_y), jnp.float32)],
    )(coupling, ctop)


def field_solve(forced, coupling, ctop, ratio, inv):
    fields, levels, cols_x, cols_y = forced.shape
    pairs = coupling.shape[0]
    bx = 8 if cols_x % 8 == 0 else cols_x
    fspec = _specs(fields, levels, bx, cols_y)
    cspec = _specs(pairs, levels, bx, cols_y)
    return pl.pallas_call(
        field_kernel,
        grid=(cols_x // bx,),
        in_specs=[fspec, cspec, _plane_spec(pairs, bx, cols_y), cspec, cspec],
        out_specs=[fspec, _plane_spec(2 * fields, bx, cols_y)],
        out_shape=[jax.ShapeDtypeStruct(forced.shape, jnp.float32),
                   jax.ShapeDtypeStruct((2 * fields, cols_x, cols_y), jnp.float32)],
    )(forced, coupling, ctop, ratio, inv)


def interface_values(y_ends, uv_ends, place, peers):
    fields = 4
    y0 = y_ends[:, 0:fields]
    y1 = y_ends[:, fields:2 * fields]
    rest = jnp.repeat(uv_ends, 2, axis=1)
    u0 = rest[:, 0:4]
    u1 = rest[:, 4:8]
    v0 = rest[:, 8:12]
    v1 = rest[:, 12:16]
    pt, qt, pb, qb = [], [], [], []
    for q in range(peers):
        if q == 0:
            pt_q, qt_q = y0[q], v0[q]
            pb_q, qb_q = y1[q], v1[q]
        else:
            inv = 1.0 / (1.0 - u0[q] * qb[-1])
            pt_q = (y0[q] + u0[q] * pb[-1]) * inv
            qt_q = v0[q] * inv
            pb_q = y1[q] + u1[q] * (pb[-1] + qb[-1] * pt_q)
            qb_q = v1[q] + u1[q] * qb[-1] * qt_q
        pt.append(pt_q)
        qt.append(qt_q)
        pb.append(pb_q)
        qb.append(qb_q)
    tops = [None] * peers
    bots = [None] * peers
    t_next = jnp.zeros_like(pt[0])
    for q in range(peers - 1, -1, -1):
        tops[q] = pt[q] + qt[q] * t_next
        bots[q] = pb[q] + qb[q] * t_next
        t_next = tops[q]
    above = jnp.zeros_like(pt[0])
    below = jnp.zeros_like(pt[0])
    for q in range(peers):
        if q >= 1:
            above = jnp.where(place == q, bots[q - 1], above)
        if q <= peers - 2:
            below = jnp.where(place == q, tops[q + 1], below)
    return above, below


def gather_by_permutes(part, axis, place, peers):
    received = [part]
    for hop in range(1, peers):
        shift = [(i, (i + hop) % peers) for i in range(peers)]
        received.append(lax.ppermute(part, axis, shift))
    rows = []
    for q in range(peers):
        row = received[0]
        for hop in range(1, peers):
            row = jnp.where((place - hop) % peers == q, received[hop], row)
        rows.append(row)
    return jnp.stack(rows)


def _density(t, s, w):
    return (-0.3 * t + 0.7 * s - 0.05 * t * t) * w


def _flux(vel, lo, hi, w):
    return 0.25 * (jnp.maximum(vel, 0.0) * lo + jnp.minimum(vel, 0.0) * hi) - 0.08 * w * (hi - lo)


def fused_kernel(st_ref, xw_ref, xe_ref, ys_ref, yn_ref,
                 dc_ref, de_ref, dw_ref, dn_ref, ds_ref,
                 dxw_ref, dxe_ref, dys_ref, dyn_ref,
                 sc_ref, sxw_ref, sxe_ref, sys_ref, syn_ref,
                 lane_ref, wind_ref, c_ref, inv_ref, ratio_ref,
                 y_ref, ends_ref,
                 run_c_s, run_xw_s, run_xe_s, run_ys_s, run_yn_s, vy_s, cprev_s):
    fields, chunk, nx, ny = st_ref.shape
    levels = y_ref.shape[1]
    step_i = pl.program_id(0)
    row = lax.broadcasted_iota(jnp.int32, (nx, ny), 0)
    lane = lax.broadcasted_iota(jnp.int32, (nx, ny), 1)
    wall_n = lane_ref[0:1]
    wall_s = lane_ref[1:2]
    cor03 = lane_ref[2:3]
    d_c, d_e, d_w, d_n, d_s = dc_ref[...], de_ref[...], dw_ref[...], dn_ref[...], ds_ref[...]
    d_xw, d_xe, d_ys, d_yn = dxw_ref[...], dxe_ref[...], dys_ref[...], dyn_ref[...]

    @pl.when(step_i == 0)
    def _():
        run_c_s[...] = jnp.zeros_like(run_c_s)
        run_xw_s[...] = jnp.zeros_like(run_xw_s)
        run_xe_s[...] = jnp.zeros_like(run_xe_s)
        run_ys_s[...] = jnp.zeros_like(run_ys_s)
        run_yn_s[...] = jnp.zeros_like(run_yn_s)
        vy_s[...] = jnp.zeros_like(vy_s)
        cprev_s[...] = jnp.zeros_like(cprev_s)

    def east(r, h):
        return jnp.where(row == nx - 1, h, pltpu.roll(r, nx - 1, 0))

    def west(r, h):
        return jnp.where(row == 0, h, pltpu.roll(r, 1, 0))

    def north(r, h):
        return jnp.where(lane == ny - 1, h, pltpu.roll(r, ny - 1, 1))

    def south(r, h):
        return jnp.where(lane == 0, h, pltpu.roll(r, 1, 1))

    def level(kk, carry):
        run, vy_prev, c_prev = carry
        k = step_i * chunk + kk
        wc = (k < d_c).astype(jnp.float32)
        we = (k < d_e).astype(jnp.float32)
        ww = (k < d_w).astype(jnp.float32)
        wn = (k < d_n).astype(jnp.float32)
        ws = (k < d_s).astype(jnp.float32)
        wxw = (k < d_xw).astype(jnp.float32)
        wxe = (k < d_xe).astype(jnp.float32)
        wys = (k < d_ys).astype(jnp.float32)
        wyn = (k < d_yn).astype(jnp.float32)
        cen = [st_ref[f, kk] for f in range(fields)]
        hxw = [xw_ref[f, pl.ds(k, 1), :] for f in range(fields)]
        hxe = [xe_ref[f, pl.ds(k, 1), :] for f in range(fields)]
        hys = [ys_ref[f, kk] for f in range(fields)]
        hyn = [yn_ref[f, kk] for f in range(fields)]
        run_c, run_xw, run_xe, run_ys, run_yn = run
        den_c = _density(cen[0], cen[1], wc)
        den_xw = _density(hxw[0], hxw[1], wxw)
        den_xe = _density(hxe[0], hxe[1], wxe)
        den_ys = _density(hys[0], hys[1], wys)
        den_yn = _density(hyn[0], hyn[1], wyn)
        run_c = run_c + den_c
        run_xw = run_xw + den_xw
        run_xe = run_xe + den_xe
        run_ys = run_ys + den_ys
        run_yn = run_yn + den_yn
        p_c = 0.03 * (sc_ref[...] + run_c - 0.5 * den_c)
        p_xw = 0.03 * (sxw_ref[...] + run_xw - 0.5 * den_xw)
        p_xe = 0.03 * (sxe_ref[...] + run_xe - 0.5 * den_xe)
        p_ys = 0.03 * (sys_ref[...] + run_ys - 0.5 * den_ys)
        p_yn = 0.03 * (syn_ref[...] + run_yn - 0.5 * den_yn)
        p_e = east(p_c, p_xe)
        p_w = west(p_c, p_xw)
        p_n = north(p_c, p_yn)
        p_s = south(p_c, p_ys)
        face_e = wc * we
        face_w = ww * wc
        face_n = wc * wn * wall_n
        face_s = ws * wc * wall_s
        nbr_e = [east(cen[f], hxe[f]) for f in range(fields)]
        nbr_w = [west(cen[f], hxw[f]) for f in range(fields)]
        nbr_n = [north(cen[f], hyn[f]) for f in range(fields)]
        nbr_s = [south(cen[f], hys[f]) for f in range(fields)]
        vel_e = 0.5 * (cen[2] + nbr_e[2]) * face_e
        vel_w = 0.5 * (nbr_w[2] + cen[2]) * face_w
        vel_n = 0.5 * (cen[3] + nbr_n[3]) * face_n
        vel_s = 0.5 * (nbr_s[3] + cen[3]) * face_s
        moved = []
        for f in range(fields):
            fe = _flux(vel_e, cen[f], nbr_e[f], face_e)
            fw = _flux(vel_w, nbr_w[f], cen[f], face_w)
            fn = _flux(vel_n, cen[f], nbr_n[f], face_n)
            fs = _flux(vel_s, nbr_s[f], cen[f], face_s)
            moved.append(cen[f] - (fe - fw + fn - fs))
        grad_x = 0.5 * (face_e * (p_e - p_c) + face_w * (p_c - p_w))
        grad_y = 0.5 * (face_n * (p_n - p_c) + face_s * (p_c - p_s))
        east_new = moved[2] + cor03 * cen[3] - grad_x
        north_new = moved[3] - cor03 * cen[2] - grad_y
        top = (k == 0).astype(jnp.float32)
        forced = [moved[0] * wc, moved[1] * wc,
                  east_new * wc + wind_ref[0] * wc * top,
                  north_new * wc + wind_ref[1] * wc * top]
        vy = []
        for f in range(fields):
            m = f // 2
            val = (forced[f] + c_prev[m] * vy_prev[f]) * inv_ref[m, kk]
            y_ref[f, k] = val
            vy.append(val)
        c_here = jnp.stack([c_ref[0, kk], c_ref[1, kk]])
        return (run_c, run_xw, run_xe, run_ys, run_yn), jnp.stack(vy), c_here

    run = (run_c_s[...], run_xw_s[...], run_xe_s[...], run_ys_s[...], run_yn_s[...])
    carry = lax.fori_loop(0, chunk, level, (run, vy_s[...], cprev_s[...]), unroll=chunk)
    run, vy, c_prev = carry
    run_c_s[...], run_xw_s[...], run_xe_s[...], run_ys_s[...], run_yn_s[...] = run
    vy_s[...] = vy
    cprev_s[...] = c_prev

    @pl.when(step_i == pl.num_programs(0) - 1)
    def _():
        for f in range(fields):
            ends_ref[fields + f] = vy[f]

        def back(j, later):
            k = levels - 2 - j
            out = []
            for f in range(fields):
                val = y_ref[f, k] + ratio_ref[f // 2, k] * later[f]
                y_ref[f, k] = val
                out.append(val)
            return jnp.stack(out)

        later = lax.fori_loop(0, levels - 1, back, vy, unroll=2)
        for f in range(fields):
            ends_ref[f] = later[f]


def fused_solve(*operands):
    st = operands[0]
    fields, levels, nx, ny = st.shape
    pairs = operands[21].shape[0]
    chunk = 6 if levels % 6 == 0 else levels
    whole = [pl.BlockSpec(op.shape, (lambda i, n=op.ndim: (0,) * n)) for op in operands]
    by_level = lambda op: pl.BlockSpec((op.shape[0], chunk) + op.shape[2:], lambda i: (0, i, 0, 0))
    specs = list(whole)
    for idx in (0, 3, 4, 21, 22):
        specs[idx] = by_level(operands[idx])
    return pl.pallas_call(
        fused_kernel,
        grid=(levels // chunk,),
        in_specs=specs,
        out_specs=[pl.BlockSpec(st.shape, lambda i: (0, 0, 0, 0)),
                   pl.BlockSpec((2 * fields, nx, ny), lambda i: (0, 0, 0))],
        out_shape=[jax.ShapeDtypeStruct(st.shape, jnp.float32),
                   jax.ShapeDtypeStruct((2 * fields, nx, ny), jnp.float32)],
        scratch_shapes=[pltpu.VMEM((nx, ny), jnp.float32), pltpu.VMEM((1, ny), jnp.float32),
                        pltpu.VMEM((1, ny), jnp.float32), pltpu.VMEM((nx, 1), jnp.float32),
                        pltpu.VMEM((nx, 1), jnp.float32), pltpu.VMEM((fields, nx, ny), jnp.float32),
                        pltpu.VMEM((pairs, nx, ny), jnp.float32)],
        compiler_params=pltpu.CompilerParams(vmem_limit_bytes=60 * 1024 * 1024),
    )(*operands)


def per_device(state, mixing, depth_levels, wind):
    fields, lev_count, col_x, col_y = state.shape
    total_x, total_y = depth_levels.shape
    peers_z = lax.axis_size("gz")
    place_z = lax.axis_index("gz")
    peers_x = lax.axis_size("gx")
    peers_y = lax.axis_size("gy")
    start_x = lax.axis_index("gx") * col_x
    start_y = lax.axis_index("gy") * col_y
    start_z = place_z * lev_count
    down_z = [(i, i + 1) for i in range(peers_z - 1)]
    mix_above = lax.ppermute(mixing[:, lev_count - 1], "gz", down_z)
    up_x = [(i, (i + 1) % peers_x) for i in range(peers_x)]
    dn_x = [(j, i) for i, j in up_x]
    up_y = [(i, (i + 1) % peers_y) for i in range(peers_y)]
    dn_y = [(j, i) for i, j in up_y]
    halo_xw = lax.ppermute(state[:, :, col_x - 1], "gx", up_x)
    halo_xe = lax.ppermute(state[:, :, 0], "gx", dn_x)
    halo_ys = lax.ppermute(state[:, :, :, col_y - 1], "gy", up_y)
    halo_yn = lax.ppermute(state[:, :, :, 0], "gy", dn_y)
    levels = start_z + jnp.arange(lev_count, dtype=jnp.int32)
    row_index = (start_x - 1 + jnp.arange(col_x + 2, dtype=jnp.int32)) % total_x
    col_index = (start_y - 1 + jnp.arange(col_y + 2, dtype=jnp.int32)) % total_y
    depth_pad = jnp.take(jnp.take(depth_levels, row_index, axis=0), col_index, axis=1) - start_z
    d_c = depth_pad[1:-1, 1:-1]
    d_e = depth_pad[2:, 1:-1]
    d_w = depth_pad[:-2, 1:-1]
    d_n = depth_pad[1:-1, 2:]
    d_s = depth_pad[1:-1, :-2]
    d_xw = depth_pad[0:1, 1:-1]
    d_xe = depth_pad[col_x + 1:, 1:-1]
    d_ys = depth_pad[1:-1, 0:1]
    d_yn = depth_pad[1:-1, col_y + 1:]
    local = jnp.arange(lev_count, dtype=jnp.int32)
    wet_here = (local[:, None, None] < d_c[None]).astype(jnp.float32)
    wet_next = ((local + 1)[:, None, None] < d_c[None]).astype(jnp.float32)
    coupling = mixing * (wet_here * wet_next)[None]
    wet_up = (-1 < d_c).astype(jnp.float32)
    ctop = mix_above * (wet_up * wet_here[0])[None]
    ctop = jnp.where(place_z > 0, ctop, 0.0)
    ratio, inv, u, v, uv_ends = coupling_solve(coupling, ctop)
    uv_all = lax.all_gather(uv_ends, "gz")
    lev3 = local[:, None, None]
    tot_c = jnp.sum(density_of(state, (lev3 < d_c[None]).astype(jnp.float32)), axis=0)
    lev2 = local[:, None]
    tot_xw = jnp.sum(density_of(halo_xw, (lev2 < d_xw[0][None]).astype(jnp.float32)), axis=0)
    tot_xe = jnp.sum(density_of(halo_xe, (lev2 < d_xe[0][None]).astype(jnp.float32)), axis=0)
    tot_ys = jnp.sum(density_of(halo_ys, (lev2 < d_ys[:, 0][None]).astype(jnp.float32)), axis=0)
    tot_yn = jnp.sum(density_of(halo_yn, (lev2 < d_yn[:, 0][None]).astype(jnp.float32)), axis=0)
    side = jnp.zeros((2, col_y), jnp.float32)
    side = side.at[0, :col_x].set(tot_ys).at[1, :col_x].set(tot_yn)
    pack = jnp.concatenate([tot_c, tot_xw[None], tot_xe[None], side], axis=0)
    shallower = jnp.zeros_like(pack)
    for hop in range(1, peers_z):
        pairs_z = [(i, i + hop) for i in range(peers_z - hop)]
        shallower = shallower + lax.ppermute(pack, "gz", pairs_z)
    s_c = shallower[:col_x]
    s_xw = shallower[col_x:col_x + 1]
    s_xe = shallower[col_x + 1:col_x + 2]
    s_ys = shallower[col_x + 2, :col_x][:, None]
    s_yn = shallower[col_x + 3, :col_x][:, None]
    face_row = start_y + jnp.arange(col_y, dtype=jnp.int32)
    wall_n = (face_row <= total_y - 2).astype(jnp.float32)
    wall_s = (face_row - 1 >= 0).astype(jnp.float32)
    coriolis = 0.5 + (face_row.astype(jnp.float32) + 0.5) / total_y
    lanes = jnp.stack([wall_n, wall_s, 0.3 * coriolis] + [jnp.zeros_like(wall_n)] * 5)
    wind_top = jnp.where(place_z == 0, wind, 0.0)
    y, y_ends = fused_solve(state, halo_xw, halo_xe, halo_ys[..., None], halo_yn[..., None],
                            d_c, d_e, d_w, d_n, d_s, d_xw, d_xe, d_ys, d_yn,
                            s_c, s_xw, s_xe, s_ys, s_yn, lanes, wind_top,
                            coupling, inv, ratio)
    y_all = gather_by_permutes(y_ends, "gz", place_z, peers_z)
    x_above, x_below = interface_values(y_all, uv_all, place_z, peers_z)
    pairs = u.shape[0]
    shape5 = (pairs, fields // pairs) + y.shape[1:]
    plane5 = (pairs, fields // pairs, 1, col_x, col_y)
    x = (y.reshape(shape5) + x_above.reshape(plane5) * u[:, None]
         + x_below.reshape(plane5) * v[:, None])
    return x.reshape(y.shape)


def solution(mesh):
    return jax.shard_map(
        per_device,
        mesh=mesh,
        in_specs=(P(None, "gz", "gx", "gy"), P(None, "gz", "gx", "gy"), P(), P(None, "gx", "gy")),
        out_specs=P(None, "gz", "gx", "gy"),
        check_vma=False,
    )
```

```python
import jax
import jax.numpy as jnp
from jax import lax
from jax.experimental import pallas as pl
from jax.experimental.pallas import tpu as pltpu
from jax.sharding import PartitionSpec as P


def padded_2(array, sides, width):
    for axis, dim in sides:
        peers, length = (lax.axis_size(axis), array.shape[dim])
        up = [(i, (i + 1) % peers) for i in range(peers)]
        down = [(j, i) for i, j in up]
        last = lax.slice_in_dim(array, length - width, length, axis=dim)
        initial = lax.slice_in_dim(array, 0, width, axis=dim)
        before = lax.ppermute(last, axis, up)
        after = lax.ppermute(initial, axis, down)
        array = jnp.concatenate([before, array, after], axis=dim)
    return array


def density_of(fields, wet_mask):
    return (-0.3 * fields[0] + 0.7 * fields[1] - 0.05 * fields[0] * fields[0]) * wet_mask


def advance(padded, wet_pad, pressure, wall_face, coriolis):
    wet_x = wet_pad[:, :-1, 1:-1] * wet_pad[:, 1:, 1:-1]
    wet_y = wet_pad[:, 1:-1, :-1] * wet_pad[:, 1:-1, 1:] * wall_face
    east_vel = 0.5 * (padded[2, :, :-1, 1:-1] + padded[2, :, 1:, 1:-1]) * wet_x
    north_vel = 0.5 * (padded[3, :, 1:-1, :-1] + padded[3, :, 1:-1, 1:]) * wet_y
    west_side = padded[:, :, :-1, 1:-1]
    east_side = padded[:, :, 1:, 1:-1]
    flux_x = 0.25 * (
        jnp.maximum(east_vel, 0.0) * west_side + jnp.minimum(east_vel, 0.0) * east_side
    ) - 0.08 * wet_x * (east_side - west_side)
    south_side = padded[:, :, 1:-1, :-1]
    north_side = padded[:, :, 1:-1, 1:]
    flux_y = 0.25 * (
        jnp.maximum(north_vel, 0.0) * south_side + jnp.minimum(north_vel, 0.0) * north_side
    ) - 0.08 * wet_y * (north_side - south_side)
    interior = padded[:, :, 1:-1, 1:-1]
    moved = interior - (
        flux_x[:, :, 1:] - flux_x[:, :, :-1] + flux_y[:, :, :, 1:] - flux_y[:, :, :, :-1]
    )
    centre = pressure[:, 1:-1, 1:-1]
    grad_x = 0.5 * (
        wet_x[:, 1:] * (pressure[:, 2:, 1:-1] - centre)
        + wet_x[:, :-1] * (centre - pressure[:, :-2, 1:-1])
    )
    grad_y = 0.5 * (
        wet_y[:, :, 1:] * (pressure[:, 1:-1, 2:] - centre)
        + wet_y[:, :, :-1] * (centre - pressure[:, 1:-1, :-2])
    )
    east_new = moved[2] + 0.3 * coriolis * interior[3] - grad_x
    north_new = moved[3] - 0.3 * coriolis * interior[2] - grad_y
    wet_inner = wet_pad[:, 1:-1, 1:-1]
    return jnp.stack([moved[0], moved[1], east_new, north_new]) * wet_inner


def coupling_kernel(c_ref, ctop_ref, ratio_ref, inv_ref, u_ref, v_ref, ends_ref):
    levels = c_ref.shape[1]
    ctop = ctop_ref[...]
    ratio_prev = None
    vu_prev = None
    for k in range(levels):
        above = ctop if k == 0 else c_ref[:, k - 1]
        below = c_ref[:, k]
        if k == 0:
            divisor = 1.0 + above + below
        else:
            divisor = 1.0 + above * (1.0 - ratio_prev) + below
        inv = 1.0 / divisor
        ratio = below * inv
        vu = ctop * inv if k == 0 else above * vu_prev * inv
        ratio_ref[:, k] = ratio
        inv_ref[:, k] = inv
        u_ref[:, k] = vu
        ratio_prev, vu_prev = ratio, vu
    u_later = vu_prev
    v_later = ratio_prev
    pairs = c_ref.shape[0]
    ends_ref[pairs:2 * pairs] = u_later
    ends_ref[3 * pairs:4 * pairs] = v_later
    v_ref[:, levels - 1] = v_later
    for k in range(levels - 2, -1, -1):
        ratio = ratio_ref[:, k]
        u_later = u_ref[:, k] + ratio * u_later
        v_later = ratio * v_later
        u_ref[:, k] = u_later
        v_ref[:, k] = v_later
    ends_ref[0:pairs] = u_later
    ends_ref[2 * pairs:3 * pairs] = v_later


def field_kernel(f_ref, c_ref, ctop_ref, ratio_ref, inv_ref, y_ref, ends_ref):
    levels = f_ref.shape[1]
    fields = f_ref.shape[0]
    vy = None
    for k in range(levels):
        inv = jnp.repeat(inv_ref[:, k], 2, axis=0)
        rhs = f_ref[:, k]
        if k == 0:
            vy = rhs * inv
        else:
            above = jnp.repeat(c_ref[:, k - 1], 2, axis=0)
            vy = (rhs + above * vy) * inv
        y_ref[:, k] = vy
    y_later = vy
    ends_ref[fields:2 * fields] = y_later
    for k in range(levels - 2, -1, -1):
        ratio = jnp.repeat(ratio_ref[:, k], 2, axis=0)
        y_later = y_ref[:, k] + ratio * y_later
        y_ref[:, k] = y_later
    ends_ref[0:fields] = y_later


def _specs(lead, levels, bx, cols_y):
    return pl.BlockSpec((lead, levels, bx, cols_y), lambda i: (0, 0, i, 0))


def _plane_spec(lead, bx, cols_y):
    return pl.BlockSpec((lead, bx, cols_y), lambda i: (0, i, 0))


def coupling_solve(coupling, ctop):
    pairs, levels, cols_x, cols_y = coupling.shape
    bx = 16 if cols_x % 16 == 0 else cols_x
    cspec = _specs(pairs, levels, bx, cols_y)
    full = jax.ShapeDtypeStruct(coupling.shape, jnp.float32)
    return pl.pallas_call(
        coupling_kernel,
        grid=(cols_x // bx,),
        in_specs=[cspec, _plane_spec(pairs, bx, cols_y)],
        out_specs=[cspec, cspec, cspec, cspec, _plane_spec(4 * pairs, bx, cols_y)],
        out_shape=[full, full, full, full,
                   jax.ShapeDtypeStruct((4 * pairs, cols_x, cols_y), jnp.float32)],
    )(coupling, ctop)


def field_solve(forced, coupling, ctop, ratio, inv):
    fields, levels, cols_x, cols_y = forced.shape
    pairs = coupling.shape[0]
    bx = 8 if cols_x % 8 == 0 else cols_x
    fspec = _specs(fields, levels, bx, cols_y)
    cspec = _specs(pairs, levels, bx, cols_y)
    return pl.pallas_call(
        field_kernel,
        grid=(cols_x // bx,),
        in_specs=[fspec, cspec, _plane_spec(pairs, bx, cols_y), cspec, cspec],
        out_specs=[fspec, _plane_spec(2 * fields, bx, cols_y)],
        out_shape=[jax.ShapeDtypeStruct(forced.shape, jnp.float32),
                   jax.ShapeDtypeStruct((2 * fields, cols_x, cols_y), jnp.float32)],
    )(forced, coupling, ctop, ratio, inv)


def interface_values(y_ends, uv_ends, place, peers):
    fields = 4
    y0 = y_ends[:, 0:fields]
    y1 = y_ends[:, fields:2 * fields]
    rest = jnp.repeat(uv_ends, 2, axis=1)
    u0 = rest[:, 0:4]
    u1 = rest[:, 4:8]
    v0 = rest[:, 8:12]
    v1 = rest[:, 12:16]
    pt, qt, pb, qb = [], [], [], []
    for q in range(peers):
        if q == 0:
            pt_q, qt_q = y0[q], v0[q]
            pb_q, qb_q = y1[q], v1[q]
        else:
            inv = 1.0 / (1.0 - u0[q] * qb[-1])
            pt_q = (y0[q] + u0[q] * pb[-1]) * inv
            qt_q = v0[q] * inv
            pb_q = y1[q] + u1[q] * (pb[-1] + qb[-1] * pt_q)
            qb_q = v1[q] + u1[q] * qb[-1] * qt_q
        pt.append(pt_q)
        qt.append(qt_q)
        pb.append(pb_q)
        qb.append(qb_q)
    tops = [None] * peers
    bots = [None] * peers
    t_next = jnp.zeros_like(pt[0])
    for q in range(peers - 1, -1, -1):
        tops[q] = pt[q] + qt[q] * t_next
        bots[q] = pb[q] + qb[q] * t_next
        t_next = tops[q]
    above = jnp.zeros_like(pt[0])
    below = jnp.zeros_like(pt[0])
    for q in range(peers):
        if q >= 1:
            above = jnp.where(place == q, bots[q - 1], above)
        if q <= peers - 2:
            below = jnp.where(place == q, tops[q + 1], below)
    return above, below


def gather_by_permutes(part, axis, place, peers):
    received = [part]
    for hop in range(1, peers):
        shift = [(i, (i + hop) % peers) for i in range(peers)]
        received.append(lax.ppermute(part, axis, shift))
    rows = []
    for q in range(peers):
        row = received[0]
        for hop in range(1, peers):
            row = jnp.where((place - hop) % peers == q, received[hop], row)
        rows.append(row)
    return jnp.stack(rows)


def _density(t, s, w):
    return (-0.3 * t + 0.7 * s - 0.05 * t * t) * w


def _flux(vel, lo, hi, w):
    return 0.25 * (jnp.maximum(vel, 0.0) * lo + jnp.minimum(vel, 0.0) * hi) - 0.08 * w * (hi - lo)


def fused_kernel(st_ref, xw_ref, xe_ref, ys_ref, yn_ref,
                 dc_ref, de_ref, dw_ref, dn_ref, ds_ref,
                 dxw_ref, dxe_ref, dys_ref, dyn_ref,
                 sc_ref, sxw_ref, sxe_ref, sys_ref, syn_ref,
                 lane_ref, wind_ref, c_ref, inv_ref, ratio_ref,
                 y_ref, ends_ref,
                 run_c_s, run_xw_s, run_xe_s, run_ys_s, run_yn_s, vy_s, cprev_s):
    fields, chunk, nx, ny = st_ref.shape
    levels = y_ref.shape[1]
    step_i = pl.program_id(0)
    row = lax.broadcasted_iota(jnp.int32, (nx, ny), 0)
    lane = lax.broadcasted_iota(jnp.int32, (nx, ny), 1)
    wall_n = lane_ref[0:1]
    wall_s = lane_ref[1:2]
    cor03 = lane_ref[2:3]
    d_c, d_e, d_w, d_n, d_s = dc_ref[...], de_ref[...], dw_ref[...], dn_ref[...], ds_ref[...]
    d_xw, d_xe, d_ys, d_yn = dxw_ref[...], dxe_ref[...], dys_ref[...], dyn_ref[...]

    @pl.when(step_i == 0)
    def _():
        run_c_s[...] = jnp.zeros_like(run_c_s)
        run_xw_s[...] = jnp.zeros_like(run_xw_s)
        run_xe_s[...] = jnp.zeros_like(run_xe_s)
        run_ys_s[...] = jnp.zeros_like(run_ys_s)
        run_yn_s[...] = jnp.zeros_like(run_yn_s)
        vy_s[...] = jnp.zeros_like(vy_s)
        cprev_s[...] = jnp.zeros_like(cprev_s)

    def east(r, h):
        return jnp.where(row == nx - 1, h, pltpu.roll(r, nx - 1, 0))

    def west(r, h):
        return jnp.where(row == 0, h, pltpu.roll(r, 1, 0))

    def north(r, h):
        return jnp.where(lane == ny - 1, h, pltpu.roll(r, ny - 1, 1))

    def south(r, h):
        return jnp.where(lane == 0, h, pltpu.roll(r, 1, 1))

    def level(kk, carry):
        run, vy_prev, c_prev = carry
        k = step_i * chunk + kk
        wc = (k < d_c).astype(jnp.float32)
        we = (k < d_e).astype(jnp.float32)
        ww = (k < d_w).astype(jnp.float32)
        wn = (k < d_n).astype(jnp.float32)
        ws = (k < d_s).astype(jnp.float32)
        wxw = (k < d_xw).astype(jnp.float32)
        wxe = (k < d_xe).astype(jnp.float32)
        wys = (k < d_ys).astype(jnp.float32)
        wyn = (k < d_yn).astype(jnp.float32)
        cen = [st_ref[f, kk] for f in range(fields)]
        hxw = [xw_ref[f, pl.ds(k, 1), :] for f in range(fields)]
        hxe = [xe_ref[f, pl.ds(k, 1), :] for f in range(fields)]
        hys = [ys_ref[f, kk] for f in range(fields)]
        hyn = [yn_ref[f, kk] for f in range(fields)]
        run_c, run_xw, run_xe, run_ys, run_yn = run
        den_c = _density(cen[0], cen[1], wc)
        den_xw = _density(hxw[0], hxw[1], wxw)
        den_xe = _density(hxe[0], hxe[1], wxe)
        den_ys = _density(hys[0], hys[1], wys)
        den_yn = _density(hyn[0], hyn[1], wyn)
        run_c = run_c + den_c
        run_xw = run_xw + den_xw
        run_xe = run_xe + den_xe
        run_ys = run_ys + den_ys
        run_yn = run_yn + den_yn
        p_c = 0.03 * (sc_ref[...] + run_c - 0.5 * den_c)
        p_xw = 0.03 * (sxw_ref[...] + run_xw - 0.5 * den_xw)
        p_xe = 0.03 * (sxe_ref[...] + run_xe - 0.5 * den_xe)
        p_ys = 0.03 * (sys_ref[...] + run_ys - 0.5 * den_ys)
        p_yn = 0.03 * (syn_ref[...] + run_yn - 0.5 * den_yn)
        p_e = east(p_c, p_xe)
        p_w = west(p_c, p_xw)
        p_n = north(p_c, p_yn)
        p_s = south(p_c, p_ys)
        face_e = wc * we
        face_w = ww * wc
        face_n = wc * wn * wall_n
        face_s = ws * wc * wall_s
        nbr_e = [east(cen[f], hxe[f]) for f in range(fields)]
        nbr_w = [west(cen[f], hxw[f]) for f in range(fields)]
        nbr_n = [north(cen[f], hyn[f]) for f in range(fields)]
        nbr_s = [south(cen[f], hys[f]) for f in range(fields)]
        vel_e = 0.5 * (cen[2] + nbr_e[2]) * face_e
        vel_w = 0.5 * (nbr_w[2] + cen[2]) * face_w
        vel_n = 0.5 * (cen[3] + nbr_n[3]) * face_n
        vel_s = 0.5 * (nbr_s[3] + cen[3]) * face_s
        moved = []
        for f in range(fields):
            fe = _flux(vel_e, cen[f], nbr_e[f], face_e)
            fw = _flux(vel_w, nbr_w[f], cen[f], face_w)
            fn = _flux(vel_n, cen[f], nbr_n[f], face_n)
            fs = _flux(vel_s, nbr_s[f], cen[f], face_s)
            moved.append(cen[f] - (fe - fw + fn - fs))
        grad_x = 0.5 * (face_e * (p_e - p_c) + face_w * (p_c - p_w))
        grad_y = 0.5 * (face_n * (p_n - p_c) + face_s * (p_c - p_s))
        east_new = moved[2] + cor03 * cen[3] - grad_x
        north_new = moved[3] - cor03 * cen[2] - grad_y
        top = (k == 0).astype(jnp.float32)
        forced = [moved[0] * wc, moved[1] * wc,
                  east_new * wc + wind_ref[0] * wc * top,
                  north_new * wc + wind_ref[1] * wc * top]
        vy = []
        for f in range(fields):
            m = f // 2
            val = (forced[f] + c_prev[m] * vy_prev[f]) * inv_ref[m, kk]
            y_ref[f, k] = val
            vy.append(val)
        c_here = jnp.stack([c_ref[0, kk], c_ref[1, kk]])
        return (run_c, run_xw, run_xe, run_ys, run_yn), jnp.stack(vy), c_here

    run = (run_c_s[...], run_xw_s[...], run_xe_s[...], run_ys_s[...], run_yn_s[...])
    carry = lax.fori_loop(0, chunk, level, (run, vy_s[...], cprev_s[...]), unroll=chunk)
    run, vy, c_prev = carry
    run_c_s[...], run_xw_s[...], run_xe_s[...], run_ys_s[...], run_yn_s[...] = run
    vy_s[...] = vy
    cprev_s[...] = c_prev

    @pl.when(step_i == pl.num_programs(0) - 1)
    def _():
        for f in range(fields):
            ends_ref[fields + f] = vy[f]

        def back(j, later):
            k = levels - 2 - j
            out = []
            for f in range(fields):
                val = y_ref[f, k] + ratio_ref[f // 2, k] * later[f]
                y_ref[f, k] = val
                out.append(val)
            return jnp.stack(out)

        later = lax.fori_loop(0, levels - 1, back, vy, unroll=2)
        for f in range(fields):
            ends_ref[f] = later[f]


def fused_solve(*operands):
    st = operands[0]
    fields, levels, nx, ny = st.shape
    pairs = operands[21].shape[0]
    chunk = 4 if levels % 4 == 0 else levels
    whole = [pl.BlockSpec(op.shape, (lambda i, n=op.ndim: (0,) * n)) for op in operands]
    by_level = lambda op: pl.BlockSpec((op.shape[0], chunk) + op.shape[2:], lambda i: (0, i, 0, 0))
    specs = list(whole)
    for idx in (0, 3, 4, 21, 22):
        specs[idx] = by_level(operands[idx])
    return pl.pallas_call(
        fused_kernel,
        grid=(levels // chunk,),
        in_specs=specs,
        out_specs=[pl.BlockSpec(st.shape, lambda i: (0, 0, 0, 0)),
                   pl.BlockSpec((2 * fields, nx, ny), lambda i: (0, 0, 0))],
        out_shape=[jax.ShapeDtypeStruct(st.shape, jnp.float32),
                   jax.ShapeDtypeStruct((2 * fields, nx, ny), jnp.float32)],
        scratch_shapes=[pltpu.VMEM((nx, ny), jnp.float32), pltpu.VMEM((1, ny), jnp.float32),
                        pltpu.VMEM((1, ny), jnp.float32), pltpu.VMEM((nx, 1), jnp.float32),
                        pltpu.VMEM((nx, 1), jnp.float32), pltpu.VMEM((fields, nx, ny), jnp.float32),
                        pltpu.VMEM((pairs, nx, ny), jnp.float32)],
        compiler_params=pltpu.CompilerParams(vmem_limit_bytes=60 * 1024 * 1024),
    )(*operands)


def per_device(state, mixing, depth_levels, wind):
    fields, lev_count, col_x, col_y = state.shape
    total_x, total_y = depth_levels.shape
    peers_z = lax.axis_size("gz")
    place_z = lax.axis_index("gz")
    peers_x = lax.axis_size("gx")
    peers_y = lax.axis_size("gy")
    start_x = lax.axis_index("gx") * col_x
    start_y = lax.axis_index("gy") * col_y
    start_z = place_z * lev_count
    down_z = [(i, i + 1) for i in range(peers_z - 1)]
    mix_above = lax.ppermute(mixing[:, lev_count - 1], "gz", down_z)
    up_x = [(i, (i + 1) % peers_x) for i in range(peers_x)]
    dn_x = [(j, i) for i, j in up_x]
    up_y = [(i, (i + 1) % peers_y) for i in range(peers_y)]
    dn_y = [(j, i) for i, j in up_y]
    halo_xw = lax.ppermute(state[:, :, col_x - 1], "gx", up_x)
    halo_xe = lax.ppermute(state[:, :, 0], "gx", dn_x)
    halo_ys = lax.ppermute(state[:, :, :, col_y - 1], "gy", up_y)
    halo_yn = lax.ppermute(state[:, :, :, 0], "gy", dn_y)
    levels = start_z + jnp.arange(lev_count, dtype=jnp.int32)
    row_index = (start_x - 1 + jnp.arange(col_x + 2, dtype=jnp.int32)) % total_x
    col_index = (start_y - 1 + jnp.arange(col_y + 2, dtype=jnp.int32)) % total_y
    depth_pad = jnp.take(jnp.take(depth_levels, row_index, axis=0), col_index, axis=1) - start_z
    d_c = depth_pad[1:-1, 1:-1]
    d_e = depth_pad[2:, 1:-1]
    d_w = depth_pad[:-2, 1:-1]
    d_n = depth_pad[1:-1, 2:]
    d_s = depth_pad[1:-1, :-2]
    d_xw = depth_pad[0:1, 1:-1]
    d_xe = depth_pad[col_x + 1:, 1:-1]
    d_ys = depth_pad[1:-1, 0:1]
    d_yn = depth_pad[1:-1, col_y + 1:]
    local = jnp.arange(lev_count, dtype=jnp.int32)
    wet_here = (local[:, None, None] < d_c[None]).astype(jnp.float32)
    wet_next = ((local + 1)[:, None, None] < d_c[None]).astype(jnp.float32)
    coupling = mixing * (wet_here * wet_next)[None]
    wet_up = (-1 < d_c).astype(jnp.float32)
    ctop = mix_above * (wet_up * wet_here[0])[None]
    ctop = jnp.where(place_z > 0, ctop, 0.0)
    ratio, inv, u, v, uv_ends = coupling_solve(coupling, ctop)
    uv_all = lax.all_gather(uv_ends, "gz")
    lev3 = local[:, None, None]
    tot_c = jnp.sum(density_of(state, (lev3 < d_c[None]).astype(jnp.float32)), axis=0)
    lev2 = local[:, None]
    tot_xw = jnp.sum(density_of(halo_xw, (lev2 < d_xw[0][None]).astype(jnp.float32)), axis=0)
    tot_xe = jnp.sum(density_of(halo_xe, (lev2 < d_xe[0][None]).astype(jnp.float32)), axis=0)
    tot_ys = jnp.sum(density_of(halo_ys, (lev2 < d_ys[:, 0][None]).astype(jnp.float32)), axis=0)
    tot_yn = jnp.sum(density_of(halo_yn, (lev2 < d_yn[:, 0][None]).astype(jnp.float32)), axis=0)
    side = jnp.zeros((2, col_y), jnp.float32)
    side = side.at[0, :col_x].set(tot_ys).at[1, :col_x].set(tot_yn)
    pack = jnp.concatenate([tot_c, tot_xw[None], tot_xe[None], side], axis=0)
    shallower = jnp.zeros_like(pack)
    for hop in range(1, peers_z):
        pairs_z = [(i, i + hop) for i in range(peers_z - hop)]
        shallower = shallower + lax.ppermute(pack, "gz", pairs_z)
    s_c = shallower[:col_x]
    s_xw = shallower[col_x:col_x + 1]
    s_xe = shallower[col_x + 1:col_x + 2]
    s_ys = shallower[col_x + 2, :col_x][:, None]
    s_yn = shallower[col_x + 3, :col_x][:, None]
    face_row = start_y + jnp.arange(col_y, dtype=jnp.int32)
    wall_n = (face_row <= total_y - 2).astype(jnp.float32)
    wall_s = (face_row - 1 >= 0).astype(jnp.float32)
    coriolis = 0.5 + (face_row.astype(jnp.float32) + 0.5) / total_y
    lanes = jnp.stack([wall_n, wall_s, 0.3 * coriolis] + [jnp.zeros_like(wall_n)] * 5)
    wind_top = jnp.where(place_z == 0, wind, 0.0)
    y, y_ends = fused_solve(state, halo_xw, halo_xe, halo_ys[..., None], halo_yn[..., None],
                            d_c, d_e, d_w, d_n, d_s, d_xw, d_xe, d_ys, d_yn,
                            s_c, s_xw, s_xe, s_ys, s_yn, lanes, wind_top,
                            coupling, inv, ratio)
    y_all = gather_by_permutes(y_ends, "gz", place_z, peers_z)
    x_above, x_below = interface_values(y_all, uv_all, place_z, peers_z)
    pairs = u.shape[0]
    shape5 = (pairs, fields // pairs) + y.shape[1:]
    plane5 = (pairs, fields // pairs, 1, col_x, col_y)
    x = (y.reshape(shape5) + x_above.reshape(plane5) * u[:, None]
         + x_below.reshape(plane5) * v[:, None])
    return x.reshape(y.shape)


def solution(mesh):
    return jax.shard_map(
        per_device,
        mesh=mesh,
        in_specs=(P(None, "gz", "gx", "gy"), P(None, "gz", "gx", "gy"), P(), P(None, "gx", "gy")),
        out_specs=P(None, "gz", "gx", "gy"),
        check_vma=False,
    )
```
